32 devices in a mesh: group: 2 (over y), seq: 4 (over z), batch: 2 (over x), mp: 2 (over core).
Axes of the slice: x: 2, y: 2, z: 4, core: 2. Of those that a mesh axis runs over, the one named last changes fastest.
Arguments:
- features: bfloat16 [4, 512, 384], P(('group', 'batch'), 'seq'), parts along dimension 0, may hold values from -6 to 6
- noise: float32 [4, 512, 384], P(('group', 'batch'), 'seq'), parts along dimension 0, may hold values from -3 to 3
- conv_weight: bfloat16 [5, 384, 768], P(None, 'seq', 'mp'), may hold values from -0.125 to 0.125
- conv_bias: float32 [768], P('mp'), may hold values from -3 to 3
- norm_gain: float32 [768], replicated, may hold values from 0.25 to 1.75
- qkv_weight: bfloat16 [3, 768, 768], P(None, 'seq', 'mp'), may hold values from -1.010363 to 1.010363
- out_weight: bfloat16 [768, 768], P('mp', 'seq'), may hold values from -0.21875 to 0.21875
Outputs:
- block_out: bfloat16 [4, 256, 768], P(('group', 'batch'), 'seq', 'mp'), parts along dimension 0
- new_noise: float32 [4, 512, 384], P(('group', 'batch'), 'seq'), parts along dimension 0
The draws below stay inside these ranges and needn't reach their ends.
There are 2 independent parts, one for each index of `group`. The reference program is written for one: setup_inputs(seed, part) draws one part's arguments, and reference() takes and returns one part's arrays. A program takes and returns all parts, laid end to end along the dimension named above; an argument that names none is the same for every part. Nothing has to cross between parts.
All inputs are finite; a program needn't handle non-finite values.
Results may differ from the reference program's by a relative error of at most 0.014.
Values may be sent and summed in bfloat16 or wider, within the bound.
No kernel may reach another device: no remote copies, remote signals or barrier semaphores. Data moves between devices by JAX's collectives and lax.ppermute only.
A program may use at most 64 MiB of HBM per device.

```python
import math
from functools import partial
import jax
import jax.numpy as jnp
from jax import lax

C = 384
F = 768
H = 8
HD = 96
KW = 5
HW = 768
POSITIONS = 512
SEQS = 2


def draw_qkv_weight(key, part):
    bound_value = 5.6 / math.sqrt(F)
    drawn = jax.random.normal(key, (3, F, HW), jnp.float32) * (1.4 / math.sqrt(F))
    drawn = jnp.clip(drawn, -bound_value, bound_value)
    return drawn.astype(jnp.bfloat16)


def block_levels(stream_key, extent, shards, smallest, high):
    def one(position, shards_of):
        heights = jax.random.uniform(jax.random.fold_in(jax.random.fold_in(stream_key, 6), position), (shards_of,), jnp.float32, smallest / len(shards), high / len(shards))
        return jnp.repeat(jnp.exp(heights), extent[position] // shards_of).reshape((-1,) + (1,) * (len(extent) - position - 1))

    gain = one(*shards[0])
    for cut in shards[1:]:
        gain = gain * one(*cut)
    return gain


def normal_values(key, extent, width, limit, shards=(), dtype=jnp.bfloat16):
    gain = block_levels(key, extent, shards, -0.22, 0.18) if shards else 1.0
    values = jax.random.normal(key, extent, jnp.float32) * width * gain
    return jnp.minimum(jnp.maximum(values, -limit), limit).astype(dtype)


def setup_inputs(seed: int = 0, part: int = 0) -> dict:
    streams_of = jax.random.split(jax.random.key(seed), 8)
    part_splits = jax.random.split(jax.random.fold_in(streams_of[7], part), 8)
    features = normal_values(part_splits[0], (SEQS, POSITIONS, C), 1.0, 6.0, ((0, 2), (1, 4)))
    noise = normal_values(part_splits[1], (SEQS, POSITIONS, C), 0.5, 3.0, ((0, 2), (1, 4)), jnp.float32)
    conv_weight = normal_values(streams_of[2], (KW, C, F), (KW * C) ** -0.5, 0.125, ((1, 4), (2, 2)))
    conv_bias = normal_values(streams_of[3], (F,), 0.5, 3.0, ((0, 2),), jnp.float32)
    norm_gain = jnp.clip(1.0 + 0.15 * jax.random.normal(streams_of[4], (F,), jnp.float32), 0.25, 1.75)
    qkv_weight = draw_qkv_weight(jax.random.fold_in(streams_of[7], 71), part)
    out_weight = normal_values(streams_of[6], (HW, F), HW ** -0.5, 0.21875, ((0, 2), (1, 4)))
    return dict(features=features, noise=noise, conv_weight=conv_weight, conv_bias=conv_bias, norm_gain=norm_gain, qkv_weight=qkv_weight, out_weight=out_weight)


step_size = 0.5
epsilon = 1e-06

def conv_section(inputs, conv_weight, conv_bias):
    positions = inputs.shape[0]
    reach = KW // 2
    padded = jnp.pad(inputs, ((reach, reach), (0, 0)))
    running = jnp.zeros((positions, conv_weight.shape[2]), jnp.float32)
    for offset in range(KW):
        running = running + jnp.dot(padded[offset:offset + positions], conv_weight[offset], preferred_element_type=jnp.float32)
    pre_act = running + conv_bias
    paired = jax.nn.gelu(pre_act).reshape(positions // 2, 2, conv_weight.shape[2])
    pooled = (0.5 * (paired[:, 0] + paired[:, 1])).astype(jnp.bfloat16)
    return (pre_act, pooled)

def split_heads(matrix):
    return matrix.reshape(matrix.shape[0], H, HD).transpose(1, 0, 2)

def merge_heads(stacked):
    return stacked.transpose(1, 0, 2).reshape(stacked.shape[1], H * HD)

def head_forward(operands):
    query, keys, values = operands
    score_scale = keys.shape[1] ** (-0.5)
    scores = jnp.dot(query, keys.T, preferred_element_type=jnp.float32) * score_scale
    row_top = lax.optimization_barrier(jnp.max(scores, axis=1, keepdims=True))
    log_mass = row_top + jnp.log(lax.optimization_barrier(jnp.sum(jnp.exp(scores - row_top), axis=1, keepdims=True)))
    soft_weights = jnp.exp(scores - log_mass).astype(jnp.bfloat16)
    attended = jnp.dot(soft_weights, values, preferred_element_type=jnp.float32).astype(jnp.bfloat16)
    return (attended, log_mass)

def head_backward(operands):
    query, keys, values, attended, log_mass, out_grad = operands
    score_scale = keys.shape[1] ** (-0.5)
    scores = jnp.dot(query, keys.T, preferred_element_type=jnp.float32) * score_scale
    exp_weights = jnp.exp(scores - log_mass)
    row_dot = lax.optimization_barrier(jnp.sum(out_grad.astype(jnp.float32) * attended.astype(jnp.float32), axis=1, keepdims=True))
    value_grad = jnp.dot(exp_weights.astype(jnp.bfloat16).T, out_grad, preferred_element_type=jnp.float32).astype(jnp.bfloat16)
    prob_grad = jnp.dot(out_grad, values.T, preferred_element_type=jnp.float32)
    score_grad = (exp_weights * (prob_grad - row_dot)).astype(jnp.bfloat16)
    query_grad = (jnp.dot(score_grad, keys, preferred_element_type=jnp.float32) * score_scale).astype(jnp.bfloat16)
    key_grad = (jnp.dot(score_grad.T, query, preferred_element_type=jnp.float32) * score_scale).astype(jnp.bfloat16)
    return (query_grad, key_grad, value_grad)

def forward(inputs, conv_weight, conv_bias, norm_gain, qkv_weight, out_weight):
    pre_act, pooled = conv_section(inputs, conv_weight, conv_bias)
    pooled_wide = lax.optimization_barrier(pooled).astype(jnp.float32)
    row_scale = lax.rsqrt(lax.optimization_barrier(jnp.mean(pooled_wide * pooled_wide, axis=1, keepdims=True)) + epsilon)
    normed = (pooled_wide * row_scale * norm_gain).astype(jnp.bfloat16)
    parts = [split_heads(jnp.dot(normed, qkv_weight[index], preferred_element_type=jnp.float32).astype(jnp.bfloat16)) for index in range(3)]
    attended, log_mass = lax.map(head_forward, (parts[0], parts[1], parts[2]))
    mixed = pooled_wide + jnp.dot(merge_heads(attended), out_weight, preferred_element_type=jnp.float32)
    return (pre_act, pooled_wide, row_scale, parts, attended, log_mass, mixed)

def one_sequence(operands, conv_weight, conv_bias, norm_gain, qkv_weight, out_weight):
    features_row, noise_row = operands
    moved = (features_row.astype(jnp.float32) + noise_row).astype(jnp.bfloat16)
    clean_run = forward(features_row, conv_weight, conv_bias, norm_gain, qkv_weight, out_weight)
    pre_act, pooled_wide, row_scale, parts, attended, log_mass, mixed = forward(moved, conv_weight, conv_bias, norm_gain, qkv_weight, out_weight)
    difference = mixed - clean_run[6]
    difference_half = difference.astype(jnp.bfloat16)
    out_grad = jnp.dot(difference_half, out_weight.T, preferred_element_type=jnp.float32).astype(jnp.bfloat16)
    grads = lax.map(head_backward, (parts[0], parts[1], parts[2], attended, log_mass, split_heads(out_grad)))
    normed_grad = jnp.dot(merge_heads(grads[0]), qkv_weight[0].T, preferred_element_type=jnp.float32)
    normed_grad = normed_grad + jnp.dot(merge_heads(grads[1]), qkv_weight[1].T, preferred_element_type=jnp.float32)
    normed_grad = normed_grad + jnp.dot(merge_heads(grads[2]), qkv_weight[2].T, preferred_element_type=jnp.float32)
    weighted = lax.optimization_barrier(jnp.sum(normed_grad * norm_gain * pooled_wide, axis=1, keepdims=True))
    pooled_grad = difference + row_scale * norm_gain * normed_grad - pooled_wide * row_scale ** 3 * weighted / F
    bins = pooled_grad.shape[0]
    positions = pre_act.shape[0]
    spread = jnp.broadcast_to((0.5 * pooled_grad)[:, None, :], (bins, 2, F)).reshape(positions, F)
    gelu_back = jax.vjp(jax.nn.gelu, pre_act)[1]
    pre_grad = gelu_back(spread)[0].astype(jnp.bfloat16)
    reach = KW // 2
    padded = jnp.pad(pre_grad, ((reach, reach), (0, 0)))
    input_grad = jnp.zeros((positions, C), jnp.float32)
    for offset in range(KW):
        lower = 2 * reach - offset
        input_grad = input_grad + jnp.dot(padded[lower:lower + positions], conv_weight[offset].T, preferred_element_type=jnp.float32)
    new_noise = noise_row + step_size * input_grad * lax.rsqrt(lax.optimization_barrier(jnp.mean(input_grad * input_grad, axis=1, keepdims=True)) + epsilon)
    return (clean_run[6].astype(jnp.bfloat16), new_noise)

def reference(features, noise, conv_weight, conv_bias, norm_gain, qkv_weight, out_weight):
    runner = partial(one_sequence, conv_weight=conv_weight, conv_bias=conv_bias, norm_gain=norm_gain, qkv_weight=qkv_weight, out_weight=out_weight)
    block_out, new_noise = lax.map(runner, (features, noise))
    return (block_out, new_noise)
```

```python
import jax
import jax.numpy as jnp
from jax import lax
from jax.sharding import PartitionSpec as P

F = 768
HD = 96
KW = 5


step_size = 0.5
epsilon = 1e-06


def with_halo(cells, sides, width):
    for axis, dim in sides:
        count = lax.axis_size(axis)
        ends = count - 1
        head = lax.slice_in_dim(cells, 0, width, axis=dim)
        tail = lax.slice_in_dim(cells, cells.shape[dim] - width, cells.shape[dim], axis=dim)
        cells = jnp.concatenate(
            [
                lax.ppermute(tail, axis, [(i, (i + 1) % count) for i in range(ends)]),
                cells,
                lax.ppermute(head, axis, [((i + 1) % count, i) for i in range(ends)]),
            ],
            axis=dim,
        )
    return cells


def gather_seq(cells, dim):
    spread = ("group", "batch")
    count = lax.axis_size("group") * lax.axis_size("batch")
    ring = lax.axis_size("seq")
    flat = cells.reshape(-1, cells.shape[-1])
    rows = flat.shape[0]
    size = -(-rows // count)
    if size * count != rows:
        flat = jnp.pad(flat, ((0, size * count - rows), (0, 0)))
    piece = lax.dynamic_slice_in_dim(flat, lax.axis_index(spread) * size, size, 0)
    along = lax.all_gather(piece, "seq", axis=0, tiled=False)
    whole = lax.all_gather(along, spread, axis=0, tiled=False)
    whole = whole.transpose(1, 0, 2, 3).reshape(ring, count * size, flat.shape[1])[:, :rows]
    whole = jnp.moveaxis(whole.reshape((ring,) + cells.shape), 0, dim)
    shape = list(cells.shape)
    shape[dim] = shape[dim] * ring
    return whole.reshape(shape)


def swap_mp(cells):
    return lax.ppermute(cells, "mp", [(0, 1), (1, 0)])


def add_halves(cells, dim):
    half = cells.shape[dim] // 2
    index = lax.axis_index("mp")
    own = lax.dynamic_slice_in_dim(cells, index * half, half, dim)
    other = lax.dynamic_slice_in_dim(cells, (1 - index) * half, half, dim)
    return (own.astype(jnp.float32) + swap_mp(other).astype(jnp.float32)).astype(
        jnp.bfloat16
    ).astype(jnp.float32)


def attend_rows(query, keys, values):
    key_total = keys.shape[0]
    block_len = min(512, key_total)
    head_size = keys.shape[1]
    score_scale = head_size ** (-0.5)
    key_blocks = keys.reshape(key_total // block_len, block_len, head_size)
    value_blocks = values.reshape(key_total // block_len, block_len, head_size)
    query_count = query.shape[0]

    def find_top(carry, key_block):
        row_top, row_mass = carry
        scores = jnp.dot(query, key_block.T, preferred_element_type=jnp.float32) * score_scale
        new_top = jnp.maximum(row_top, jnp.max(scores, axis=1))
        row_mass = row_mass * jnp.exp(row_top - new_top) + jnp.sum(
            jnp.exp(scores - new_top[:, None]), axis=1
        )
        return ((new_top, row_mass), None)

    start_top = jnp.full((query_count,), -1e30, jnp.float32)
    (row_top, row_mass), _ = lax.scan(
        find_top, (start_top, jnp.zeros((query_count,), jnp.float32)), key_blocks
    )
    log_mass = row_top + jnp.log(row_mass)

    def collect(running, blocks):
        key_block, value_block = blocks
        scores = jnp.dot(query, key_block.T, preferred_element_type=jnp.float32) * score_scale
        soft_weights = jnp.exp(scores - log_mass[:, None]).astype(jnp.bfloat16)
        return (
            running + jnp.dot(soft_weights, value_block, preferred_element_type=jnp.float32),
            None,
        )

    running, _ = lax.scan(
        collect, jnp.zeros((query_count, head_size), jnp.float32), (key_blocks, value_blocks)
    )
    return (running.astype(jnp.bfloat16), log_mass)


def attend_back(query, keys, values, attended, log_mass, out_grad):
    key_total = keys.shape[0]
    block_len = min(512, key_total)
    head_size = keys.shape[1]
    score_scale = head_size ** (-0.5)
    key_blocks = keys.reshape(key_total // block_len, block_len, head_size)
    value_blocks = values.reshape(key_total // block_len, block_len, head_size)
    row_dot = jnp.sum(out_grad.astype(jnp.float32) * attended.astype(jnp.float32), axis=1)

    def step_back(query_acc, blocks):
        key_block, value_block = blocks
        scores = jnp.dot(query, key_block.T, preferred_element_type=jnp.float32) * score_scale
        exp_weights = jnp.exp(scores - log_mass[:, None])
        value_part = jnp.einsum(
            "qk,qd->kd",
            exp_weights.astype(jnp.bfloat16),
            out_grad,
            preferred_element_type=jnp.float32,
        )
        prob_grad = jnp.dot(out_grad, value_block.T, preferred_element_type=jnp.float32)
        score_grad = (exp_weights * (prob_grad - row_dot[:, None])).astype(jnp.bfloat16)
        query_acc = (
            query_acc
            + jnp.dot(score_grad, key_block, preferred_element_type=jnp.float32) * score_scale
        )
        key_part = (
            jnp.einsum("qk,qd->kd", score_grad, query, preferred_element_type=jnp.float32)
            * score_scale
        )
        return (query_acc, jnp.concatenate([key_part, value_part], axis=1))

    query_grad, keyval_parts = lax.scan(
        step_back, jnp.zeros((query.shape[0], head_size), jnp.float32), (key_blocks, value_blocks)
    )
    return (query_grad, keyval_parts.reshape(key_total, 2 * head_size))


def forward(stack, conv_weight, conv_bias, norm_gain, qkv_weight, out_weight):
    pass_count, positions, channels = stack.shape
    reach = KW // 2
    half_width = conv_weight.shape[2]
    padded_input = with_halo(stack, (("seq", 1),), reach)
    running = jnp.zeros((pass_count, positions, half_width), jnp.float32)
    piece = conv_weight
    for offset in range(piece.shape[0]):
        running = running + jnp.einsum(
            "ptc,cf->ptf",
            padded_input[:, offset : offset + positions],
            piece[offset],
            preferred_element_type=jnp.float32,
        )
    pre_act = running + conv_bias
    paired = jax.nn.gelu(pre_act).reshape(pass_count, positions // 2, 2, half_width)
    pooled = (0.5 * (paired[:, :, 0] + paired[:, :, 1])).astype(jnp.bfloat16)
    pooled_wide = lax.optimization_barrier(pooled).astype(jnp.float32)
    whole = lax.all_gather(pooled, "mp", axis=2, tiled=True)
    whole_wide = whole.astype(jnp.float32)
    row_scale = lax.rsqrt(jnp.mean(whole_wide * whole_wide, axis=2, keepdims=True) + epsilon)
    normed = (whole_wide * row_scale * norm_gain).astype(jnp.bfloat16)
    rows = positions // 2
    proj_width = qkv_weight.shape[2]
    projected = jnp.einsum(
        "prf,jfh->jprh",
        normed,
        qkv_weight,
        preferred_element_type=jnp.float32,
    ).astype(jnp.bfloat16)
    head_size = HD
    head_count = proj_width // head_size
    devices = lax.axis_size("seq")
    query_groups = devices // head_count
    sub_rows = rows // query_groups
    query_send = (
        projected[0]
        .reshape(pass_count, query_groups, sub_rows, head_count, head_size)
        .transpose(3, 1, 0, 2, 4)
        .reshape(devices, pass_count, sub_rows * head_size)
    )
    keyval = jnp.concatenate(
        [
            projected[1].reshape(pass_count, rows, head_count, head_size),
            projected[2].reshape(pass_count, rows, head_count, head_size),
        ],
        axis=3,
    )
    keyval_flat = keyval.transpose(2, 0, 1, 3).reshape(
        head_count, 1, pass_count, rows * 2 * head_size
    )
    keyval_send = jnp.broadcast_to(
        keyval_flat, (head_count, query_groups, pass_count, rows * 2 * head_size)
    ).reshape(devices, pass_count, rows * 2 * head_size)
    query_in, keyval_in = (
        lax.all_to_all(query_send, "seq", split_axis=0, concat_axis=2, tiled=True),
        lax.all_to_all(keyval_send, "seq", split_axis=0, concat_axis=2, tiled=True),
    )
    query_heads = query_in.reshape(pass_count, devices * sub_rows, head_size)
    keyval_heads = keyval_in.reshape(pass_count, devices * rows, 2 * head_size)
    outputs = []
    masses = []
    for index in range(pass_count):
        out_now, mass_now = attend_rows(
            query_heads[index],
            keyval_heads[index, :, :head_size],
            keyval_heads[index, :, head_size:],
        )
        outputs.append(out_now)
        masses.append(mass_now)
    attended_heads = jnp.stack(outputs)
    log_mass = jnp.stack(masses)
    out_send = attended_heads.reshape(pass_count, devices, sub_rows * head_size).transpose(1, 0, 2)
    out_back = lax.all_to_all(out_send, "seq", split_axis=0, concat_axis=0, tiled=True)
    attended = (
        out_back.reshape(head_count, query_groups, pass_count, sub_rows, head_size)
        .transpose(2, 1, 3, 0, 4)
        .reshape(pass_count, rows, proj_width)
    )
    terms = jnp.einsum(
        "prh,hf->prf",
        attended,
        out_weight,
        preferred_element_type=jnp.float32,
    )
    mixed = (
        add_halves(terms.astype(jnp.bfloat16), 2) + pooled_wide
    )
    return (
        pre_act,
        pooled_wide,
        whole_wide,
        row_scale,
        query_heads,
        keyval_heads,
        attended_heads,
        log_mass,
        mixed,
    )


def shards(features, noise, conv_weight, conv_bias, norm_gain, qkv_weight, out_weight):
    conv_weight = gather_seq(conv_weight, 1)
    qkv_weight = gather_seq(qkv_weight, 1)
    out_weight = gather_seq(out_weight, 1)
    clean = features[0]
    moved = (clean.astype(jnp.float32) + noise[0]).astype(jnp.bfloat16)
    joint = forward(
        jnp.stack([clean, moved]), conv_weight, conv_bias, norm_gain, qkv_weight, out_weight
    )
    clean_run = [item[0:1] for item in joint]
    moved_run = [item[1:2] for item in joint]
    (
        pre_act,
        pooled_wide,
        whole_wide,
        row_scale,
        query_heads,
        keyval_heads,
        attended_heads,
        log_mass,
        mixed,
    ) = [item[0] for item in moved_run]
    clean_mixed = clean_run[8][0]
    rows, half_width = pooled_wide.shape
    positions = pre_act.shape[0]
    proj_width = qkv_weight.shape[2]
    head_size = HD
    head_count = proj_width // head_size
    devices = lax.axis_size("seq")
    query_groups = devices // head_count
    sub_rows = rows // query_groups
    difference = mixed - clean_mixed
    difference_half = difference.astype(jnp.bfloat16)
    difference_whole = lax.all_gather(difference_half, "mp", axis=1, tiled=True)
    out_grad = jnp.einsum(
        "rf,hf->rh",
        difference_whole,
        out_weight,
        preferred_element_type=jnp.float32,
    ).astype(jnp.bfloat16)
    grad_send = (
        out_grad.reshape(query_groups, sub_rows, head_count, head_size)
        .transpose(2, 0, 1, 3)
        .reshape(devices, sub_rows * head_size)
    )
    grad_in = lax.all_to_all(grad_send, "seq", split_axis=0, concat_axis=1, tiled=True)
    grad_heads = grad_in.reshape(devices * sub_rows, head_size)
    query_grad, keyval_grad = attend_back(
        query_heads,
        keyval_heads[:, :head_size],
        keyval_heads[:, head_size:],
        attended_heads,
        log_mass,
        grad_heads,
    )
    query_back, keyval_back = (
        lax.all_to_all(
            query_grad.reshape(devices, sub_rows * head_size).astype(jnp.bfloat16),
            "seq",
            split_axis=0,
            concat_axis=0,
            tiled=True,
        ).astype(jnp.float32),
        lax.all_to_all(
            keyval_grad.reshape(devices, rows * 2 * head_size).astype(jnp.bfloat16),
            "seq",
            split_axis=0,
            concat_axis=0,
            tiled=True,
        ).astype(jnp.float32),
    )
    query_rows = (
        query_back.reshape(head_count, query_groups, sub_rows, head_size)
        .transpose(1, 2, 0, 3)
        .reshape(rows, proj_width)
        .astype(jnp.bfloat16)
    )
    keyval_rows = jnp.sum(keyval_back.reshape(head_count, query_groups, rows, 2, head_size), axis=1)
    key_rows = (
        keyval_rows[:, :, 0].transpose(1, 0, 2).reshape(rows, proj_width).astype(jnp.bfloat16)
    )
    value_rows = (
        keyval_rows[:, :, 1].transpose(1, 0, 2).reshape(rows, proj_width).astype(jnp.bfloat16)
    )
    grads = jnp.stack([query_rows, key_rows, value_rows])
    normed_terms = jnp.einsum(
        "jrh,jfh->rf",
        grads,
        qkv_weight,
        preferred_element_type=jnp.float32,
    )
    offset_mp = lax.axis_index("mp") * half_width
    gain_own = lax.dynamic_slice_in_dim(norm_gain, offset_mp, half_width, 0)
    normed_grad = add_halves(normed_terms.astype(jnp.bfloat16), 1)
    weighted = lax.psum(jnp.sum(normed_grad * gain_own * pooled_wide, axis=1, keepdims=True), "mp")
    pooled_grad = (
        difference + row_scale * gain_own * normed_grad - pooled_wide * row_scale**3 * weighted / F
    )
    spread = jnp.broadcast_to((0.5 * pooled_grad)[:, None, :], (rows, 2, half_width)).reshape(
        positions, half_width
    )
    gelu_back = jax.vjp(jax.nn.gelu, pre_act)[1]
    pre_grad = gelu_back(spread)[0].astype(jnp.bfloat16)
    reach = KW // 2
    padded = with_halo(pre_grad, (("seq", 0),), reach)
    piece = conv_weight
    running = jnp.zeros((positions, piece.shape[1]), jnp.float32)
    for offset in range(piece.shape[0]):
        lower = 2 * reach - offset
        running = running + jnp.einsum(
            "tf,cf->tc",
            padded[lower : lower + positions],
            piece[offset],
            preferred_element_type=jnp.float32,
        )
    own_grad = running.astype(jnp.bfloat16)
    input_grad = (own_grad.astype(jnp.float32) + swap_mp(own_grad).astype(jnp.float32)).astype(
        jnp.bfloat16
    ).astype(jnp.float32)
    new_noise = noise[0] + step_size * input_grad * lax.rsqrt(
        jnp.mean(input_grad * input_grad, axis=1, keepdims=True) + epsilon
    )
    return (clean_mixed.astype(jnp.bfloat16)[None], new_noise[None])


def solution(mesh):
    return jax.shard_map(
        shards,
        mesh=mesh,
        in_specs=(
            P(("group", "batch"), "seq", None),
            P(("group", "batch"), "seq", None),
            P(None, "seq", "mp"),
            P("mp"),
            P(),
            P(None, "seq", "mp"),
            P("mp", "seq"),
        ),
        out_specs=(P(("group", "batch"), "seq", "mp"), P(("group", "batch"), "seq", None)),
        check_vma=False,
    )
```

```python
import jax
import jax.numpy as jnp
from jax import lax
from jax.sharding import PartitionSpec as P

F = 768
HD = 96
KW = 5


step_size = 0.5
epsilon = 1e-06


def with_halo(cells, sides, width):
    for axis, dim in sides:
        count = lax.axis_size(axis)
        ends = count - 1
        head = lax.slice_in_dim(cells, 0, width, axis=dim)
        tail = lax.slice_in_dim(cells, cells.shape[dim] - width, cells.shape[dim], axis=dim)
        cells = jnp.concatenate(
            [
                lax.ppermute(tail, axis, [(i, (i + 1) % count) for i in range(ends)]),
                cells,
                lax.ppermute(head, axis, [((i + 1) % count, i) for i in range(ends)]),
            ],
            axis=dim,
        )
    return cells


def gather_seq(cells, dim):
    spread = ("group", "batch")
    count = lax.axis_size("group") * lax.axis_size("batch")
    ring = lax.axis_size("seq")
    flat = cells.reshape(-1, cells.shape[-1])
    rows = flat.shape[0]
    size = -(-rows // count)
    if size * count != rows:
        flat = jnp.pad(flat, ((0, size * count - rows), (0, 0)))
    piece = lax.dynamic_slice_in_dim(flat, lax.axis_index(spread) * size, size, 0)
    if ring <= 8:
        place = lax.axis_index("seq")
        along = jnp.zeros((ring,) + piece.shape, piece.dtype)
        along = lax.dynamic_update_slice_in_dim(along, piece[None], place, 0)
        for shift in range(1, ring):
            arrived = lax.ppermute(piece, "seq", [(i, (i + shift) % ring) for i in range(ring)])
            along = lax.dynamic_update_slice_in_dim(
                along, arrived[None], (place + ring - shift) % ring, 0
            )
    else:
        along = lax.all_gather(piece, "seq", axis=0, tiled=False)
    whole = lax.all_gather(along, spread, axis=0, tiled=False)
    whole = whole.transpose(1, 0, 2, 3).reshape(ring, count * size, flat.shape[1])[:, :rows]
    whole = jnp.moveaxis(whole.reshape((ring,) + cells.shape), 0, dim)
    shape = list(cells.shape)
    shape[dim] = shape[dim] * ring
    return whole.reshape(shape)


def swap_mp(cells):
    return lax.ppermute(cells, "mp", [(0, 1), (1, 0)])


def add_halves(cells, dim):
    half = cells.shape[dim] // 2
    index = lax.axis_index("mp")
    own = lax.dynamic_slice_in_dim(cells, index * half, half, dim)
    other = lax.dynamic_slice_in_dim(cells, (1 - index) * half, half, dim)
    return (own.astype(jnp.float32) + swap_mp(other).astype(jnp.float32)).astype(
        jnp.bfloat16
    ).astype(jnp.float32)


def attend_rows(query, keys, values):
    key_total = keys.shape[0]
    block_len = min(512, key_total)
    head_size = keys.shape[1]
    score_scale = head_size ** (-0.5)
    key_blocks = keys.reshape(key_total // block_len, block_len, head_size)
    value_blocks = values.reshape(key_total // block_len, block_len, head_size)
    query_count = query.shape[0]

    def find_top(carry, key_block):
        row_top, row_mass = carry
        scores = jnp.dot(query, key_block.T, preferred_element_type=jnp.float32) * score_scale
        new_top = jnp.maximum(row_top, jnp.max(scores, axis=1))
        row_mass = row_mass * jnp.exp(row_top - new_top) + jnp.sum(
            jnp.exp(scores - new_top[:, None]), axis=1
        )
        return ((new_top, row_mass), None)

    start_top = jnp.full((query_count,), -1e30, jnp.float32)
    (row_top, row_mass), _ = lax.scan(
        find_top, (start_top, jnp.zeros((query_count,), jnp.float32)), key_blocks
    )
    log_mass = row_top + jnp.log(row_mass)

    def collect(running, blocks):
        key_block, value_block = blocks
        scores = jnp.dot(query, key_block.T, preferred_element_type=jnp.float32) * score_scale
        soft_weights = jnp.exp(scores - log_mass[:, None]).astype(jnp.bfloat16)
        return (
            running + jnp.dot(soft_weights, value_block, preferred_element_type=jnp.float32),
            None,
        )

    running, _ = lax.scan(
        collect, jnp.zeros((query_count, head_size), jnp.float32), (key_blocks, value_blocks)
    )
    return (running.astype(jnp.bfloat16), log_mass)


def attend_back(query, keys, values, attended, log_mass, out_grad):
    key_total = keys.shape[0]
    block_len = min(512, key_total)
    head_size = keys.shape[1]
    score_scale = head_size ** (-0.5)
    key_blocks = keys.reshape(key_total // block_len, block_len, head_size)
    value_blocks = values.reshape(key_total // block_len, block_len, head_size)
    row_dot = jnp.sum(out_grad.astype(jnp.float32) * attended.astype(jnp.float32), axis=1)

    def step_back(query_acc, blocks):
        key_block, value_block = blocks
        scores = jnp.dot(query, key_block.T, preferred_element_type=jnp.float32) * score_scale
        exp_weights = jnp.exp(scores - log_mass[:, None])
        value_part = jnp.einsum(
            "qk,qd->kd",
            exp_weights.astype(jnp.bfloat16),
            out_grad,
            preferred_element_type=jnp.float32,
        )
        prob_grad = jnp.dot(out_grad, value_block.T, preferred_element_type=jnp.float32)
        score_grad = (exp_weights * (prob_grad - row_dot[:, None])).astype(jnp.bfloat16)
        query_acc = (
            query_acc
            + jnp.dot(score_grad, key_block, preferred_element_type=jnp.float32) * score_scale
        )
        key_part = (
            jnp.einsum("qk,qd->kd", score_grad, query, preferred_element_type=jnp.float32)
            * score_scale
        )
        return (query_acc, jnp.concatenate([key_part, value_part], axis=1))

    query_grad, keyval_parts = lax.scan(
        step_back, jnp.zeros((query.shape[0], head_size), jnp.float32), (key_blocks, value_blocks)
    )
    return (query_grad, keyval_parts.reshape(key_total, 2 * head_size))


def forward(stack, conv_weight, conv_bias, norm_gain, qkv_weight, out_weight):
    pass_count, positions, channels = stack.shape
    reach = KW // 2
    half_width = conv_weight.shape[2]
    padded_input = with_halo(stack, (("seq", 1),), reach)
    running = jnp.zeros((pass_count, positions, half_width), jnp.float32)
    piece = conv_weight
    for offset in range(piece.shape[0]):
        running = running + jnp.einsum(
            "ptc,cf->ptf",
            padded_input[:, offset : offset + positions],
            piece[offset],
            preferred_element_type=jnp.float32,
        )
    pre_act = running + conv_bias
    paired = jax.nn.gelu(pre_act).reshape(pass_count, positions // 2, 2, half_width)
    pooled = (0.5 * (paired[:, :, 0] + paired[:, :, 1])).astype(jnp.bfloat16)
    pooled_wide = lax.optimization_barrier(pooled).astype(jnp.float32)
    whole = lax.all_gather(pooled, "mp", axis=2, tiled=True)
    whole_wide = whole.astype(jnp.float32)
    row_scale = lax.rsqrt(jnp.mean(whole_wide * whole_wide, axis=2, keepdims=True) + epsilon)
    normed = (whole_wide * row_scale * norm_gain).astype(jnp.bfloat16)
    rows = positions // 2
    proj_width = qkv_weight.shape[2]
    projected = jnp.einsum(
        "prf,jfh->jprh",
        normed,
        qkv_weight,
        preferred_element_type=jnp.float32,
    ).astype(jnp.bfloat16)
    head_size = HD
    head_count = proj_width // head_size
    devices = lax.axis_size("seq")
    query_groups = devices // head_count
    sub_rows = rows // query_groups
    query_send = (
        projected[0]
        .reshape(pass_count, query_groups, sub_rows, head_count, head_size)
        .transpose(3, 1, 0, 2, 4)
        .reshape(devices, pass_count, sub_rows * head_size)
    )
    keyval = jnp.concatenate(
        [
            projected[1].reshape(pass_count, rows, head_count, head_size),
            projected[2].reshape(pass_count, rows, head_count, head_size),
        ],
        axis=3,
    )
    keyval_flat = keyval.transpose(2, 0, 1, 3).reshape(
        head_count, 1, pass_count, rows * 2 * head_size
    )
    keyval_send = jnp.broadcast_to(
        keyval_flat, (head_count, query_groups, pass_count, rows * 2 * head_size)
    ).reshape(devices, pass_count, rows * 2 * head_size)
    query_in, keyval_in = (
        lax.all_to_all(query_send, "seq", split_axis=0, concat_axis=2, tiled=True),
        lax.all_to_all(keyval_send, "seq", split_axis=0, concat_axis=2, tiled=True),
    )
    query_heads = query_in.reshape(pass_count, devices * sub_rows, head_size)
    keyval_heads = keyval_in.reshape(pass_count, devices * rows, 2 * head_size)
    outputs = []
    masses = []
    for index in range(pass_count):
        out_now, mass_now = attend_rows(
            query_heads[index],
            keyval_heads[index, :, :head_size],
            keyval_heads[index, :, head_size:],
        )
        outputs.append(out_now)
        masses.append(mass_now)
    attended_heads = jnp.stack(outputs)
    log_mass = jnp.stack(masses)
    out_send = attended_heads.reshape(pass_count, devices, sub_rows * head_size).transpose(1, 0, 2)
    out_back = lax.all_to_all(out_send, "seq", split_axis=0, concat_axis=0, tiled=True)
    attended = (
        out_back.reshape(head_count, query_groups, pass_count, sub_rows, head_size)
        .transpose(2, 1, 3, 0, 4)
        .reshape(pass_count, rows, proj_width)
    )
    terms = jnp.einsum(
        "prh,hf->prf",
        attended,
        out_weight,
        preferred_element_type=jnp.float32,
    )
    mixed = (
        add_halves(terms.astype(jnp.bfloat16), 2) + pooled_wide
    )
    return (
        pre_act,
        pooled_wide,
        whole_wide,
        row_scale,
        query_heads,
        keyval_heads,
        attended_heads,
        log_mass,
        mixed,
    )


def shards(features, noise, conv_weight, conv_bias, norm_gain, qkv_weight, out_weight):
    conv_weight = gather_seq(conv_weight, 1)
    qkv_weight = gather_seq(qkv_weight, 1)
    out_weight = gather_seq(out_weight, 1)
    clean = features[0]
    moved = (clean.astype(jnp.float32) + noise[0]).astype(jnp.bfloat16)
    joint = forward(
        jnp.stack([clean, moved]), conv_weight, conv_bias, norm_gain, qkv_weight, out_weight
    )
    clean_run = [item[0:1] for item in joint]
    moved_run = [item[1:2] for item in joint]
    (
        pre_act,
        pooled_wide,
        whole_wide,
        row_scale,
        query_heads,
        keyval_heads,
        attended_heads,
        log_mass,
        mixed,
    ) = [item[0] for item in moved_run]
    clean_mixed = clean_run[8][0]
    rows, half_width = pooled_wide.shape
    positions = pre_act.shape[0]
    proj_width = qkv_weight.shape[2]
    head_size = HD
    head_count = proj_width // head_size
    devices = lax.axis_size("seq")
    query_groups = devices // head_count
    sub_rows = rows // query_groups
    difference = mixed - clean_mixed
    difference_half = difference.astype(jnp.bfloat16)
    difference_whole = lax.all_gather(difference_half, "mp", axis=1, tiled=True)
    out_grad = jnp.einsum(
        "rf,hf->rh",
        difference_whole,
        out_weight,
        preferred_element_type=jnp.float32,
    ).astype(jnp.bfloat16)
    grad_send = (
        out_grad.reshape(query_groups, sub_rows, head_count, head_size)
        .transpose(2, 0, 1, 3)
        .reshape(devices, sub_rows * head_size)
    )
    grad_in = lax.all_to_all(grad_send, "seq", split_axis=0, concat_axis=1, tiled=True)
    grad_heads = grad_in.reshape(devices * sub_rows, head_size)
    query_grad, keyval_grad = attend_back(
        query_heads,
        keyval_heads[:, :head_size],
        keyval_heads[:, head_size:],
        attended_heads,
        log_mass,
        grad_heads,
    )
    query_back, keyval_back = (
        lax.all_to_all(
            query_grad.reshape(devices, sub_rows * head_size).astype(jnp.bfloat16),
            "seq",
            split_axis=0,
            concat_axis=0,
            tiled=True,
        ).astype(jnp.float32),
        lax.all_to_all(
            keyval_grad.reshape(devices, rows * 2 * head_size).astype(jnp.bfloat16),
            "seq",
            split_axis=0,
            concat_axis=0,
            tiled=True,
        ).astype(jnp.float32),
    )
    query_rows = (
        query_back.reshape(head_count, query_groups, sub_rows, head_size)
        .transpose(1, 2, 0, 3)
        .reshape(rows, proj_width)
        .astype(jnp.bfloat16)
    )
    keyval_rows = jnp.sum(keyval_back.reshape(head_count, query_groups, rows, 2, head_size), axis=1)
    key_rows = (
        keyval_rows[:, :, 0].transpose(1, 0, 2).reshape(rows, proj_width).astype(jnp.bfloat16)
    )
    value_rows = (
        keyval_rows[:, :, 1].transpose(1, 0, 2).reshape(rows, proj_width).astype(jnp.bfloat16)
    )
    grads = jnp.stack([query_rows, key_rows, value_rows])
    normed_terms = jnp.einsum(
        "jrh,jfh->rf",
        grads,
        qkv_weight,
        preferred_element_type=jnp.float32,
    )
    offset_mp = lax.axis_index("mp") * half_width
    gain_own = lax.dynamic_slice_in_dim(norm_gain, offset_mp, half_width, 0)
    normed_grad = add_halves(normed_terms.astype(jnp.bfloat16), 1)
    weighted = lax.psum(jnp.sum(normed_grad * gain_own * pooled_wide, axis=1, keepdims=True), "mp")
    pooled_grad = (
        difference + row_scale * gain_own * normed_grad - pooled_wide * row_scale**3 * weighted / F
    )
    spread = jnp.broadcast_to((0.5 * pooled_grad)[:, None, :], (rows, 2, half_width)).reshape(
        positions, half_width
    )
    gelu_back = jax.vjp(jax.nn.gelu, pre_act)[1]
    pre_grad = gelu_back(spread)[0].astype(jnp.bfloat16)
    reach = KW // 2
    padded = with_halo(pre_grad, (("seq", 0),), reach)
    piece = conv_weight
    running = jnp.zeros((positions, piece.shape[1]), jnp.float32)
    for offset in range(piece.shape[0]):
        lower = 2 * reach - offset
        running = running + jnp.einsum(
            "tf,cf->tc",
            padded[lower : lower + positions],
            piece[offset],
            preferred_element_type=jnp.float32,
        )
    own_grad = running.astype(jnp.bfloat16)
    input_grad = (own_grad.astype(jnp.float32) + swap_mp(own_grad).astype(jnp.float32)).astype(
        jnp.bfloat16
    ).astype(jnp.float32)
    new_noise = noise[0] + step_size * input_grad * lax.rsqrt(
        jnp.mean(input_grad * input_grad, axis=1, keepdims=True) + epsilon
    )
    return (clean_mixed.astype(jnp.bfloat16)[None], new_noise[None])


def solution(mesh):
    return jax.shard_map(
        shards,
        mesh=mesh,
        in_specs=(
            P(("group", "batch"), "seq", None),
            P(("group", "batch"), "seq", None),
            P(None, "seq", "mp"),
            P("mp"),
            P(),
            P(None, "seq", "mp"),
            P("mp", "seq"),
        ),
        out_specs=(P(("group", "batch"), "seq", "mp"), P(("group", "batch"), "seq", None)),
        check_vma=False,
    )
```

```python
import jax
import jax.numpy as jnp
from jax import lax
from jax.sharding import PartitionSpec as P

F = 768
HD = 96
KW = 5


step_size = 0.5
epsilon = 1e-06


def with_halo(cells, sides, width):
    for axis, dim in sides:
        count = lax.axis_size(axis)
        ends = count - 1
        head = lax.slice_in_dim(cells, 0, width, axis=dim)
        tail = lax.slice_in_dim(cells, cells.shape[dim] - width, cells.shape[dim], axis=dim)
        cells = jnp.concatenate(
            [
                lax.ppermute(tail, axis, [(i, (i + 1) % count) for i in range(ends)]),
                cells,
                lax.ppermute(head, axis, [((i + 1) % count, i) for i in range(ends)]),
            ],
            axis=dim,
        )
    return cells


def gather_seq(parts):
    spread = ("group", "batch")
    count = lax.axis_size("group") * lax.axis_size("batch")
    ring = lax.axis_size("seq")
    width = parts[0][0].shape[-1]
    flats = [cells.reshape(-1, width) for cells, _ in parts]
    flat = jnp.concatenate(flats, axis=0) if len(flats) > 1 else flats[0]
    rows = flat.shape[0]
    size = -(-rows // count)
    if size * count != rows:
        flat = jnp.pad(flat, ((0, size * count - rows), (0, 0)))
    piece = lax.dynamic_slice_in_dim(flat, lax.axis_index(spread) * size, size, 0)
    if ring <= 8:
        place = lax.axis_index("seq")
        along = jnp.zeros((ring,) + piece.shape, piece.dtype)
        along = lax.dynamic_update_slice_in_dim(along, piece[None], place, 0)
        for shift in range(1, ring):
            arrived = lax.ppermute(piece, "seq", [(i, (i + shift) % ring) for i in range(ring)])
            along = lax.dynamic_update_slice_in_dim(
                along, arrived[None], (place + ring - shift) % ring, 0
            )
    else:
        along = lax.all_gather(piece, "seq", axis=0, tiled=False)
    whole = lax.all_gather(along, spread, axis=0, tiled=False)
    whole = whole.transpose(1, 0, 2, 3).reshape(ring, count * size, width)
    results = []
    offset = 0
    for (cells, dim), part in zip(parts, flats):
        block = whole[:, offset : offset + part.shape[0]]
        offset += part.shape[0]
        block = jnp.moveaxis(block.reshape((ring,) + cells.shape), 0, dim)
        shape = list(cells.shape)
        shape[dim] = shape[dim] * ring
        results.append(block.reshape(shape))
    return results


def swap_mp(cells):
    return lax.ppermute(cells, "mp", [(0, 1), (1, 0)])


def add_halves(cells, dim):
    half = cells.shape[dim] // 2
    index = lax.axis_index("mp")
    own = lax.dynamic_slice_in_dim(cells, index * half, half, dim)
    other = lax.dynamic_slice_in_dim(cells, (1 - index) * half, half, dim)
    return (own.astype(jnp.float32) + swap_mp(other).astype(jnp.float32)).astype(
        jnp.bfloat16
    ).astype(jnp.float32)


def attend_rows(query, keys, values):
    key_total = keys.shape[0]
    block_len = min(512, key_total)
    head_size = keys.shape[1]
    score_scale = head_size ** (-0.5)
    key_blocks = keys.reshape(key_total // block_len, block_len, head_size)
    value_blocks = values.reshape(key_total // block_len, block_len, head_size)
    query_count = query.shape[0]

    def find_top(carry, key_block):
        row_top, row_mass = carry
        scores = jnp.dot(query, key_block.T, preferred_element_type=jnp.float32) * score_scale
        new_top = jnp.maximum(row_top, jnp.max(scores, axis=1))
        row_mass = row_mass * jnp.exp(row_top - new_top) + jnp.sum(
            jnp.exp(scores - new_top[:, None]), axis=1
        )
        return ((new_top, row_mass), None)

    start_top = jnp.full((query_count,), -1e30, jnp.float32)
    (row_top, row_mass), _ = lax.scan(
        find_top, (start_top, jnp.zeros((query_count,), jnp.float32)), key_blocks
    )
    log_mass = row_top + jnp.log(row_mass)

    def collect(running, blocks):
        key_block, value_block = blocks
        scores = jnp.dot(query, key_block.T, preferred_element_type=jnp.float32) * score_scale
        soft_weights = jnp.exp(scores - log_mass[:, None]).astype(jnp.bfloat16)
        return (
            running + jnp.dot(soft_weights, value_block, preferred_element_type=jnp.float32),
            None,
        )

    running, _ = lax.scan(
        collect, jnp.zeros((query_count, head_size), jnp.float32), (key_blocks, value_blocks)
    )
    return (running.astype(jnp.bfloat16), log_mass)


def attend_back(query, keys, values, attended, log_mass, out_grad):
    key_total = keys.shape[0]
    block_len = min(512, key_total)
    head_size = keys.shape[1]
    score_scale = head_size ** (-0.5)
    key_blocks = keys.reshape(key_total // block_len, block_len, head_size)
    value_blocks = values.reshape(key_total // block_len, block_len, head_size)
    row_dot = jnp.sum(out_grad.astype(jnp.float32) * attended.astype(jnp.float32), axis=1)

    def step_back(query_acc, blocks):
        key_block, value_block = blocks
        scores = jnp.dot(query, key_block.T, preferred_element_type=jnp.float32) * score_scale
        exp_weights = jnp.exp(scores - log_mass[:, None])
        value_part = jnp.einsum(
            "qk,qd->kd",
            exp_weights.astype(jnp.bfloat16),
            out_grad,
            preferred_element_type=jnp.float32,
        )
        prob_grad = jnp.dot(out_grad, value_block.T, preferred_element_type=jnp.float32)
        score_grad = (exp_weights * (prob_grad - row_dot[:, None])).astype(jnp.bfloat16)
        query_acc = (
            query_acc
            + jnp.dot(score_grad, key_block, preferred_element_type=jnp.float32) * score_scale
        )
        key_part = (
            jnp.einsum("qk,qd->kd", score_grad, query, preferred_element_type=jnp.float32)
            * score_scale
        )
        return (query_acc, jnp.concatenate([key_part, value_part], axis=1))

    query_grad, keyval_parts = lax.scan(
        step_back, jnp.zeros((query.shape[0], head_size), jnp.float32), (key_blocks, value_blocks)
    )
    return (query_grad, keyval_parts.reshape(key_total, 2 * head_size))


def forward(stack, conv_weight, conv_bias, norm_gain, qkv_weight, out_weight):
    pass_count, positions, channels = stack.shape
    reach = KW // 2
    half_width = conv_weight.shape[2]
    padded_input = with_halo(stack, (("seq", 1),), reach)
    running = jnp.zeros((pass_count, positions, half_width), jnp.float32)
    piece = conv_weight
    for offset in range(piece.shape[0]):
        running = running + jnp.einsum(
            "ptc,cf->ptf",
            padded_input[:, offset : offset + positions],
            piece[offset],
            preferred_element_type=jnp.float32,
        )
    pre_act = running + conv_bias
    paired = jax.nn.gelu(pre_act).reshape(pass_count, positions // 2, 2, half_width)
    pooled = (0.5 * (paired[:, :, 0] + paired[:, :, 1])).astype(jnp.bfloat16)
    pooled_wide = lax.optimization_barrier(pooled).astype(jnp.float32)
    whole = lax.all_gather(pooled, "mp", axis=2, tiled=True)
    whole_wide = whole.astype(jnp.float32)
    row_scale = lax.rsqrt(jnp.mean(whole_wide * whole_wide, axis=2, keepdims=True) + epsilon)
    normed = (whole_wide * row_scale * norm_gain).astype(jnp.bfloat16)
    rows = positions // 2
    proj_width = qkv_weight.shape[2]
    projected = jnp.einsum(
        "prf,jfh->jprh",
        normed,
        qkv_weight,
        preferred_element_type=jnp.float32,
    ).astype(jnp.bfloat16)
    head_size = HD
    head_count = proj_width // head_size
    devices = lax.axis_size("seq")
    query_groups = devices // head_count
    sub_rows = rows // query_groups
    query_send = (
        projected[0]
        .reshape(pass_count, query_groups, sub_rows, head_count, head_size)
        .transpose(3, 1, 0, 2, 4)
        .reshape(devices, pass_count, sub_rows * head_size)
    )
    keyval = jnp.concatenate(
        [
            projected[1].reshape(pass_count, rows, head_count, head_size),
            projected[2].reshape(pass_count, rows, head_count, head_size),
        ],
        axis=3,
    )
    keyval_flat = keyval.transpose(2, 0, 1, 3).reshape(
        head_count, 1, pass_count, rows * 2 * head_size
    )
    keyval_send = jnp.broadcast_to(
        keyval_flat, (head_count, query_groups, pass_count, rows * 2 * head_size)
    ).reshape(devices, pass_count, rows * 2 * head_size)
    query_len = query_send.shape[2]
    both_in = lax.all_to_all(
        jnp.concatenate([query_send, keyval_send], axis=2),
        "seq",
        split_axis=0,
        concat_axis=2,
        tiled=True,
    ).reshape(pass_count, devices, query_len + keyval_send.shape[2])
    query_heads = both_in[:, :, :query_len].reshape(pass_count, devices * sub_rows, head_size)
    keyval_heads = both_in[:, :, query_len:].reshape(pass_count, devices * rows, 2 * head_size)
    outputs = []
    masses = []
    for index in range(pass_count):
        out_now, mass_now = attend_rows(
            query_heads[index],
            keyval_heads[index, :, :head_size],
            keyval_heads[index, :, head_size:],
        )
        outputs.append(out_now)
        masses.append(mass_now)
    attended_heads = jnp.stack(outputs)
    log_mass = jnp.stack(masses)
    out_send = attended_heads.reshape(pass_count, devices, sub_rows * head_size).transpose(1, 0, 2)
    out_back = lax.all_to_all(out_send, "seq", split_axis=0, concat_axis=0, tiled=True)
    attended = (
        out_back.reshape(head_count, query_groups, pass_count, sub_rows, head_size)
        .transpose(2, 1, 3, 0, 4)
        .reshape(pass_count, rows, proj_width)
    )
    terms = jnp.einsum(
        "prh,hf->prf",
        attended,
        out_weight,
        preferred_element_type=jnp.float32,
    )
    mixed = (
        add_halves(terms.astype(jnp.bfloat16), 2) + pooled_wide
    )
    return (
        pre_act,
        pooled_wide,
        whole_wide,
        row_scale,
        query_heads,
        keyval_heads,
        attended_heads,
        log_mass,
        mixed,
    )


def shards(features, noise, conv_weight, conv_bias, norm_gain, qkv_weight, out_weight):
    (conv_weight,) = gather_seq([(conv_weight, 1)])
    qkv_weight, out_weight = gather_seq([(qkv_weight, 1), (out_weight, 1)])
    clean = features[0]
    moved = (clean.astype(jnp.float32) + noise[0]).astype(jnp.bfloat16)
    joint = forward(
        jnp.stack([clean, moved]), conv_weight, conv_bias, norm_gain, qkv_weight, out_weight
    )
    clean_run = [item[0:1] for item in joint]
    moved_run = [item[1:2] for item in joint]
    (
        pre_act,
        pooled_wide,
        whole_wide,
        row_scale,
        query_heads,
        keyval_heads,
        attended_heads,
        log_mass,
        mixed,
    ) = [item[0] for item in moved_run]
    clean_mixed = clean_run[8][0]
    rows, half_width = pooled_wide.shape
    positions = pre_act.shape[0]
    proj_width = qkv_weight.shape[2]
    head_size = HD
    head_count = proj_width // head_size
    devices = lax.axis_size("seq")
    query_groups = devices // head_count
    sub_rows = rows // query_groups
    difference = mixed - clean_mixed
    difference_half = difference.astype(jnp.bfloat16)
    difference_whole = lax.all_gather(difference_half, "mp", axis=1, tiled=True)
    out_grad = jnp.einsum(
        "rf,hf->rh",
        difference_whole,
        out_weight,
        preferred_element_type=jnp.float32,
    ).astype(jnp.bfloat16)
    grad_send = (
        out_grad.reshape(query_groups, sub_rows, head_count, head_size)
        .transpose(2, 0, 1, 3)
        .reshape(devices, sub_rows * head_size)
    )
    grad_in = lax.all_to_all(grad_send, "seq", split_axis=0, concat_axis=1, tiled=True)
    grad_heads = grad_in.reshape(devices * sub_rows, head_size)
    query_grad, keyval_grad = attend_back(
        query_heads,
        keyval_heads[:, :head_size],
        keyval_heads[:, head_size:],
        attended_heads,
        log_mass,
        grad_heads,
    )
    query_len = sub_rows * head_size
    both_back = lax.all_to_all(
        jnp.concatenate(
            [
                query_grad.reshape(devices, query_len).astype(jnp.bfloat16),
                keyval_grad.reshape(devices, rows * 2 * head_size).astype(jnp.bfloat16),
            ],
            axis=1,
        ),
        "seq",
        split_axis=0,
        concat_axis=0,
        tiled=True,
    ).astype(jnp.float32)
    query_back = both_back[:, :query_len]
    keyval_back = both_back[:, query_len:]
    query_rows = (
        query_back.reshape(head_count, query_groups, sub_rows, head_size)
        .transpose(1, 2, 0, 3)
        .reshape(rows, proj_width)
        .astype(jnp.bfloat16)
    )
    keyval_rows = jnp.sum(keyval_back.reshape(head_count, query_groups, rows, 2, head_size), axis=1)
    key_rows = (
        keyval_rows[:, :, 0].transpose(1, 0, 2).reshape(rows, proj_width).astype(jnp.bfloat16)
    )
    value_rows = (
        keyval_rows[:, :, 1].transpose(1, 0, 2).reshape(rows, proj_width).astype(jnp.bfloat16)
    )
    grads = jnp.stack([query_rows, key_rows, value_rows])
    normed_terms = jnp.einsum(
        "jrh,jfh->rf",
        grads,
        qkv_weight,
        preferred_element_type=jnp.float32,
    )
    offset_mp = lax.axis_index("mp") * half_width
    gain_own = lax.dynamic_slice_in_dim(norm_gain, offset_mp, half_width, 0)
    normed_grad = add_halves(normed_terms.astype(jnp.bfloat16), 1)
    weighted = lax.psum(jnp.sum(normed_grad * gain_own * pooled_wide, axis=1, keepdims=True), "mp")
    pooled_grad = (
        difference + row_scale * gain_own * normed_grad - pooled_wide * row_scale**3 * weighted / F
    )
    spread = jnp.broadcast_to((0.5 * pooled_grad)[:, None, :], (rows, 2, half_width)).reshape(
        positions, half_width
    )
    gelu_back = jax.vjp(jax.nn.gelu, pre_act)[1]
    pre_grad = gelu_back(spread)[0].astype(jnp.bfloat16)
    reach = KW // 2
    padded = with_halo(pre_grad, (("seq", 0),), reach)
    piece = conv_weight
    running = jnp.zeros((positions, piece.shape[1]), jnp.float32)
    for offset in range(piece.shape[0]):
        lower = 2 * reach - offset
        running = running + jnp.einsum(
            "tf,cf->tc",
            padded[lower : lower + positions],
            piece[offset],
            preferred_element_type=jnp.float32,
        )
    own_grad = running.astype(jnp.bfloat16)
    input_grad = (own_grad.astype(jnp.float32) + swap_mp(own_grad).astype(jnp.float32)).astype(
        jnp.bfloat16
    ).astype(jnp.float32)
    new_noise = noise[0] + step_size * input_grad * lax.rsqrt(
        jnp.mean(input_grad * input_grad, axis=1, keepdims=True) + epsilon
    )
    return (clean_mixed.astype(jnp.bfloat16)[None], new_noise[None])


def solution(mesh):
    return jax.shard_map(
        shards,
        mesh=mesh,
        in_specs=(
            P(("group", "batch"), "seq", None),
            P(("group", "batch"), "seq", None),
            P(None, "seq", "mp"),
            P("mp"),
            P(),
            P(None, "seq", "mp"),
            P("mp", "seq"),
        ),
        out_specs=(P(("group", "batch"), "seq", "mp"), P(("group", "batch"), "seq", None)),
        check_vma=False,
    )
```

```python
import jax
import jax.numpy as jnp
from jax import lax
from jax.sharding import PartitionSpec as P

F = 768
HD = 96
KW = 5


step_size = 0.5
epsilon = 1e-06


def with_halo(cells, sides, width):
    for axis, dim in sides:
        count = lax.axis_size(axis)
        ends = count - 1
        head = lax.slice_in_dim(cells, 0, width, axis=dim)
        tail = lax.slice_in_dim(cells, cells.shape[dim] - width, cells.shape[dim], axis=dim)
        cells = jnp.concatenate(
            [
                lax.ppermute(tail, axis, [(i, (i + 1) % count) for i in range(ends)]),
                cells,
                lax.ppermute(head, axis, [((i + 1) % count, i) for i in range(ends)]),
            ],
            axis=dim,
        )
    return cells


def gather_seq(parts):
    spread = ("group", "batch")
    count = lax.axis_size("group") * lax.axis_size("batch")
    ring = lax.axis_size("seq")
    width = parts[0][0].shape[-1]
    flats = [cells.reshape(-1, width) for cells, _ in parts]
    flat = jnp.concatenate(flats, axis=0) if len(flats) > 1 else flats[0]
    rows = flat.shape[0]
    size = -(-rows // count)
    if size * count != rows:
        flat = jnp.pad(flat, ((0, size * count - rows), (0, 0)))
    piece = lax.dynamic_slice_in_dim(flat, lax.axis_index(spread) * size, size, 0)
    if ring <= 8:
        place = lax.axis_index("seq")
        along = jnp.zeros((ring,) + piece.shape, piece.dtype)
        along = lax.dynamic_update_slice_in_dim(along, piece[None], place, 0)
        for shift in range(1, ring):
            arrived = lax.ppermute(piece, "seq", [(i, (i + shift) % ring) for i in range(ring)])
            along = lax.dynamic_update_slice_in_dim(
                along, arrived[None], (place + ring - shift) % ring, 0
            )
    else:
        along = lax.all_gather(piece, "seq", axis=0, tiled=False)
    if ring <= 8 and count <= 4:
        place = lax.axis_index(spread)
        whole = jnp.zeros((count,) + along.shape, along.dtype)
        whole = lax.dynamic_update_slice_in_dim(whole, along[None], place, 0)
        for mask in range(1, count):
            arrived = lax.ppermute(along, spread, [(i, i ^ mask) for i in range(count)])
            whole = lax.dynamic_update_slice_in_dim(
                whole, arrived[None], lax.bitwise_xor(place, mask), 0
            )
    else:
        whole = lax.all_gather(along, spread, axis=0, tiled=False)
    whole = whole.transpose(1, 0, 2, 3).reshape(ring, count * size, width)
    results = []
    offset = 0
    for (cells, dim), part in zip(parts, flats):
        block = whole[:, offset : offset + part.shape[0]]
        offset += part.shape[0]
        block = jnp.moveaxis(block.reshape((ring,) + cells.shape), 0, dim)
        shape = list(cells.shape)
        shape[dim] = shape[dim] * ring
        results.append(block.reshape(shape))
    return results


def swap_mp(cells):
    return lax.ppermute(cells, "mp", [(0, 1), (1, 0)])


def add_halves(cells, dim):
    half = cells.shape[dim] // 2
    index = lax.axis_index("mp")
    own = lax.dynamic_slice_in_dim(cells, index * half, half, dim)
    other = lax.dynamic_slice_in_dim(cells, (1 - index) * half, half, dim)
    return (own.astype(jnp.float32) + swap_mp(other).astype(jnp.float32)).astype(
        jnp.bfloat16
    ).astype(jnp.float32)


def attend_rows(query, keys, values):
    key_total = keys.shape[0]
    block_len = min(512, key_total)
    head_size = keys.shape[1]
    score_scale = head_size ** (-0.5)
    key_blocks = keys.reshape(key_total // block_len, block_len, head_size)
    value_blocks = values.reshape(key_total // block_len, block_len, head_size)
    query_count = query.shape[0]

    def find_top(carry, key_block):
        row_top, row_mass = carry
        scores = jnp.dot(query, key_block.T, preferred_element_type=jnp.float32) * score_scale
        new_top = jnp.maximum(row_top, jnp.max(scores, axis=1))
        row_mass = row_mass * jnp.exp(row_top - new_top) + jnp.sum(
            jnp.exp(scores - new_top[:, None]), axis=1
        )
        return ((new_top, row_mass), None)

    start_top = jnp.full((query_count,), -1e30, jnp.float32)
    (row_top, row_mass), _ = lax.scan(
        find_top, (start_top, jnp.zeros((query_count,), jnp.float32)), key_blocks
    )
    log_mass = row_top + jnp.log(row_mass)

    def collect(running, blocks):
        key_block, value_block = blocks
        scores = jnp.dot(query, key_block.T, preferred_element_type=jnp.float32) * score_scale
        soft_weights = jnp.exp(scores - log_mass[:, None]).astype(jnp.bfloat16)
        return (
            running + jnp.dot(soft_weights, value_block, preferred_element_type=jnp.float32),
            None,
        )

    running, _ = lax.scan(
        collect, jnp.zeros((query_count, head_size), jnp.float32), (key_blocks, value_blocks)
    )
    return (running.astype(jnp.bfloat16), log_mass)


def attend_back(query, keys, values, attended, log_mass, out_grad):
    key_total = keys.shape[0]
    block_len = min(512, key_total)
    head_size = keys.shape[1]
    score_scale = head_size ** (-0.5)
    key_blocks = keys.reshape(key_total // block_len, block_len, head_size)
    value_blocks = values.reshape(key_total // block_len, block_len, head_size)
    row_dot = jnp.sum(out_grad.astype(jnp.float32) * attended.astype(jnp.float32), axis=1)

    def step_back(query_acc, blocks):
        key_block, value_block = blocks
        scores = jnp.dot(query, key_block.T, preferred_element_type=jnp.float32) * score_scale
        exp_weights = jnp.exp(scores - log_mass[:, None])
        value_part = jnp.einsum(
            "qk,qd->kd",
            exp_weights.astype(jnp.bfloat16),
            out_grad,
            preferred_element_type=jnp.float32,
        )
        prob_grad = jnp.dot(out_grad, value_block.T, preferred_element_type=jnp.float32)
        score_grad = (exp_weights * (prob_grad - row_dot[:, None])).astype(jnp.bfloat16)
        query_acc = (
            query_acc
            + jnp.dot(score_grad, key_block, preferred_element_type=jnp.float32) * score_scale
        )
        key_part = (
            jnp.einsum("qk,qd->kd", score_grad, query, preferred_element_type=jnp.float32)
            * score_scale
        )
        return (query_acc, jnp.concatenate([key_part, value_part], axis=1))

    query_grad, keyval_parts = lax.scan(
        step_back, jnp.zeros((query.shape[0], head_size), jnp.float32), (key_blocks, value_blocks)
    )
    return (query_grad, keyval_parts.reshape(key_total, 2 * head_size))


def forward(stack, conv_weight, conv_bias, norm_gain, qkv_weight, out_weight):
    pass_count, positions, channels = stack.shape
    reach = KW // 2
    half_width = conv_weight.shape[2]
    padded_input = with_halo(stack, (("seq", 1),), reach)
    running = jnp.zeros((pass_count, positions, half_width), jnp.float32)
    piece = conv_weight
    for offset in range(piece.shape[0]):
        running = running + jnp.einsum(
            "ptc,cf->ptf",
            padded_input[:, offset : offset + positions],
            piece[offset],
            preferred_element_type=jnp.float32,
        )
    pre_act = running + conv_bias
    paired = jax.nn.gelu(pre_act).reshape(pass_count, positions // 2, 2, half_width)
    pooled = (0.5 * (paired[:, :, 0] + paired[:, :, 1])).astype(jnp.bfloat16)
    pooled_wide = lax.optimization_barrier(pooled).astype(jnp.float32)
    whole = lax.all_gather(pooled, "mp", axis=2, tiled=True)
    whole_wide = whole.astype(jnp.float32)
    row_scale = lax.rsqrt(jnp.mean(whole_wide * whole_wide, axis=2, keepdims=True) + epsilon)
    normed = (whole_wide * row_scale * norm_gain).astype(jnp.bfloat16)
    rows = positions // 2
    proj_width = qkv_weight.shape[2]
    projected = jnp.einsum(
        "prf,jfh->jprh",
        normed,
        qkv_weight,
        preferred_element_type=jnp.float32,
    ).astype(jnp.bfloat16)
    head_size = HD
    head_count = proj_width // head_size
    devices = lax.axis_size("seq")
    query_groups = devices // head_count
    sub_rows = rows // query_groups
    query_send = (
        projected[0]
        .reshape(pass_count, query_groups, sub_rows, head_count, head_size)
        .transpose(3, 1, 0, 2, 4)
        .reshape(devices, pass_count, sub_rows * head_size)
    )
    keyval = jnp.concatenate(
        [
            projected[1].reshape(pass_count, rows, head_count, head_size),
            projected[2].reshape(pass_count, rows, head_count, head_size),
        ],
        axis=3,
    )
    keyval_flat = keyval.transpose(2, 0, 1, 3).reshape(
        head_count, 1, pass_count, rows * 2 * head_size
    )
    keyval_send = jnp.broadcast_to(
        keyval_flat, (head_count, query_groups, pass_count, rows * 2 * head_size)
    ).reshape(devices, pass_count, rows * 2 * head_size)
    query_len = query_send.shape[2]
    both_in = lax.all_to_all(
        jnp.concatenate([query_send, keyval_send], axis=2),
        "seq",
        split_axis=0,
        concat_axis=2,
        tiled=True,
    ).reshape(pass_count, devices, query_len + keyval_send.shape[2])
    query_heads = both_in[:, :, :query_len].reshape(pass_count, devices * sub_rows, head_size)
    keyval_heads = both_in[:, :, query_len:].reshape(pass_count, devices * rows, 2 * head_size)
    outputs = []
    masses = []
    for index in range(pass_count):
        out_now, mass_now = attend_rows(
            query_heads[index],
            keyval_heads[index, :, :head_size],
            keyval_heads[index, :, head_size:],
        )
        outputs.append(out_now)
        masses.append(mass_now)
    attended_heads = jnp.stack(outputs)
    log_mass = jnp.stack(masses)
    out_send = attended_heads.reshape(pass_count, devices, sub_rows * head_size).transpose(1, 0, 2)
    out_back = lax.all_to_all(out_send, "seq", split_axis=0, concat_axis=0, tiled=True)
    attended = (
        out_back.reshape(head_count, query_groups, pass_count, sub_rows, head_size)
        .transpose(2, 1, 3, 0, 4)
        .reshape(pass_count, rows, proj_width)
    )
    terms = jnp.einsum(
        "prh,hf->prf",
        attended,
        out_weight,
        preferred_element_type=jnp.float32,
    )
    mixed = (
        add_halves(terms.astype(jnp.bfloat16), 2) + pooled_wide
    )
    return (
        pre_act,
        pooled_wide,
        whole_wide,
        row_scale,
        query_heads,
        keyval_heads,
        attended_heads,
        log_mass,
        mixed,
    )


def shards(features, noise, conv_weight, conv_bias, norm_gain, qkv_weight, out_weight):
    (conv_weight,) = gather_seq([(conv_weight, 1)])
    qkv_weight, out_weight = gather_seq([(qkv_weight, 1), (out_weight, 1)])
    clean = features[0]
    moved = (clean.astype(jnp.float32) + noise[0]).astype(jnp.bfloat16)
    joint = forward(
        jnp.stack([clean, moved]), conv_weight, conv_bias, norm_gain, qkv_weight, out_weight
    )
    clean_run = [item[0:1] for item in joint]
    moved_run = [item[1:2] for item in joint]
    (
        pre_act,
        pooled_wide,
        whole_wide,
        row_scale,
        query_heads,
        keyval_heads,
        attended_heads,
        log_mass,
        mixed,
    ) = [item[0] for item in moved_run]
    clean_mixed = clean_run[8][0]
    rows, half_width = pooled_wide.shape
    positions = pre_act.shape[0]
    proj_width = qkv_weight.shape[2]
    head_size = HD
    head_count = proj_width // head_size
    devices = lax.axis_size("seq")
    query_groups = devices // head_count
    sub_rows = rows // query_groups
    difference = mixed - clean_mixed
    difference_half = difference.astype(jnp.bfloat16)
    difference_whole = lax.all_gather(difference_half, "mp", axis=1, tiled=True)
    out_grad = jnp.einsum(
        "rf,hf->rh",
        difference_whole,
        out_weight,
        preferred_element_type=jnp.float32,
    ).astype(jnp.bfloat16)
    grad_send = (
        out_grad.reshape(query_groups, sub_rows, head_count, head_size)
        .transpose(2, 0, 1, 3)
        .reshape(devices, sub_rows * head_size)
    )
    grad_in = lax.all_to_all(grad_send, "seq", split_axis=0, concat_axis=1, tiled=True)
    grad_heads = grad_in.reshape(devices * sub_rows, head_size)
    query_grad, keyval_grad = attend_back(
        query_heads,
        keyval_heads[:, :head_size],
        keyval_heads[:, head_size:],
        attended_heads,
        log_mass,
        grad_heads,
    )
    query_len = sub_rows * head_size
    both_back = lax.all_to_all(
        jnp.concatenate(
            [
                query_grad.reshape(devices, query_len).astype(jnp.bfloat16),
                keyval_grad.reshape(devices, rows * 2 * head_size).astype(jnp.bfloat16),
            ],
            axis=1,
        ),
        "seq",
        split_axis=0,
        concat_axis=0,
        tiled=True,
    ).astype(jnp.float32)
    query_back = both_back[:, :query_len]
    keyval_back = both_back[:, query_len:]
    query_rows = (
        query_back.reshape(head_count, query_groups, sub_rows, head_size)
        .transpose(1, 2, 0, 3)
        .reshape(rows, proj_width)
        .astype(jnp.bfloat16)
    )
    keyval_rows = jnp.sum(keyval_back.reshape(head_count, query_groups, rows, 2, head_size), axis=1)
    key_rows = (
        keyval_rows[:, :, 0].transpose(1, 0, 2).reshape(rows, proj_width).astype(jnp.bfloat16)
    )
    value_rows = (
        keyval_rows[:, :, 1].transpose(1, 0, 2).reshape(rows, proj_width).astype(jnp.bfloat16)
    )
    grads = jnp.stack([query_rows, key_rows, value_rows])
    normed_terms = jnp.einsum(
        "jrh,jfh->rf",
        grads,
        qkv_weight,
        preferred_element_type=jnp.float32,
    )
    offset_mp = lax.axis_index("mp") * half_width
    gain_own = lax.dynamic_slice_in_dim(norm_gain, offset_mp, half_width, 0)
    normed_grad = add_halves(normed_terms.astype(jnp.bfloat16), 1)
    weighted = lax.psum(jnp.sum(normed_grad * gain_own * pooled_wide, axis=1, keepdims=True), "mp")
    pooled_grad = (
        difference + row_scale * gain_own * normed_grad - pooled_wide * row_scale**3 * weighted / F
    )
    spread = jnp.broadcast_to((0.5 * pooled_grad)[:, None, :], (rows, 2, half_width)).reshape(
        positions, half_width
    )
    gelu_back = jax.vjp(jax.nn.gelu, pre_act)[1]
    pre_grad = gelu_back(spread)[0].astype(jnp.bfloat16)
    reach = KW // 2
    padded = with_halo(pre_grad, (("seq", 0),), reach)
    piece = conv_weight
    running = jnp.zeros((positions, piece.shape[1]), jnp.float32)
    for offset in range(piece.shape[0]):
        lower = 2 * reach - offset
        running = running + jnp.einsum(
            "tf,cf->tc",
            padded[lower : lower + positions],
            piece[offset],
            preferred_element_type=jnp.float32,
        )
    own_grad = running.astype(jnp.bfloat16)
    input_grad = (own_grad.astype(jnp.float32) + swap_mp(own_grad).astype(jnp.float32)).astype(
        jnp.bfloat16
    ).astype(jnp.float32)
    new_noise = noise[0] + step_size * input_grad * lax.rsqrt(
        jnp.mean(input_grad * input_grad, axis=1, keepdims=True) + epsilon
    )
    return (clean_mixed.astype(jnp.bfloat16)[None], new_noise[None])


def solution(mesh):
    return jax.shard_map(
        shards,
        mesh=mesh,
        in_specs=(
            P(("group", "batch"), "seq", None),
            P(("group", "batch"), "seq", None),
            P(None, "seq", "mp"),
            P("mp"),
            P(),
            P(None, "seq", "mp"),
            P("mp", "seq"),
        ),
        out_specs=(P(("group", "batch"), "seq", "mp"), P(("group", "batch"), "seq", None)),
        check_vma=False,
    )
```

```python
import jax
import jax.numpy as jnp
from jax import lax
from jax.sharding import PartitionSpec as P

F = 768
HD = 96
KW = 5


step_size = 0.5
epsilon = 1e-06


def with_halo(cells, sides, width):
    for axis, dim in sides:
        count = lax.axis_size(axis)
        ends = count - 1
        head = lax.slice_in_dim(cells, 0, width, axis=dim)
        tail = lax.slice_in_dim(cells, cells.shape[dim] - width, cells.shape[dim], axis=dim)
        cells = jnp.concatenate(
            [
                lax.ppermute(tail, axis, [(i, (i + 1) % count) for i in range(ends)]),
                cells,
                lax.ppermute(head, axis, [((i + 1) % count, i) for i in range(ends)]),
            ],
            axis=dim,
        )
    return cells


def gather_seq(parts, width):
    spread = ("group", "batch")
    count = lax.axis_size("group") * lax.axis_size("batch")
    ring = lax.axis_size("seq")
    flats = [cells.reshape(-1, width) for cells, _ in parts]
    flat = jnp.concatenate(flats, axis=0) if len(flats) > 1 else flats[0]
    rows = flat.shape[0]
    size = -(-rows // count)
    if size * count != rows:
        flat = jnp.pad(flat, ((0, size * count - rows), (0, 0)))
    piece = lax.dynamic_slice_in_dim(flat, lax.axis_index(spread) * size, size, 0)
    whole = lax.all_gather(piece, ("seq",) + spread, axis=0, tiled=True)
    whole = whole.reshape(ring, count * size, width)
    results = []
    offset = 0
    for (cells, dim), part in zip(parts, flats):
        block = whole[:, offset : offset + part.shape[0]]
        offset += part.shape[0]
        block = jnp.moveaxis(block.reshape((ring,) + cells.shape), 0, dim)
        shape = list(cells.shape)
        shape[dim] = shape[dim] * ring
        results.append(block.reshape(shape))
    return results


def swap_mp(cells):
    return lax.ppermute(cells, "mp", [(0, 1), (1, 0)])


def add_halves(cells, dim):
    half = cells.shape[dim] // 2
    index = lax.axis_index("mp")
    own = lax.dynamic_slice_in_dim(cells, index * half, half, dim)
    other = lax.dynamic_slice_in_dim(cells, (1 - index) * half, half, dim)
    return (own.astype(jnp.float32) + swap_mp(other).astype(jnp.float32)).astype(
        jnp.bfloat16
    ).astype(jnp.float32)


def attend_rows(query, keys, values):
    key_total = keys.shape[0]
    block_len = min(512, key_total)
    head_size = keys.shape[1]
    score_scale = head_size ** (-0.5)
    key_blocks = keys.reshape(key_total // block_len, block_len, head_size)
    value_blocks = values.reshape(key_total // block_len, block_len, head_size)
    query_count = query.shape[0]

    def find_top(carry, key_block):
        row_top, row_mass = carry
        scores = jnp.dot(query, key_block.T, preferred_element_type=jnp.float32) * score_scale
        new_top = jnp.maximum(row_top, jnp.max(scores, axis=1))
        row_mass = row_mass * jnp.exp(row_top - new_top) + jnp.sum(
            jnp.exp(scores - new_top[:, None]), axis=1
        )
        return ((new_top, row_mass), None)

    start_top = jnp.full((query_count,), -1e30, jnp.float32)
    (row_top, row_mass), _ = lax.scan(
        find_top, (start_top, jnp.zeros((query_count,), jnp.float32)), key_blocks
    )
    log_mass = row_top + jnp.log(row_mass)

    def collect(running, blocks):
        key_block, value_block = blocks
        scores = jnp.dot(query, key_block.T, preferred_element_type=jnp.float32) * score_scale
        soft_weights = jnp.exp(scores - log_mass[:, None]).astype(jnp.bfloat16)
        return (
            running + jnp.dot(soft_weights, value_block, preferred_element_type=jnp.float32),
            None,
        )

    running, _ = lax.scan(
        collect, jnp.zeros((query_count, head_size), jnp.float32), (key_blocks, value_blocks)
    )
    return (running.astype(jnp.bfloat16), log_mass)


def attend_back(query, keys, values, attended, log_mass, out_grad):
    key_total = keys.shape[0]
    block_len = min(512, key_total)
    head_size = keys.shape[1]
    score_scale = head_size ** (-0.5)
    key_blocks = keys.reshape(key_total // block_len, block_len, head_size)
    value_blocks = values.reshape(key_total // block_len, block_len, head_size)
    row_dot = jnp.sum(out_grad.astype(jnp.float32) * attended.astype(jnp.float32), axis=1)

    def step_back(query_acc, blocks):
        key_block, value_block = blocks
        scores = jnp.dot(query, key_block.T, preferred_element_type=jnp.float32) * score_scale
        exp_weights = jnp.exp(scores - log_mass[:, None])
        value_part = jnp.einsum(
            "qk,qd->kd",
            exp_weights.astype(jnp.bfloat16),
            out_grad,
            preferred_element_type=jnp.float32,
        )
        prob_grad = jnp.dot(out_grad, value_block.T, preferred_element_type=jnp.float32)
        score_grad = (exp_weights * (prob_grad - row_dot[:, None])).astype(jnp.bfloat16)
        query_acc = (
            query_acc
            + jnp.dot(score_grad, key_block, preferred_element_type=jnp.float32) * score_scale
        )
        key_part = (
            jnp.einsum("qk,qd->kd", score_grad, query, preferred_element_type=jnp.float32)
            * score_scale
        )
        return (query_acc, jnp.concatenate([key_part, value_part], axis=1))

    query_grad, keyval_parts = lax.scan(
        step_back, jnp.zeros((query.shape[0], head_size), jnp.float32), (key_blocks, value_blocks)
    )
    return (query_grad, keyval_parts.reshape(key_total, 2 * head_size))


def forward(stack, conv_weight, conv_bias, norm_gain, qkv_weight, out_weight):
    pass_count, positions, channels = stack.shape
    reach = KW // 2
    half_width = conv_weight.shape[2]
    padded_input = with_halo(stack, (("seq", 1),), reach)
    running = jnp.zeros((pass_count, positions, half_width), jnp.float32)
    piece = conv_weight
    for offset in range(piece.shape[0]):
        running = running + jnp.einsum(
            "ptc,cf->ptf",
            padded_input[:, offset : offset + positions],
            piece[offset],
            preferred_element_type=jnp.float32,
        )
    pre_act = running + conv_bias
    paired = jax.nn.gelu(pre_act).reshape(pass_count, positions // 2, 2, half_width)
    pooled = (0.5 * (paired[:, :, 0] + paired[:, :, 1])).astype(jnp.bfloat16)
    pooled_wide = lax.optimization_barrier(pooled).astype(jnp.float32)
    whole = lax.all_gather(pooled, "mp", axis=2, tiled=True)
    whole_wide = whole.astype(jnp.float32)
    row_scale = lax.rsqrt(jnp.mean(whole_wide * whole_wide, axis=2, keepdims=True) + epsilon)
    normed = (whole_wide * row_scale * norm_gain).astype(jnp.bfloat16)
    rows = positions // 2
    proj_width = qkv_weight.shape[2]
    projected = jnp.einsum(
        "prf,jfh->jprh",
        normed,
        qkv_weight,
        preferred_element_type=jnp.float32,
    ).astype(jnp.bfloat16)
    head_size = HD
    head_count = proj_width // head_size
    devices = lax.axis_size("seq")
    query_groups = devices // head_count
    sub_rows = rows // query_groups
    query_send = (
        projected[0]
        .reshape(pass_count, query_groups, sub_rows, head_count, head_size)
        .transpose(3, 1, 0, 2, 4)
        .reshape(devices, pass_count, sub_rows * head_size)
    )
    keyval = jnp.concatenate(
        [
            projected[1].reshape(pass_count, rows, head_count, head_size),
            projected[2].reshape(pass_count, rows, head_count, head_size),
        ],
        axis=3,
    )
    keyval_flat = keyval.transpose(2, 0, 1, 3).reshape(
        head_count, 1, pass_count, rows * 2 * head_size
    )
    keyval_send = jnp.broadcast_to(
        keyval_flat, (head_count, query_groups, pass_count, rows * 2 * head_size)
    ).reshape(devices, pass_count, rows * 2 * head_size)
    query_len = query_send.shape[2]
    both_in = lax.all_to_all(
        jnp.concatenate([query_send, keyval_send], axis=2),
        "seq",
        split_axis=0,
        concat_axis=2,
        tiled=True,
    ).reshape(pass_count, devices, query_len + keyval_send.shape[2])
    query_heads = both_in[:, :, :query_len].reshape(pass_count, devices * sub_rows, head_size)
    keyval_heads = both_in[:, :, query_len:].reshape(pass_count, devices * rows, 2 * head_size)
    outputs = []
    masses = []
    for index in range(pass_count):
        out_now, mass_now = attend_rows(
            query_heads[index],
            keyval_heads[index, :, :head_size],
            keyval_heads[index, :, head_size:],
        )
        outputs.append(out_now)
        masses.append(mass_now)
    attended_heads = jnp.stack(outputs)
    log_mass = jnp.stack(masses)
    out_send = attended_heads.reshape(pass_count, devices, sub_rows * head_size).transpose(1, 0, 2)
    out_back = lax.all_to_all(out_send, "seq", split_axis=0, concat_axis=0, tiled=True)
    attended = (
        out_back.reshape(head_count, query_groups, pass_count, sub_rows, head_size)
        .transpose(2, 1, 3, 0, 4)
        .reshape(pass_count, rows, proj_width)
    )
    terms = jnp.einsum(
        "prh,hf->prf",
        attended,
        out_weight,
        preferred_element_type=jnp.float32,
    )
    mixed = (
        add_halves(terms.astype(jnp.bfloat16), 2) + pooled_wide
    )
    return (
        pre_act,
        pooled_wide,
        whole_wide,
        row_scale,
        query_heads,
        keyval_heads,
        attended_heads,
        log_mass,
        mixed,
    )


def shards(features, noise, conv_weight, conv_bias, norm_gain, qkv_weight, out_weight):
    width = conv_weight.shape[-1]
    (conv_weight,) = gather_seq([(conv_weight, 1)], width)
    qkv_weight, out_weight = gather_seq([(qkv_weight, 1), (out_weight, 1)], width)
    clean = features[0]
    moved = (clean.astype(jnp.float32) + noise[0]).astype(jnp.bfloat16)
    joint = forward(
        jnp.stack([clean, moved]), conv_weight, conv_bias, norm_gain, qkv_weight, out_weight
    )
    clean_run = [item[0:1] for item in joint]
    moved_run = [item[1:2] for item in joint]
    (
        pre_act,
        pooled_wide,
        whole_wide,
        row_scale,
        query_heads,
        keyval_heads,
        attended_heads,
        log_mass,
        mixed,
    ) = [item[0] for item in moved_run]
    clean_mixed = clean_run[8][0]
    rows, half_width = pooled_wide.shape
    positions = pre_act.shape[0]
    proj_width = qkv_weight.shape[2]
    head_size = HD
    head_count = proj_width // head_size
    devices = lax.axis_size("seq")
    query_groups = devices // head_count
    sub_rows = rows // query_groups
    difference = mixed - clean_mixed
    difference_half = difference.astype(jnp.bfloat16)
    difference_whole = lax.all_gather(difference_half, "mp", axis=1, tiled=True)
    out_grad = jnp.einsum(
        "rf,hf->rh",
        difference_whole,
        out_weight,
        preferred_element_type=jnp.float32,
    ).astype(jnp.bfloat16)
    grad_send = (
        out_grad.reshape(query_groups, sub_rows, head_count, head_size)
        .transpose(2, 0, 1, 3)
        .reshape(devices, sub_rows * head_size)
    )
    grad_in = lax.all_to_all(grad_send, "seq", split_axis=0, concat_axis=1, tiled=True)
    grad_heads = grad_in.reshape(devices * sub_rows, head_size)
    query_grad, keyval_grad = attend_back(
        query_heads,
        keyval_heads[:, :head_size],
        keyval_heads[:, head_size:],
        attended_heads,
        log_mass,
        grad_heads,
    )
    query_len = sub_rows * head_size
    both_back = lax.all_to_all(
        jnp.concatenate(
            [
                query_grad.reshape(devices, query_len).astype(jnp.bfloat16),
                keyval_grad.reshape(devices, rows * 2 * head_size).astype(jnp.bfloat16),
            ],
            axis=1,
        ),
        "seq",
        split_axis=0,
        concat_axis=0,
        tiled=True,
    ).astype(jnp.float32)
    query_back = both_back[:, :query_len]
    keyval_back = both_back[:, query_len:]
    query_rows = (
        query_back.reshape(head_count, query_groups, sub_rows, head_size)
        .transpose(1, 2, 0, 3)
        .reshape(rows, proj_width)
        .astype(jnp.bfloat16)
    )
    keyval_rows = jnp.sum(keyval_back.reshape(head_count, query_groups, rows, 2, head_size), axis=1)
    key_rows = (
        keyval_rows[:, :, 0].transpose(1, 0, 2).reshape(rows, proj_width).astype(jnp.bfloat16)
    )
    value_rows = (
        keyval_rows[:, :, 1].transpose(1, 0, 2).reshape(rows, proj_width).astype(jnp.bfloat16)
    )
    grads = jnp.stack([query_rows, key_rows, value_rows])
    normed_terms = jnp.einsum(
        "jrh,jfh->rf",
        grads,
        qkv_weight,
        preferred_element_type=jnp.float32,
    )
    offset_mp = lax.axis_index("mp") * half_width
    gain_own = lax.dynamic_slice_in_dim(norm_gain, offset_mp, half_width, 0)
    normed_grad = add_halves(normed_terms.astype(jnp.bfloat16), 1)
    weighted = lax.psum(jnp.sum(normed_grad * gain_own * pooled_wide, axis=1, keepdims=True), "mp")
    pooled_grad = (
        difference + row_scale * gain_own * normed_grad - pooled_wide * row_scale**3 * weighted / F
    )
    spread = jnp.broadcast_to((0.5 * pooled_grad)[:, None, :], (rows, 2, half_width)).reshape(
        positions, half_width
    )
    gelu_back = jax.vjp(jax.nn.gelu, pre_act)[1]
    pre_grad = gelu_back(spread)[0].astype(jnp.bfloat16)
    reach = KW // 2
    padded = with_halo(pre_grad, (("seq", 0),), reach)
    piece = conv_weight
    running = jnp.zeros((positions, piece.shape[1]), jnp.float32)
    for offset in range(piece.shape[0]):
        lower = 2 * reach - offset
        running = running + jnp.einsum(
            "tf,cf->tc",
            padded[lower : lower + positions],
            piece[offset],
            preferred_element_type=jnp.float32,
        )
    own_grad = running.astype(jnp.bfloat16)
    input_grad = (own_grad.astype(jnp.float32) + swap_mp(own_grad).astype(jnp.float32)).astype(
        jnp.bfloat16
    ).astype(jnp.float32)
    new_noise = noise[0] + step_size * input_grad * lax.rsqrt(
        jnp.mean(input_grad * input_grad, axis=1, keepdims=True) + epsilon
    )
    return (clean_mixed.astype(jnp.bfloat16)[None], new_noise[None])


def solution(mesh):
    return jax.shard_map(
        shards,
        mesh=mesh,
        in_specs=(
            P(("group", "batch"), "seq", None),
            P(("group", "batch"), "seq", None),
            P(None, "seq", "mp"),
            P("mp"),
            P(),
            P(None, "seq", "mp"),
            P("mp", "seq"),
        ),
        out_specs=(P(("group", "batch"), "seq", "mp"), P(("group", "batch"), "seq", None)),
        check_vma=False,
    )
```

```python
import jax
import jax.numpy as jnp
from jax import lax
from jax.sharding import PartitionSpec as P

F = 768
HD = 96
KW = 5


step_size = 0.5
epsilon = 1e-06


def with_halo(cells, sides, width):
    for axis, dim in sides:
        count = lax.axis_size(axis)
        ends = count - 1
        head = lax.slice_in_dim(cells, 0, width, axis=dim)
        tail = lax.slice_in_dim(cells, cells.shape[dim] - width, cells.shape[dim], axis=dim)
        cells = jnp.concatenate(
            [
                lax.ppermute(tail, axis, [(i, (i + 1) % count) for i in range(ends)]),
                cells,
                lax.ppermute(head, axis, [((i + 1) % count, i) for i in range(ends)]),
            ],
            axis=dim,
        )
    return cells


def ring_gather(piece):
    ring = lax.axis_size("seq")
    place = lax.axis_index("seq")
    along = jnp.zeros((ring,) + piece.shape, piece.dtype)
    along = lax.dynamic_update_slice_in_dim(along, piece[None], place, 0)
    for shift in range(1, ring):
        arrived = lax.ppermute(piece, "seq", [(i, (i + shift) % ring) for i in range(ring)])
        along = lax.dynamic_update_slice_in_dim(along, arrived[None], (place + ring - shift) % ring, 0)
    return along


def gather_seq(parts, width, direct=0):
    spread = ("group", "batch")
    count = lax.axis_size("group") * lax.axis_size("batch")
    ring = lax.axis_size("seq")
    flats = [cells.reshape(-1, width) for cells, _ in parts]
    flat = jnp.concatenate(flats, axis=0) if len(flats) > 1 else flats[0]
    rows = flat.shape[0]
    if ring > 8:
        direct = 0
    split = rows - direct
    size = -(-split // count)
    head = flat[:split]
    if size * count != split:
        head = jnp.pad(head, ((0, size * count - split), (0, 0)))
    piece = lax.dynamic_slice_in_dim(head, lax.axis_index(spread) * size, size, 0)
    if ring <= 8:
        along = ring_gather(piece)
    else:
        along = lax.all_gather(piece, "seq", axis=0, tiled=False)
    whole = lax.all_gather(along, spread, axis=0, tiled=False)
    whole = whole.transpose(1, 0, 2, 3).reshape(ring, count * size, width)[:, :split]
    if direct:
        whole = jnp.concatenate([whole, ring_gather(flat[split:])], axis=1)
    results = []
    offset = 0
    for (cells, dim), part in zip(parts, flats):
        block = whole[:, offset : offset + part.shape[0]]
        offset += part.shape[0]
        block = jnp.moveaxis(block.reshape((ring,) + cells.shape), 0, dim)
        shape = list(cells.shape)
        shape[dim] = shape[dim] * ring
        results.append(block.reshape(shape))
    return results


def swap_mp(cells):
    return lax.ppermute(cells, "mp", [(0, 1), (1, 0)])


def add_halves(cells, dim):
    half = cells.shape[dim] // 2
    index = lax.axis_index("mp")
    own = lax.dynamic_slice_in_dim(cells, index * half, half, dim)
    other = lax.dynamic_slice_in_dim(cells, (1 - index) * half, half, dim)
    return (own.astype(jnp.float32) + swap_mp(other).astype(jnp.float32)).astype(
        jnp.bfloat16
    ).astype(jnp.float32)


def attend_rows(query, keys, values):
    key_total = keys.shape[0]
    block_len = min(512, key_total)
    head_size = keys.shape[1]
    score_scale = head_size ** (-0.5)
    key_blocks = keys.reshape(key_total // block_len, block_len, head_size)
    value_blocks = values.reshape(key_total // block_len, block_len, head_size)
    query_count = query.shape[0]

    def find_top(carry, key_block):
        row_top, row_mass = carry
        scores = jnp.dot(query, key_block.T, preferred_element_type=jnp.float32) * score_scale
        new_top = jnp.maximum(row_top, jnp.max(scores, axis=1))
        row_mass = row_mass * jnp.exp(row_top - new_top) + jnp.sum(
            jnp.exp(scores - new_top[:, None]), axis=1
        )
        return ((new_top, row_mass), None)

    start_top = jnp.full((query_count,), -1e30, jnp.float32)
    (row_top, row_mass), _ = lax.scan(
        find_top, (start_top, jnp.zeros((query_count,), jnp.float32)), key_blocks
    )
    log_mass = row_top + jnp.log(row_mass)

    def collect(running, blocks):
        key_block, value_block = blocks
        scores = jnp.dot(query, key_block.T, preferred_element_type=jnp.float32) * score_scale
        soft_weights = jnp.exp(scores - log_mass[:, None]).astype(jnp.bfloat16)
        return (
            running + jnp.dot(soft_weights, value_block, preferred_element_type=jnp.float32),
            None,
        )

    running, _ = lax.scan(
        collect, jnp.zeros((query_count, head_size), jnp.float32), (key_blocks, value_blocks)
    )
    return (running.astype(jnp.bfloat16), log_mass)


def attend_back(query, keys, values, attended, log_mass, out_grad):
    key_total = keys.shape[0]
    block_len = min(512, key_total)
    head_size = keys.shape[1]
    score_scale = head_size ** (-0.5)
    key_blocks = keys.reshape(key_total // block_len, block_len, head_size)
    value_blocks = values.reshape(key_total // block_len, block_len, head_size)
    row_dot = jnp.sum(out_grad.astype(jnp.float32) * attended.astype(jnp.float32), axis=1)

    def step_back(query_acc, blocks):
        key_block, value_block = blocks
        scores = jnp.dot(query, key_block.T, preferred_element_type=jnp.float32) * score_scale
        exp_weights = jnp.exp(scores - log_mass[:, None])
        value_part = jnp.einsum(
            "qk,qd->kd",
            exp_weights.astype(jnp.bfloat16),
            out_grad,
            preferred_element_type=jnp.float32,
        )
        prob_grad = jnp.dot(out_grad, value_block.T, preferred_element_type=jnp.float32)
        score_grad = (exp_weights * (prob_grad - row_dot[:, None])).astype(jnp.bfloat16)
        query_acc = (
            query_acc
            + jnp.dot(score_grad, key_block, preferred_element_type=jnp.float32) * score_scale
        )
        key_part = (
            jnp.einsum("qk,qd->kd", score_grad, query, preferred_element_type=jnp.float32)
            * score_scale
        )
        return (query_acc, jnp.concatenate([key_part, value_part], axis=1))

    query_grad, keyval_parts = lax.scan(
        step_back, jnp.zeros((query.shape[0], head_size), jnp.float32), (key_blocks, value_blocks)
    )
    return (query_grad, keyval_parts.reshape(key_total, 2 * head_size))


def forward(stack, conv_weight, conv_bias, norm_gain, qkv_weight, out_weight):
    pass_count, positions, channels = stack.shape
    reach = KW // 2
    half_width = conv_weight.shape[2]
    padded_input = with_halo(stack, (("seq", 1),), reach)
    running = jnp.zeros((pass_count, positions, half_width), jnp.float32)
    piece = conv_weight
    for offset in range(piece.shape[0]):
        running = running + jnp.einsum(
            "ptc,cf->ptf",
            padded_input[:, offset : offset + positions],
            piece[offset],
            preferred_element_type=jnp.float32,
        )
    pre_act = running + conv_bias
    paired = jax.nn.gelu(pre_act).reshape(pass_count, positions // 2, 2, half_width)
    pooled = (0.5 * (paired[:, :, 0] + paired[:, :, 1])).astype(jnp.bfloat16)
    pooled_wide = lax.optimization_barrier(pooled).astype(jnp.float32)
    whole = lax.all_gather(pooled, "mp", axis=2, tiled=True)
    whole_wide = whole.astype(jnp.float32)
    row_scale = lax.rsqrt(jnp.mean(whole_wide * whole_wide, axis=2, keepdims=True) + epsilon)
    normed = (whole_wide * row_scale * norm_gain).astype(jnp.bfloat16)
    rows = positions // 2
    proj_width = qkv_weight.shape[2]
    projected = jnp.einsum(
        "prf,jfh->jprh",
        normed,
        qkv_weight,
        preferred_element_type=jnp.float32,
    ).astype(jnp.bfloat16)
    head_size = HD
    head_count = proj_width // head_size
    devices = lax.axis_size("seq")
    query_groups = devices // head_count
    sub_rows = rows // query_groups
    query_send = (
        projected[0]
        .reshape(pass_count, query_groups, sub_rows, head_count, head_size)
        .transpose(3, 1, 0, 2, 4)
        .reshape(devices, pass_count, sub_rows * head_size)
    )
    keyval = jnp.concatenate(
        [
            projected[1].reshape(pass_count, rows, head_count, head_size),
            projected[2].reshape(pass_count, rows, head_count, head_size),
        ],
        axis=3,
    )
    keyval_flat = keyval.transpose(2, 0, 1, 3).reshape(
        head_count, 1, pass_count, rows * 2 * head_size
    )
    keyval_send = jnp.broadcast_to(
        keyval_flat, (head_count, query_groups, pass_count, rows * 2 * head_size)
    ).reshape(devices, pass_count, rows * 2 * head_size)
    query_len = query_send.shape[2]
    both_in = lax.all_to_all(
        jnp.concatenate([query_send, keyval_send], axis=2),
        "seq",
        split_axis=0,
        concat_axis=2,
        tiled=True,
    ).reshape(pass_count, devices, query_len + keyval_send.shape[2])
    query_heads = both_in[:, :, :query_len].reshape(pass_count, devices * sub_rows, head_size)
    keyval_heads = both_in[:, :, query_len:].reshape(pass_count, devices * rows, 2 * head_size)
    outputs = []
    masses = []
    for index in range(pass_count):
        out_now, mass_now = attend_rows(
            query_heads[index],
            keyval_heads[index, :, :head_size],
            keyval_heads[index, :, head_size:],
        )
        outputs.append(out_now)
        masses.append(mass_now)
    attended_heads = jnp.stack(outputs)
    log_mass = jnp.stack(masses)
    out_send = attended_heads.reshape(pass_count, devices, sub_rows * head_size).transpose(1, 0, 2)
    out_back = lax.all_to_all(out_send, "seq", split_axis=0, concat_axis=0, tiled=True)
    attended = (
        out_back.reshape(head_count, query_groups, pass_count, sub_rows, head_size)
        .transpose(2, 1, 3, 0, 4)
        .reshape(pass_count, rows, proj_width)
    )
    terms = jnp.einsum(
        "prh,hf->prf",
        attended,
        out_weight,
        preferred_element_type=jnp.float32,
    )
    mixed = (
        add_halves(terms.astype(jnp.bfloat16), 2) + pooled_wide
    )
    return (
        pre_act,
        pooled_wide,
        whole_wide,
        row_scale,
        query_heads,
        keyval_heads,
        attended_heads,
        log_mass,
        mixed,
    )


def shards(features, noise, conv_weight, conv_bias, norm_gain, qkv_weight, out_weight):
    width = conv_weight.shape[-1]
    conv_rows = conv_weight.size // width
    (conv_weight,) = gather_seq([(conv_weight, 1)], width, conv_rows // 2 // 16 * 16)
    qkv_weight, out_weight = gather_seq([(qkv_weight, 1), (out_weight, 1)], width)
    clean = features[0]
    moved = (clean.astype(jnp.float32) + noise[0]).astype(jnp.bfloat16)
    joint = forward(
        jnp.stack([clean, moved]), conv_weight, conv_bias, norm_gain, qkv_weight, out_weight
    )
    clean_run = [item[0:1] for item in joint]
    moved_run = [item[1:2] for item in joint]
    (
        pre_act,
        pooled_wide,
        whole_wide,
        row_scale,
        query_heads,
        keyval_heads,
        attended_heads,
        log_mass,
        mixed,
    ) = [item[0] for item in moved_run]
    clean_mixed = clean_run[8][0]
    rows, half_width = pooled_wide.shape
    positions = pre_act.shape[0]
    proj_width = qkv_weight.shape[2]
    head_size = HD
    head_count = proj_width // head_size
    devices = lax.axis_size("seq")
    query_groups = devices // head_count
    sub_rows = rows // query_groups
    difference = mixed - clean_mixed
    difference_half = difference.astype(jnp.bfloat16)
    difference_whole = lax.all_gather(difference_half, "mp", axis=1, tiled=True)
    out_grad = jnp.einsum(
        "rf,hf->rh",
        difference_whole,
        out_weight,
        preferred_element_type=jnp.float32,
    ).astype(jnp.bfloat16)
    grad_send = (
        out_grad.reshape(query_groups, sub_rows, head_count, head_size)
        .transpose(2, 0, 1, 3)
        .reshape(devices, sub_rows * head_size)
    )
    grad_in = lax.all_to_all(grad_send, "seq", split_axis=0, concat_axis=1, tiled=True)
    grad_heads = grad_in.reshape(devices * sub_rows, head_size)
    query_grad, keyval_grad = attend_back(
        query_heads,
        keyval_heads[:, :head_size],
        keyval_heads[:, head_size:],
        attended_heads,
        log_mass,
        grad_heads,
    )
    query_len = sub_rows * head_size
    both_back = lax.all_to_all(
        jnp.concatenate(
            [
                query_grad.reshape(devices, query_len).astype(jnp.bfloat16),
                keyval_grad.reshape(devices, rows * 2 * head_size).astype(jnp.bfloat16),
            ],
            axis=1,
        ),
        "seq",
        split_axis=0,
        concat_axis=0,
        tiled=True,
    ).astype(jnp.float32)
    query_back = both_back[:, :query_len]
    keyval_back = both_back[:, query_len:]
    query_rows = (
        query_back.reshape(head_count, query_groups, sub_rows, head_size)
        .transpose(1, 2, 0, 3)
        .reshape(rows, proj_width)
        .astype(jnp.bfloat16)
    )
    keyval_rows = jnp.sum(keyval_back.reshape(head_count, query_groups, rows, 2, head_size), axis=1)
    key_rows = (
        keyval_rows[:, :, 0].transpose(1, 0, 2).reshape(rows, proj_width).astype(jnp.bfloat16)
    )
    value_rows = (
        keyval_rows[:, :, 1].transpose(1, 0, 2).reshape(rows, proj_width).astype(jnp.bfloat16)
    )
    grads = jnp.stack([query_rows, key_rows, value_rows])
    normed_terms = jnp.einsum(
        "jrh,jfh->rf",
        grads,
        qkv_weight,
        preferred_element_type=jnp.float32,
    )
    offset_mp = lax.axis_index("mp") * half_width
    gain_own = lax.dynamic_slice_in_dim(norm_gain, offset_mp, half_width, 0)
    normed_grad = add_halves(normed_terms.astype(jnp.bfloat16), 1)
    weighted = lax.psum(jnp.sum(normed_grad * gain_own * pooled_wide, axis=1, keepdims=True), "mp")
    pooled_grad = (
        difference + row_scale * gain_own * normed_grad - pooled_wide * row_scale**3 * weighted / F
    )
    spread = jnp.broadcast_to((0.5 * pooled_grad)[:, None, :], (rows, 2, half_width)).reshape(
        positions, half_width
    )
    gelu_back = jax.vjp(jax.nn.gelu, pre_act)[1]
    pre_grad = gelu_back(spread)[0].astype(jnp.bfloat16)
    reach = KW // 2
    padded = with_halo(pre_grad, (("seq", 0),), reach)
    piece = conv_weight
    running = jnp.zeros((positions, piece.shape[1]), jnp.float32)
    for offset in range(piece.shape[0]):
        lower = 2 * reach - offset
        running = running + jnp.einsum(
            "tf,cf->tc",
            padded[lower : lower + positions],
            piece[offset],
            preferred_element_type=jnp.float32,
        )
    own_grad = running.astype(jnp.bfloat16)
    input_grad = (own_grad.astype(jnp.float32) + swap_mp(own_grad).astype(jnp.float32)).astype(
        jnp.bfloat16
    ).astype(jnp.float32)
    new_noise = noise[0] + step_size * input_grad * lax.rsqrt(
        jnp.mean(input_grad * input_grad, axis=1, keepdims=True) + epsilon
    )
    return (clean_mixed.astype(jnp.bfloat16)[None], new_noise[None])


def solution(mesh):
    return jax.shard_map(
        shards,
        mesh=mesh,
        in_specs=(
            P(("group", "batch"), "seq", None),
            P(("group", "batch"), "seq", None),
            P(None, "seq", "mp"),
            P("mp"),
            P(),
            P(None, "seq", "mp"),
            P("mp", "seq"),
        ),
        out_specs=(P(("group", "batch"), "seq", "mp"), P(("group", "batch"), "seq", None)),
        check_vma=False,
    )
```

```python
import jax
import jax.numpy as jnp
from jax import lax
from jax.sharding import PartitionSpec as P

F = 768
HD = 96
KW = 5


step_size = 0.5
epsilon = 1e-06


def with_halo(cells, sides, width):
    for axis, dim in sides:
        count = lax.axis_size(axis)
        ends = count - 1
        head = lax.slice_in_dim(cells, 0, width, axis=dim)
        tail = lax.slice_in_dim(cells, cells.shape[dim] - width, cells.shape[dim], axis=dim)
        cells = jnp.concatenate(
            [
                lax.ppermute(tail, axis, [(i, (i + 1) % count) for i in range(ends)]),
                cells,
                lax.ppermute(head, axis, [((i + 1) % count, i) for i in range(ends)]),
            ],
            axis=dim,
        )
    return cells


def ring_gather(piece):
    ring = lax.axis_size("seq")
    place = lax.axis_index("seq")
    along = jnp.zeros((ring,) + piece.shape, piece.dtype)
    along = lax.dynamic_update_slice_in_dim(along, piece[None], place, 0)
    for shift in range(1, ring):
        arrived = lax.ppermute(piece, "seq", [(i, (i + shift) % ring) for i in range(ring)])
        along = lax.dynamic_update_slice_in_dim(along, arrived[None], (place + ring - shift) % ring, 0)
    return along


def gather_seq(parts, width):
    spread = ("group", "batch")
    count = lax.axis_size("group") * lax.axis_size("batch")
    ring = lax.axis_size("seq")
    flats = [cells.reshape(-1, width) for cells, _ in parts]
    flat = jnp.concatenate(flats, axis=0) if len(flats) > 1 else flats[0]
    rows = flat.shape[0]
    paired = lax.axis_size("group") == 2 and lax.axis_size("batch") == 2 and ring <= 8
    halves = rows // 2 // (4 * count) * (4 * count) if paired else 0
    split = rows - halves
    size = -(-split // count)
    head = flat[:split]
    if size * count != split:
        head = jnp.pad(head, ((0, size * count - split), (0, 0)))
    piece = lax.dynamic_slice_in_dim(head, lax.axis_index(spread) * size, size, 0)
    if ring <= 8:
        along = ring_gather(piece)
    else:
        along = lax.all_gather(piece, "seq", axis=0, tiled=False)
    whole = lax.all_gather(along, spread, axis=0, tiled=False)
    whole = whole.transpose(1, 0, 2, 3).reshape(ring, count * size, width)[:, :split]
    if halves:
        tail = flat[split:]
        half = halves // 2
        parity = (lax.axis_index("group") + lax.axis_index("batch")) % 2
        mine = ring_gather(lax.dynamic_slice_in_dim(tail, parity * half, half, 0))
        swap = [(0, 1), (1, 0)]
        other = jnp.concatenate(
            [
                lax.ppermute(mine[:, : half // 2], "batch", swap),
                lax.ppermute(mine[:, half // 2 :], "group", swap),
            ],
            axis=1,
        )
        both = jnp.where(
            parity == 0,
            jnp.concatenate([mine, other], axis=1),
            jnp.concatenate([other, mine], axis=1),
        )
        whole = jnp.concatenate([whole, both], axis=1)
    results = []
    offset = 0
    for (cells, dim), part in zip(parts, flats):
        block = whole[:, offset : offset + part.shape[0]]
        offset += part.shape[0]
        block = jnp.moveaxis(block.reshape((ring,) + cells.shape), 0, dim)
        shape = list(cells.shape)
        shape[dim] = shape[dim] * ring
        results.append(block.reshape(shape))
    return results


def swap_mp(cells):
    return lax.ppermute(cells, "mp", [(0, 1), (1, 0)])


def add_halves(cells, dim):
    half = cells.shape[dim] // 2
    index = lax.axis_index("mp")
    own = lax.dynamic_slice_in_dim(cells, index * half, half, dim)
    other = lax.dynamic_slice_in_dim(cells, (1 - index) * half, half, dim)
    return (own.astype(jnp.float32) + swap_mp(other).astype(jnp.float32)).astype(
        jnp.bfloat16
    ).astype(jnp.float32)


def attend_rows(query, keys, values):
    key_total = keys.shape[0]
    block_len = min(512, key_total)
    head_size = keys.shape[1]
    score_scale = head_size ** (-0.5)
    key_blocks = keys.reshape(key_total // block_len, block_len, head_size)
    value_blocks = values.reshape(key_total // block_len, block_len, head_size)
    query_count = query.shape[0]

    def find_top(carry, key_block):
        row_top, row_mass = carry
        scores = jnp.dot(query, key_block.T, preferred_element_type=jnp.float32) * score_scale
        new_top = jnp.maximum(row_top, jnp.max(scores, axis=1))
        row_mass = row_mass * jnp.exp(row_top - new_top) + jnp.sum(
            jnp.exp(scores - new_top[:, None]), axis=1
        )
        return ((new_top, row_mass), None)

    start_top = jnp.full((query_count,), -1e30, jnp.float32)
    (row_top, row_mass), _ = lax.scan(
        find_top, (start_top, jnp.zeros((query_count,), jnp.float32)), key_blocks
    )
    log_mass = row_top + jnp.log(row_mass)

    def collect(running, blocks):
        key_block, value_block = blocks
        scores = jnp.dot(query, key_block.T, preferred_element_type=jnp.float32) * score_scale
        soft_weights = jnp.exp(scores - log_mass[:, None]).astype(jnp.bfloat16)
        return (
            running + jnp.dot(soft_weights, value_block, preferred_element_type=jnp.float32),
            None,
        )

    running, _ = lax.scan(
        collect, jnp.zeros((query_count, head_size), jnp.float32), (key_blocks, value_blocks)
    )
    return (running.astype(jnp.bfloat16), log_mass)


def attend_back(query, keys, values, attended, log_mass, out_grad):
    key_total = keys.shape[0]
    block_len = min(512, key_total)
    head_size = keys.shape[1]
    score_scale = head_size ** (-0.5)
    key_blocks = keys.reshape(key_total // block_len, block_len, head_size)
    value_blocks = values.reshape(key_total // block_len, block_len, head_size)
    row_dot = jnp.sum(out_grad.astype(jnp.float32) * attended.astype(jnp.float32), axis=1)

    def step_back(query_acc, blocks):
        key_block, value_block = blocks
        scores = jnp.dot(query, key_block.T, preferred_element_type=jnp.float32) * score_scale
        exp_weights = jnp.exp(scores - log_mass[:, None])
        value_part = jnp.einsum(
            "qk,qd->kd",
            exp_weights.astype(jnp.bfloat16),
            out_grad,
            preferred_element_type=jnp.float32,
        )
        prob_grad = jnp.dot(out_grad, value_block.T, preferred_element_type=jnp.float32)
        score_grad = (exp_weights * (prob_grad - row_dot[:, None])).astype(jnp.bfloat16)
        query_acc = (
            query_acc
            + jnp.dot(score_grad, key_block, preferred_element_type=jnp.float32) * score_scale
        )
        key_part = (
            jnp.einsum("qk,qd->kd", score_grad, query, preferred_element_type=jnp.float32)
            * score_scale
        )
        return (query_acc, jnp.concatenate([key_part, value_part], axis=1))

    query_grad, keyval_parts = lax.scan(
        step_back, jnp.zeros((query.shape[0], head_size), jnp.float32), (key_blocks, value_blocks)
    )
    return (query_grad, keyval_parts.reshape(key_total, 2 * head_size))


def forward(stack, conv_weight, conv_bias, norm_gain, qkv_weight, out_weight):
    pass_count, positions, channels = stack.shape
    reach = KW // 2
    half_width = conv_weight.shape[2]
    padded_input = with_halo(stack, (("seq", 1),), reach)
    running = jnp.zeros((pass_count, positions, half_width), jnp.float32)
    piece = conv_weight
    for offset in range(piece.shape[0]):
        running = running + jnp.einsum(
            "ptc,cf->ptf",
            padded_input[:, offset : offset + positions],
            piece[offset],
            preferred_element_type=jnp.float32,
        )
    pre_act = running + conv_bias
    paired = jax.nn.gelu(pre_act).reshape(pass_count, positions // 2, 2, half_width)
    pooled = (0.5 * (paired[:, :, 0] + paired[:, :, 1])).astype(jnp.bfloat16)
    pooled_wide = lax.optimization_barrier(pooled).astype(jnp.float32)
    whole = lax.all_gather(pooled, "mp", axis=2, tiled=True)
    whole_wide = whole.astype(jnp.float32)
    row_scale = lax.rsqrt(jnp.mean(whole_wide * whole_wide, axis=2, keepdims=True) + epsilon)
    normed = (whole_wide * row_scale * norm_gain).astype(jnp.bfloat16)
    rows = positions // 2
    proj_width = qkv_weight.shape[2]
    projected = jnp.einsum(
        "prf,jfh->jprh",
        normed,
        qkv_weight,
        preferred_element_type=jnp.float32,
    ).astype(jnp.bfloat16)
    head_size = HD
    head_count = proj_width // head_size
    devices = lax.axis_size("seq")
    query_groups = devices // head_count
    sub_rows = rows // query_groups
    query_send = (
        projected[0]
        .reshape(pass_count, query_groups, sub_rows, head_count, head_size)
        .transpose(3, 1, 0, 2, 4)
        .reshape(devices, pass_count, sub_rows * head_size)
    )
    keyval = jnp.concatenate(
        [
            projected[1].reshape(pass_count, rows, head_count, head_size),
            projected[2].reshape(pass_count, rows, head_count, head_size),
        ],
        axis=3,
    )
    keyval_flat = keyval.transpose(2, 0, 1, 3).reshape(
        head_count, 1, pass_count, rows * 2 * head_size
    )
    keyval_send = jnp.broadcast_to(
        keyval_flat, (head_count, query_groups, pass_count, rows * 2 * head_size)
    ).reshape(devices, pass_count, rows * 2 * head_size)
    query_len = query_send.shape[2]
    both_in = lax.all_to_all(
        jnp.concatenate([query_send, keyval_send], axis=2),
        "seq",
        split_axis=0,
        concat_axis=2,
        tiled=True,
    ).reshape(pass_count, devices, query_len + keyval_send.shape[2])
    query_heads = both_in[:, :, :query_len].reshape(pass_count, devices * sub_rows, head_size)
    keyval_heads = both_in[:, :, query_len:].reshape(pass_count, devices * rows, 2 * head_size)
    outputs = []
    masses = []
    for index in range(pass_count):
        out_now, mass_now = attend_rows(
            query_heads[index],
            keyval_heads[index, :, :head_size],
            keyval_heads[index, :, head_size:],
        )
        outputs.append(out_now)
        masses.append(mass_now)
    attended_heads = jnp.stack(outputs)
    log_mass = jnp.stack(masses)
    out_send = attended_heads.reshape(pass_count, devices, sub_rows * head_size).transpose(1, 0, 2)
    out_back = lax.all_to_all(out_send, "seq", split_axis=0, concat_axis=0, tiled=True)
    attended = (
        out_back.reshape(head_count, query_groups, pass_count, sub_rows, head_size)
        .transpose(2, 1, 3, 0, 4)
        .reshape(pass_count, rows, proj_width)
    )
    terms = jnp.einsum(
        "prh,hf->prf",
        attended,
        out_weight,
        preferred_element_type=jnp.float32,
    )
    mixed = (
        add_halves(terms.astype(jnp.bfloat16), 2) + pooled_wide
    )
    return (
        pre_act,
        pooled_wide,
        whole_wide,
        row_scale,
        query_heads,
        keyval_heads,
        attended_heads,
        log_mass,
        mixed,
    )


def shards(features, noise, conv_weight, conv_bias, norm_gain, qkv_weight, out_weight):
    width = conv_weight.shape[-1]
    (conv_weight,) = gather_seq([(conv_weight, 1)], width)
    qkv_weight, out_weight = gather_seq([(qkv_weight, 1), (out_weight, 1)], width)
    clean = features[0]
    moved = (clean.astype(jnp.float32) + noise[0]).astype(jnp.bfloat16)
    joint = forward(
        jnp.stack([clean, moved]), conv_weight, conv_bias, norm_gain, qkv_weight, out_weight
    )
    clean_run = [item[0:1] for item in joint]
    moved_run = [item[1:2] for item in joint]
    (
        pre_act,
        pooled_wide,
        whole_wide,
        row_scale,
        query_heads,
        keyval_heads,
        attended_heads,
        log_mass,
        mixed,
    ) = [item[0] for item in moved_run]
    clean_mixed = clean_run[8][0]
    rows, half_width = pooled_wide.shape
    positions = pre_act.shape[0]
    proj_width = qkv_weight.shape[2]
    head_size = HD
    head_count = proj_width // head_size
    devices = lax.axis_size("seq")
    query_groups = devices // head_count
    sub_rows = rows // query_groups
    difference = mixed - clean_mixed
    difference_half = difference.astype(jnp.bfloat16)
    difference_whole = lax.all_gather(difference_half, "mp", axis=1, tiled=True)
    out_grad = jnp.einsum(
        "rf,hf->rh",
        difference_whole,
        out_weight,
        preferred_element_type=jnp.float32,
    ).astype(jnp.bfloat16)
    grad_send = (
        out_grad.reshape(query_groups, sub_rows, head_count, head_size)
        .transpose(2, 0, 1, 3)
        .reshape(devices, sub_rows * head_size)
    )
    grad_in = lax.all_to_all(grad_send, "seq", split_axis=0, concat_axis=1, tiled=True)
    grad_heads = grad_in.reshape(devices * sub_rows, head_size)
    query_grad, keyval_grad = attend_back(
        query_heads,
        keyval_heads[:, :head_size],
        keyval_heads[:, head_size:],
        attended_heads,
        log_mass,
        grad_heads,
    )
    query_len = sub_rows * head_size
    both_back = lax.all_to_all(
        jnp.concatenate(
            [
                query_grad.reshape(devices, query_len).astype(jnp.bfloat16),
                keyval_grad.reshape(devices, rows * 2 * head_size).astype(jnp.bfloat16),
            ],
            axis=1,
        ),
        "seq",
        split_axis=0,
        concat_axis=0,
        tiled=True,
    ).astype(jnp.float32)
    query_back = both_back[:, :query_len]
    keyval_back = both_back[:, query_len:]
    query_rows = (
        query_back.reshape(head_count, query_groups, sub_rows, head_size)
        .transpose(1, 2, 0, 3)
        .reshape(rows, proj_width)
        .astype(jnp.bfloat16)
    )
    keyval_rows = jnp.sum(keyval_back.reshape(head_count, query_groups, rows, 2, head_size), axis=1)
    key_rows = (
        keyval_rows[:, :, 0].transpose(1, 0, 2).reshape(rows, proj_width).astype(jnp.bfloat16)
    )
    value_rows = (
        keyval_rows[:, :, 1].transpose(1, 0, 2).reshape(rows, proj_width).astype(jnp.bfloat16)
    )
    grads = jnp.stack([query_rows, key_rows, value_rows])
    normed_terms = jnp.einsum(
        "jrh,jfh->rf",
        grads,
        qkv_weight,
        preferred_element_type=jnp.float32,
    )
    offset_mp = lax.axis_index("mp") * half_width
    gain_own = lax.dynamic_slice_in_dim(norm_gain, offset_mp, half_width, 0)
    normed_grad = add_halves(normed_terms.astype(jnp.bfloat16), 1)
    weighted = lax.psum(jnp.sum(normed_grad * gain_own * pooled_wide, axis=1, keepdims=True), "mp")
    pooled_grad = (
        difference + row_scale * gain_own * normed_grad - pooled_wide * row_scale**3 * weighted / F
    )
    spread = jnp.broadcast_to((0.5 * pooled_grad)[:, None, :], (rows, 2, half_width)).reshape(
        positions, half_width
    )
    gelu_back = jax.vjp(jax.nn.gelu, pre_act)[1]
    pre_grad = gelu_back(spread)[0].astype(jnp.bfloat16)
    reach = KW // 2
    padded = with_halo(pre_grad, (("seq", 0),), reach)
    piece = conv_weight
    running = jnp.zeros((positions, piece.shape[1]), jnp.float32)
    for offset in range(piece.shape[0]):
        lower = 2 * reach - offset
        running = running + jnp.einsum(
            "tf,cf->tc",
            padded[lower : lower + positions],
            piece[offset],
            preferred_element_type=jnp.float32,
        )
    own_grad = running.astype(jnp.bfloat16)
    input_grad = (own_grad.astype(jnp.float32) + swap_mp(own_grad).astype(jnp.float32)).astype(
        jnp.bfloat16
    ).astype(jnp.float32)
    new_noise = noise[0] + step_size * input_grad * lax.rsqrt(
        jnp.mean(input_grad * input_grad, axis=1, keepdims=True) + epsilon
    )
    return (clean_mixed.astype(jnp.bfloat16)[None], new_noise[None])


def solution(mesh):
    return jax.shard_map(
        shards,
        mesh=mesh,
        in_specs=(
            P(("group", "batch"), "seq", None),
            P(("group", "batch"), "seq", None),
            P(None, "seq", "mp"),
            P("mp"),
            P(),
            P(None, "seq", "mp"),
            P("mp", "seq"),
        ),
        out_specs=(P(("group", "batch"), "seq", "mp"), P(("group", "batch"), "seq", None)),
        check_vma=False,
    )
```

```python
import jax
import jax.numpy as jnp
from jax import lax
from jax.sharding import PartitionSpec as P

F = 768
HD = 96
KW = 5


step_size = 0.5
epsilon = 1e-06


def with_halo(cells, sides, width):
    for axis, dim in sides:
        count = lax.axis_size(axis)
        ends = count - 1
        head = lax.slice_in_dim(cells, 0, width, axis=dim)
        tail = lax.slice_in_dim(cells, cells.shape[dim] - width, cells.shape[dim], axis=dim)
        cells = jnp.concatenate(
            [
                lax.ppermute(tail, axis, [(i, (i + 1) % count) for i in range(ends)]),
                cells,
                lax.ppermute(head, axis, [((i + 1) % count, i) for i in range(ends)]),
            ],
            axis=dim,
        )
    return cells


def gather_seq(parts, width):
    spread = ("group", "batch")
    count = lax.axis_size("group") * lax.axis_size("batch")
    ring = lax.axis_size("seq")
    flats = [cells.reshape(-1, width) for cells, _ in parts]
    flat = jnp.concatenate(flats, axis=0) if len(flats) > 1 else flats[0]
    rows = flat.shape[0]
    size = -(-rows // count)
    if size * count != rows:
        flat = jnp.pad(flat, ((0, size * count - rows), (0, 0)))
    piece = lax.dynamic_slice_in_dim(flat, lax.axis_index(spread) * size, size, 0)
    if ring <= 8:
        place = lax.axis_index("seq")
        along = jnp.zeros((ring,) + piece.shape, piece.dtype)
        along = lax.dynamic_update_slice_in_dim(along, piece[None], place, 0)
        for shift in range(1, ring):
            arrived = lax.ppermute(piece, "seq", [(i, (i + shift) % ring) for i in range(ring)])
            along = lax.dynamic_update_slice_in_dim(
                along, arrived[None], (place + ring - shift) % ring, 0
            )
    else:
        along = lax.all_gather(piece, "seq", axis=0, tiled=False)
    if ring <= 8 and count <= 4:
        place = lax.axis_index(spread)
        whole = jnp.zeros((count,) + along.shape, along.dtype)
        whole = lax.dynamic_update_slice_in_dim(whole, along[None], place, 0)
        for mask in range(1, count):
            arrived = lax.ppermute(along, spread, [(i, i ^ mask) for i in range(count)])
            whole = lax.dynamic_update_slice_in_dim(
                whole, arrived[None], lax.bitwise_xor(place, mask), 0
            )
    else:
        whole = lax.all_gather(along, spread, axis=0, tiled=False)
    whole = whole.transpose(1, 0, 2, 3).reshape(ring, count * size, width)
    results = []
    offset = 0
    for (cells, dim), part in zip(parts, flats):
        block = whole[:, offset : offset + part.shape[0]]
        offset += part.shape[0]
        block = jnp.moveaxis(block.reshape((ring,) + cells.shape), 0, dim)
        shape = list(cells.shape)
        shape[dim] = shape[dim] * ring
        results.append(block.reshape(shape))
    return results


def swap_mp(cells):
    return lax.ppermute(cells, "mp", [(0, 1), (1, 0)])


def add_halves(cells, dim):
    half = cells.shape[dim] // 2
    index = lax.axis_index("mp")
    own = lax.dynamic_slice_in_dim(cells, index * half, half, dim)
    other = lax.dynamic_slice_in_dim(cells, (1 - index) * half, half, dim)
    return (own.astype(jnp.float32) + swap_mp(other).astype(jnp.float32)).astype(
        jnp.bfloat16
    ).astype(jnp.float32)


def attend_rows(query, keys, values):
    key_total = keys.shape[0]
    block_len = min(512, key_total)
    head_size = keys.shape[1]
    score_scale = head_size ** (-0.5)
    key_blocks = keys.reshape(key_total // block_len, block_len, head_size)
    value_blocks = values.reshape(key_total // block_len, block_len, head_size)
    query_count = query.shape[0]

    def find_top(carry, key_block):
        row_top, row_mass = carry
        scores = jnp.dot(query, key_block.T, preferred_element_type=jnp.float32) * score_scale
        new_top = jnp.maximum(row_top, jnp.max(scores, axis=1))
        row_mass = row_mass * jnp.exp(row_top - new_top) + jnp.sum(
            jnp.exp(scores - new_top[:, None]), axis=1
        )
        return ((new_top, row_mass), None)

    start_top = jnp.full((query_count,), -1e30, jnp.float32)
    (row_top, row_mass), _ = lax.scan(
        find_top, (start_top, jnp.zeros((query_count,), jnp.float32)), key_blocks
    )
    log_mass = row_top + jnp.log(row_mass)

    def collect(running, blocks):
        key_block, value_block = blocks
        scores = jnp.dot(query, key_block.T, preferred_element_type=jnp.float32) * score_scale
        soft_weights = jnp.exp(scores - log_mass[:, None]).astype(jnp.bfloat16)
        return (
            running + jnp.dot(soft_weights, value_block, preferred_element_type=jnp.float32),
            None,
        )

    running, _ = lax.scan(
        collect, jnp.zeros((query_count, head_size), jnp.float32), (key_blocks, value_blocks)
    )
    return (running.astype(jnp.bfloat16), log_mass)


def attend_back(query, keys, values, attended, log_mass, out_grad):
    key_total = keys.shape[0]
    block_len = min(512, key_total)
    head_size = keys.shape[1]
    score_scale = head_size ** (-0.5)
    key_blocks = keys.reshape(key_total // block_len, block_len, head_size)
    value_blocks = values.reshape(key_total // block_len, block_len, head_size)
    row_dot = jnp.sum(out_grad.astype(jnp.float32) * attended.astype(jnp.float32), axis=1)

    def step_back(query_acc, blocks):
        key_block, value_block = blocks
        scores = jnp.dot(query, key_block.T, preferred_element_type=jnp.float32) * score_scale
        exp_weights = jnp.exp(scores - log_mass[:, None])
        value_part = jnp.einsum(
            "qk,qd->kd",
            exp_weights.astype(jnp.bfloat16),
            out_grad,
            preferred_element_type=jnp.float32,
        )
        prob_grad = jnp.dot(out_grad, value_block.T, preferred_element_type=jnp.float32)
        score_grad = (exp_weights * (prob_grad - row_dot[:, None])).astype(jnp.bfloat16)
        query_acc = (
            query_acc
            + jnp.dot(score_grad, key_block, preferred_element_type=jnp.float32) * score_scale
        )
        key_part = (
            jnp.einsum("qk,qd->kd", score_grad, query, preferred_element_type=jnp.float32)
            * score_scale
        )
        return (query_acc, jnp.concatenate([key_part, value_part], axis=1))

    query_grad, keyval_parts = lax.scan(
        step_back, jnp.zeros((query.shape[0], head_size), jnp.float32), (key_blocks, value_blocks)
    )
    return (query_grad, keyval_parts.reshape(key_total, 2 * head_size))


def forward(stack, conv_weight, conv_bias, norm_gain, qkv_weight, out_weight):
    pass_count, positions, channels = stack.shape
    reach = KW // 2
    half_width = conv_weight.shape[2]
    padded_input = with_halo(stack, (("seq", 1),), reach)
    running = jnp.zeros((pass_count, positions, half_width), jnp.float32)
    piece = conv_weight
    for offset in range(piece.shape[0]):
        running = running + jnp.einsum(
            "ptc,cf->ptf",
            padded_input[:, offset : offset + positions],
            piece[offset],
            preferred_element_type=jnp.float32,
        )
    pre_act = running + conv_bias
    paired = jax.nn.gelu(pre_act).reshape(pass_count, positions // 2, 2, half_width)
    pooled = (0.5 * (paired[:, :, 0] + paired[:, :, 1])).astype(jnp.bfloat16)
    pooled_wide = lax.optimization_barrier(pooled).astype(jnp.float32)
    whole = lax.all_gather(pooled, "mp", axis=2, tiled=True)
    whole_wide = whole.astype(jnp.float32)
    row_scale = lax.rsqrt(jnp.mean(whole_wide * whole_wide, axis=2, keepdims=True) + epsilon)
    normed = (whole_wide * row_scale * norm_gain).astype(jnp.bfloat16)
    rows = positions // 2
    proj_width = qkv_weight.shape[2]
    projected = jnp.einsum(
        "prf,jfh->jprh",
        normed,
        qkv_weight,
        preferred_element_type=jnp.float32,
    ).astype(jnp.bfloat16)
    head_size = HD
    head_count = proj_width // head_size
    devices = lax.axis_size("seq")
    query_groups = devices // head_count
    sub_rows = rows // query_groups
    query_send = (
        projected[0]
        .reshape(pass_count, query_groups, sub_rows, head_count, head_size)
        .transpose(3, 1, 0, 2, 4)
        .reshape(devices, pass_count, sub_rows * head_size)
    )
    keyval = jnp.concatenate(
        [
            projected[1].reshape(pass_count, rows, head_count, head_size),
            projected[2].reshape(pass_count, rows, head_count, head_size),
        ],
        axis=3,
    )
    keyval_flat = keyval.transpose(2, 0, 1, 3).reshape(
        head_count, 1, pass_count, rows * 2 * head_size
    )
    keyval_send = jnp.broadcast_to(
        keyval_flat, (head_count, query_groups, pass_count, rows * 2 * head_size)
    ).reshape(devices, pass_count, rows * 2 * head_size)
    query_len = query_send.shape[2]
    both_in = lax.all_to_all(
        jnp.concatenate([query_send, keyval_send], axis=2),
        "seq",
        split_axis=0,
        concat_axis=2,
        tiled=True,
    ).reshape(pass_count, devices, query_len + keyval_send.shape[2])
    query_heads = both_in[:, :, :query_len].reshape(pass_count, devices * sub_rows, head_size)
    keyval_heads = both_in[:, :, query_len:].reshape(pass_count, devices * rows, 2 * head_size)
    outputs = []
    masses = []
    for index in range(pass_count):
        out_now, mass_now = attend_rows(
            query_heads[index],
            keyval_heads[index, :, :head_size],
            keyval_heads[index, :, head_size:],
        )
        outputs.append(out_now)
        masses.append(mass_now)
    attended_heads = jnp.stack(outputs)
    log_mass = jnp.stack(masses)
    out_send = attended_heads.reshape(pass_count, devices, sub_rows * head_size).transpose(1, 0, 2)
    out_back = lax.all_to_all(out_send, "seq", split_axis=0, concat_axis=0, tiled=True)
    attended = (
        out_back.reshape(head_count, query_groups, pass_count, sub_rows, head_size)
        .transpose(2, 1, 3, 0, 4)
        .reshape(pass_count, rows, proj_width)
    )
    terms = jnp.einsum(
        "prh,hf->prf",
        attended,
        out_weight,
        preferred_element_type=jnp.float32,
    )
    mixed = (
        add_halves(terms.astype(jnp.bfloat16), 2) + pooled_wide
    )
    return (
        pre_act,
        pooled_wide,
        whole_wide,
        row_scale,
        query_heads,
        keyval_heads,
        attended_heads,
        log_mass,
        mixed,
    )


def shards(features, noise, conv_weight, conv_bias, norm_gain, qkv_weight, out_weight):
    width = conv_weight.shape[-1]
    (conv_weight,) = gather_seq([(conv_weight, 1)], width)
    (qkv_weight,) = gather_seq([(qkv_weight, 1)], width)
    (out_weight,) = gather_seq([(out_weight, 1)], width)
    clean = features[0]
    moved = (clean.astype(jnp.float32) + noise[0]).astype(jnp.bfloat16)
    joint = forward(
        jnp.stack([clean, moved]), conv_weight, conv_bias, norm_gain, qkv_weight, out_weight
    )
    clean_run = [item[0:1] for item in joint]
    moved_run = [item[1:2] for item in joint]
    (
        pre_act,
        pooled_wide,
        whole_wide,
        row_scale,
        query_heads,
        keyval_heads,
        attended_heads,
        log_mass,
        mixed,
    ) = [item[0] for item in moved_run]
    clean_mixed = clean_run[8][0]
    rows, half_width = pooled_wide.shape
    positions = pre_act.shape[0]
    proj_width = qkv_weight.shape[2]
    head_size = HD
    head_count = proj_width // head_size
    devices = lax.axis_size("seq")
    query_groups = devices // head_count
    sub_rows = rows // query_groups
    difference = mixed - clean_mixed
    difference_half = difference.astype(jnp.bfloat16)
    difference_whole = lax.all_gather(difference_half, "mp", axis=1, tiled=True)
    out_grad = jnp.einsum(
        "rf,hf->rh",
        difference_whole,
        out_weight,
        preferred_element_type=jnp.float32,
    ).astype(jnp.bfloat16)
    grad_send = (
        out_grad.reshape(query_groups, sub_rows, head_count, head_size)
        .transpose(2, 0, 1, 3)
        .reshape(devices, sub_rows * head_size)
    )
    grad_in = lax.all_to_all(grad_send, "seq", split_axis=0, concat_axis=1, tiled=True)
    grad_heads = grad_in.reshape(devices * sub_rows, head_size)
    query_grad, keyval_grad = attend_back(
        query_heads,
        keyval_heads[:, :head_size],
        keyval_heads[:, head_size:],
        attended_heads,
        log_mass,
        grad_heads,
    )
    query_len = sub_rows * head_size
    both_back = lax.all_to_all(
        jnp.concatenate(
            [
                query_grad.reshape(devices, query_len).astype(jnp.bfloat16),
                keyval_grad.reshape(devices, rows * 2 * head_size).astype(jnp.bfloat16),
            ],
            axis=1,
        ),
        "seq",
        split_axis=0,
        concat_axis=0,
        tiled=True,
    ).astype(jnp.float32)
    query_back = both_back[:, :query_len]
    keyval_back = both_back[:, query_len:]
    query_rows = (
        query_back.reshape(head_count, query_groups, sub_rows, head_size)
        .transpose(1, 2, 0, 3)
        .reshape(rows, proj_width)
        .astype(jnp.bfloat16)
    )
    keyval_rows = jnp.sum(keyval_back.reshape(head_count, query_groups, rows, 2, head_size), axis=1)
    key_rows = (
        keyval_rows[:, :, 0].transpose(1, 0, 2).reshape(rows, proj_width).astype(jnp.bfloat16)
    )
    value_rows = (
        keyval_rows[:, :, 1].transpose(1, 0, 2).reshape(rows, proj_width).astype(jnp.bfloat16)
    )
    grads = jnp.stack([query_rows, key_rows, value_rows])
    normed_terms = jnp.einsum(
        "jrh,jfh->rf",
        grads,
        qkv_weight,
        preferred_element_type=jnp.float32,
    )
    offset_mp = lax.axis_index("mp") * half_width
    gain_own = lax.dynamic_slice_in_dim(norm_gain, offset_mp, half_width, 0)
    normed_grad = add_halves(normed_terms.astype(jnp.bfloat16), 1)
    weighted = lax.psum(jnp.sum(normed_grad * gain_own * pooled_wide, axis=1, keepdims=True), "mp")
    pooled_grad = (
        difference + row_scale * gain_own * normed_grad - pooled_wide * row_scale**3 * weighted / F
    )
    spread = jnp.broadcast_to((0.5 * pooled_grad)[:, None, :], (rows, 2, half_width)).reshape(
        positions, half_width
    )
    gelu_back = jax.vjp(jax.nn.gelu, pre_act)[1]
    pre_grad = gelu_back(spread)[0].astype(jnp.bfloat16)
    reach = KW // 2
    padded = with_halo(pre_grad, (("seq", 0),), reach)
    piece = conv_weight
    running = jnp.zeros((positions, piece.shape[1]), jnp.float32)
    for offset in range(piece.shape[0]):
        lower = 2 * reach - offset
        running = running + jnp.einsum(
            "tf,cf->tc",
            padded[lower : lower + positions],
            piece[offset],
            preferred_element_type=jnp.float32,
        )
    own_grad = running.astype(jnp.bfloat16)
    input_grad = (own_grad.astype(jnp.float32) + swap_mp(own_grad).astype(jnp.float32)).astype(
        jnp.bfloat16
    ).astype(jnp.float32)
    new_noise = noise[0] + step_size * input_grad * lax.rsqrt(
        jnp.mean(input_grad * input_grad, axis=1, keepdims=True) + epsilon
    )
    return (clean_mixed.astype(jnp.bfloat16)[None], new_noise[None])


def solution(mesh):
    return jax.shard_map(
        shards,
        mesh=mesh,
        in_specs=(
            P(("group", "batch"), "seq", None),
            P(("group", "batch"), "seq", None),
            P(None, "seq", "mp"),
            P("mp"),
            P(),
            P(None, "seq", "mp"),
            P("mp", "seq"),
        ),
        out_specs=(P(("group", "batch"), "seq", "mp"), P(("group", "batch"), "seq", None)),
        check_vma=False,
    )
```

```python
import jax
import jax.numpy as jnp
from jax import lax
from jax.sharding import PartitionSpec as P

F = 768
HD = 96
KW = 5


step_size = 0.5
epsilon = 1e-06


def with_halo(cells, sides, width):
    for axis, dim in sides:
        count = lax.axis_size(axis)
        ends = count - 1
        head = lax.slice_in_dim(cells, 0, width, axis=dim)
        tail = lax.slice_in_dim(cells, cells.shape[dim] - width, cells.shape[dim], axis=dim)
        cells = jnp.concatenate(
            [
                lax.ppermute(tail, axis, [(i, (i + 1) % count) for i in range(ends)]),
                cells,
                lax.ppermute(head, axis, [((i + 1) % count, i) for i in range(ends)]),
            ],
            axis=dim,
        )
    return cells


def gather_seq(parts, width, after=(None, None)):
    spread = ("group", "batch")
    count = lax.axis_size("group") * lax.axis_size("batch")
    ring = lax.axis_size("seq")
    flats = [cells.reshape(-1, width) for cells, _ in parts]
    flat = jnp.concatenate(flats, axis=0) if len(flats) > 1 else flats[0]
    rows = flat.shape[0]
    size = -(-rows // count)
    if size * count != rows:
        flat = jnp.pad(flat, ((0, size * count - rows), (0, 0)))
    piece = lax.dynamic_slice_in_dim(flat, lax.axis_index(spread) * size, size, 0)
    if after[0] is not None:
        piece = lax.optimization_barrier((piece, after[0]))[0]
    if ring <= 8:
        place = lax.axis_index("seq")
        along = jnp.zeros((ring,) + piece.shape, piece.dtype)
        along = lax.dynamic_update_slice_in_dim(along, piece[None], place, 0)
        for shift in range(1, ring):
            arrived = lax.ppermute(piece, "seq", [(i, (i + shift) % ring) for i in range(ring)])
            along = lax.dynamic_update_slice_in_dim(
                along, arrived[None], (place + ring - shift) % ring, 0
            )
    else:
        along = lax.all_gather(piece, "seq", axis=0, tiled=False)
    if after[1] is not None:
        along = lax.optimization_barrier((along, after[1]))[0]
    if ring <= 8 and count <= 4:
        place = lax.axis_index(spread)
        whole = jnp.zeros((count,) + along.shape, along.dtype)
        whole = lax.dynamic_update_slice_in_dim(whole, along[None], place, 0)
        for mask in range(1, count):
            arrived = lax.ppermute(along, spread, [(i, i ^ mask) for i in range(count)])
            whole = lax.dynamic_update_slice_in_dim(
                whole, arrived[None], lax.bitwise_xor(place, mask), 0
            )
    else:
        whole = lax.all_gather(along, spread, axis=0, tiled=False)
    whole = whole.transpose(1, 0, 2, 3).reshape(ring, count * size, width)
    results = []
    stages = (along, whole)
    offset = 0
    for (cells, dim), part in zip(parts, flats):
        block = whole[:, offset : offset + part.shape[0]]
        offset += part.shape[0]
        block = jnp.moveaxis(block.reshape((ring,) + cells.shape), 0, dim)
        shape = list(cells.shape)
        shape[dim] = shape[dim] * ring
        results.append(block.reshape(shape))
    return results, stages


def swap_mp(cells):
    return lax.ppermute(cells, "mp", [(0, 1), (1, 0)])


def add_halves(cells, dim):
    half = cells.shape[dim] // 2
    index = lax.axis_index("mp")
    own = lax.dynamic_slice_in_dim(cells, index * half, half, dim)
    other = lax.dynamic_slice_in_dim(cells, (1 - index) * half, half, dim)
    return (own.astype(jnp.float32) + swap_mp(other).astype(jnp.float32)).astype(
        jnp.bfloat16
    ).astype(jnp.float32)


def attend_rows(query, keys, values):
    key_total = keys.shape[0]
    block_len = min(512, key_total)
    head_size = keys.shape[1]
    score_scale = head_size ** (-0.5)
    key_blocks = keys.reshape(key_total // block_len, block_len, head_size)
    value_blocks = values.reshape(key_total // block_len, block_len, head_size)
    query_count = query.shape[0]

    def find_top(carry, key_block):
        row_top, row_mass = carry
        scores = jnp.dot(query, key_block.T, preferred_element_type=jnp.float32) * score_scale
        new_top = jnp.maximum(row_top, jnp.max(scores, axis=1))
        row_mass = row_mass * jnp.exp(row_top - new_top) + jnp.sum(
            jnp.exp(scores - new_top[:, None]), axis=1
        )
        return ((new_top, row_mass), None)

    start_top = jnp.full((query_count,), -1e30, jnp.float32)
    (row_top, row_mass), _ = lax.scan(
        find_top, (start_top, jnp.zeros((query_count,), jnp.float32)), key_blocks
    )
    log_mass = row_top + jnp.log(row_mass)

    def collect(running, blocks):
        key_block, value_block = blocks
        scores = jnp.dot(query, key_block.T, preferred_element_type=jnp.float32) * score_scale
        soft_weights = jnp.exp(scores - log_mass[:, None]).astype(jnp.bfloat16)
        return (
            running + jnp.dot(soft_weights, value_block, preferred_element_type=jnp.float32),
            None,
        )

    running, _ = lax.scan(
        collect, jnp.zeros((query_count, head_size), jnp.float32), (key_blocks, value_blocks)
    )
    return (running.astype(jnp.bfloat16), log_mass)


def attend_back(query, keys, values, attended, log_mass, out_grad):
    key_total = keys.shape[0]
    block_len = min(512, key_total)
    head_size = keys.shape[1]
    score_scale = head_size ** (-0.5)
    key_blocks = keys.reshape(key_total // block_len, block_len, head_size)
    value_blocks = values.reshape(key_total // block_len, block_len, head_size)
    row_dot = jnp.sum(out_grad.astype(jnp.float32) * attended.astype(jnp.float32), axis=1)

    def step_back(query_acc, blocks):
        key_block, value_block = blocks
        scores = jnp.dot(query, key_block.T, preferred_element_type=jnp.float32) * score_scale
        exp_weights = jnp.exp(scores - log_mass[:, None])
        value_part = jnp.einsum(
            "qk,qd->kd",
            exp_weights.astype(jnp.bfloat16),
            out_grad,
            preferred_element_type=jnp.float32,
        )
        prob_grad = jnp.dot(out_grad, value_block.T, preferred_element_type=jnp.float32)
        score_grad = (exp_weights * (prob_grad - row_dot[:, None])).astype(jnp.bfloat16)
        query_acc = (
            query_acc
            + jnp.dot(score_grad, key_block, preferred_element_type=jnp.float32) * score_scale
        )
        key_part = (
            jnp.einsum("qk,qd->kd", score_grad, query, preferred_element_type=jnp.float32)
            * score_scale
        )
        return (query_acc, jnp.concatenate([key_part, value_part], axis=1))

    query_grad, keyval_parts = lax.scan(
        step_back, jnp.zeros((query.shape[0], head_size), jnp.float32), (key_blocks, value_blocks)
    )
    return (query_grad, keyval_parts.reshape(key_total, 2 * head_size))


def forward(stack, conv_weight, conv_bias, norm_gain, qkv_weight, out_weight):
    pass_count, positions, channels = stack.shape
    reach = KW // 2
    half_width = conv_weight.shape[2]
    padded_input = with_halo(stack, (("seq", 1),), reach)
    running = jnp.zeros((pass_count, positions, half_width), jnp.float32)
    piece = conv_weight
    for offset in range(piece.shape[0]):
        running = running + jnp.einsum(
            "ptc,cf->ptf",
            padded_input[:, offset : offset + positions],
            piece[offset],
            preferred_element_type=jnp.float32,
        )
    pre_act = running + conv_bias
    paired = jax.nn.gelu(pre_act).reshape(pass_count, positions // 2, 2, half_width)
    pooled = (0.5 * (paired[:, :, 0] + paired[:, :, 1])).astype(jnp.bfloat16)
    pooled_wide = lax.optimization_barrier(pooled).astype(jnp.float32)
    whole = lax.all_gather(pooled, "mp", axis=2, tiled=True)
    whole_wide = whole.astype(jnp.float32)
    row_scale = lax.rsqrt(jnp.mean(whole_wide * whole_wide, axis=2, keepdims=True) + epsilon)
    normed = (whole_wide * row_scale * norm_gain).astype(jnp.bfloat16)
    rows = positions // 2
    proj_width = qkv_weight.shape[2]
    projected = jnp.einsum(
        "prf,jfh->jprh",
        normed,
        qkv_weight,
        preferred_element_type=jnp.float32,
    ).astype(jnp.bfloat16)
    head_size = HD
    head_count = proj_width // head_size
    devices = lax.axis_size("seq")
    query_groups = devices // head_count
    sub_rows = rows // query_groups
    query_send = (
        projected[0]
        .reshape(pass_count, query_groups, sub_rows, head_count, head_size)
        .transpose(3, 1, 0, 2, 4)
        .reshape(devices, pass_count, sub_rows * head_size)
    )
    keyval = jnp.concatenate(
        [
            projected[1].reshape(pass_count, rows, head_count, head_size),
            projected[2].reshape(pass_count, rows, head_count, head_size),
        ],
        axis=3,
    )
    keyval_flat = keyval.transpose(2, 0, 1, 3).reshape(
        head_count, 1, pass_count, rows * 2 * head_size
    )
    keyval_send = jnp.broadcast_to(
        keyval_flat, (head_count, query_groups, pass_count, rows * 2 * head_size)
    ).reshape(devices, pass_count, rows * 2 * head_size)
    query_len = query_send.shape[2]
    both_in = lax.all_to_all(
        jnp.concatenate([query_send, keyval_send], axis=2),
        "seq",
        split_axis=0,
        concat_axis=2,
        tiled=True,
    ).reshape(pass_count, devices, query_len + keyval_send.shape[2])
    query_heads = both_in[:, :, :query_len].reshape(pass_count, devices * sub_rows, head_size)
    keyval_heads = both_in[:, :, query_len:].reshape(pass_count, devices * rows, 2 * head_size)
    outputs = []
    masses = []
    for index in range(pass_count):
        out_now, mass_now = attend_rows(
            query_heads[index],
            keyval_heads[index, :, :head_size],
            keyval_heads[index, :, head_size:],
        )
        outputs.append(out_now)
        masses.append(mass_now)
    attended_heads = jnp.stack(outputs)
    log_mass = jnp.stack(masses)
    out_send = attended_heads.reshape(pass_count, devices, sub_rows * head_size).transpose(1, 0, 2)
    out_back = lax.all_to_all(out_send, "seq", split_axis=0, concat_axis=0, tiled=True)
    attended = (
        out_back.reshape(head_count, query_groups, pass_count, sub_rows, head_size)
        .transpose(2, 1, 3, 0, 4)
        .reshape(pass_count, rows, proj_width)
    )
    terms = jnp.einsum(
        "prh,hf->prf",
        attended,
        out_weight,
        preferred_element_type=jnp.float32,
    )
    mixed = (
        add_halves(terms.astype(jnp.bfloat16), 2) + pooled_wide
    )
    return (
        pre_act,
        pooled_wide,
        whole_wide,
        row_scale,
        query_heads,
        keyval_heads,
        attended_heads,
        log_mass,
        mixed,
    )


def shards(features, noise, conv_weight, conv_bias, norm_gain, qkv_weight, out_weight):
    width = conv_weight.shape[-1]
    (conv_weight,), conv_stages = gather_seq([(conv_weight, 1)], width)
    (qkv_weight,), qkv_stages = gather_seq([(qkv_weight, 1)], width, conv_stages)
    (out_weight,), _ = gather_seq([(out_weight, 1)], width, (qkv_stages[1], qkv_stages[1]))
    clean = features[0]
    moved = (clean.astype(jnp.float32) + noise[0]).astype(jnp.bfloat16)
    joint = forward(
        jnp.stack([clean, moved]), conv_weight, conv_bias, norm_gain, qkv_weight, out_weight
    )
    clean_run = [item[0:1] for item in joint]
    moved_run = [item[1:2] for item in joint]
    (
        pre_act,
        pooled_wide,
        whole_wide,
        row_scale,
        query_heads,
        keyval_heads,
        attended_heads,
        log_mass,
        mixed,
    ) = [item[0] for item in moved_run]
    clean_mixed = clean_run[8][0]
    rows, half_width = pooled_wide.shape
    positions = pre_act.shape[0]
    proj_width = qkv_weight.shape[2]
    head_size = HD
    head_count = proj_width // head_size
    devices = lax.axis_size("seq")
    query_groups = devices // head_count
    sub_rows = rows // query_groups
    difference = mixed - clean_mixed
    difference_half = difference.astype(jnp.bfloat16)
    difference_whole = lax.all_gather(difference_half, "mp", axis=1, tiled=True)
    out_grad = jnp.einsum(
        "rf,hf->rh",
        difference_whole,
        out_weight,
        preferred_element_type=jnp.float32,
    ).astype(jnp.bfloat16)
    grad_send = (
        out_grad.reshape(query_groups, sub_rows, head_count, head_size)
        .transpose(2, 0, 1, 3)
        .reshape(devices, sub_rows * head_size)
    )
    grad_in = lax.all_to_all(grad_send, "seq", split_axis=0, concat_axis=1, tiled=True)
    grad_heads = grad_in.reshape(devices * sub_rows, head_size)
    query_grad, keyval_grad = attend_back(
        query_heads,
        keyval_heads[:, :head_size],
        keyval_heads[:, head_size:],
        attended_heads,
        log_mass,
        grad_heads,
    )
    query_len = sub_rows * head_size
    both_back = lax.all_to_all(
        jnp.concatenate(
            [
                query_grad.reshape(devices, query_len).astype(jnp.bfloat16),
                keyval_grad.reshape(devices, rows * 2 * head_size).astype(jnp.bfloat16),
            ],
            axis=1,
        ),
        "seq",
        split_axis=0,
        concat_axis=0,
        tiled=True,
    ).astype(jnp.float32)
    query_back = both_back[:, :query_len]
    keyval_back = both_back[:, query_len:]
    query_rows = (
        query_back.reshape(head_count, query_groups, sub_rows, head_size)
        .transpose(1, 2, 0, 3)
        .reshape(rows, proj_width)
        .astype(jnp.bfloat16)
    )
    keyval_rows = jnp.sum(keyval_back.reshape(head_count, query_groups, rows, 2, head_size), axis=1)
    key_rows = (
        keyval_rows[:, :, 0].transpose(1, 0, 2).reshape(rows, proj_width).astype(jnp.bfloat16)
    )
    value_rows = (
        keyval_rows[:, :, 1].transpose(1, 0, 2).reshape(rows, proj_width).astype(jnp.bfloat16)
    )
    grads = jnp.stack([query_rows, key_rows, value_rows])
    normed_terms = jnp.einsum(
        "jrh,jfh->rf",
        grads,
        qkv_weight,
        preferred_element_type=jnp.float32,
    )
    offset_mp = lax.axis_index("mp") * half_width
    gain_own = lax.dynamic_slice_in_dim(norm_gain, offset_mp, half_width, 0)
    normed_grad = add_halves(normed_terms.astype(jnp.bfloat16), 1)
    weighted = lax.psum(jnp.sum(normed_grad * gain_own * pooled_wide, axis=1, keepdims=True), "mp")
    pooled_grad = (
        difference + row_scale * gain_own * normed_grad - pooled_wide * row_scale**3 * weighted / F
    )
    spread = jnp.broadcast_to((0.5 * pooled_grad)[:, None, :], (rows, 2, half_width)).reshape(
        positions, half_width
    )
    gelu_back = jax.vjp(jax.nn.gelu, pre_act)[1]
    pre_grad = gelu_back(spread)[0].astype(jnp.bfloat16)
    reach = KW // 2
    padded = with_halo(pre_grad, (("seq", 0),), reach)
    piece = conv_weight
    running = jnp.zeros((positions, piece.shape[1]), jnp.float32)
    for offset in range(piece.shape[0]):
        lower = 2 * reach - offset
        running = running + jnp.einsum(
            "tf,cf->tc",
            padded[lower : lower + positions],
            piece[offset],
            preferred_element_type=jnp.float32,
        )
    own_grad = running.astype(jnp.bfloat16)
    input_grad = (own_grad.astype(jnp.float32) + swap_mp(own_grad).astype(jnp.float32)).astype(
        jnp.bfloat16
    ).astype(jnp.float32)
    new_noise = noise[0] + step_size * input_grad * lax.rsqrt(
        jnp.mean(input_grad * input_grad, axis=1, keepdims=True) + epsilon
    )
    return (clean_mixed.astype(jnp.bfloat16)[None], new_noise[None])


def solution(mesh):
    return jax.shard_map(
        shards,
        mesh=mesh,
        in_specs=(
            P(("group", "batch"), "seq", None),
            P(("group", "batch"), "seq", None),
            P(None, "seq", "mp"),
            P("mp"),
            P(),
            P(None, "seq", "mp"),
            P("mp", "seq"),
        ),
        out_specs=(P(("group", "batch"), "seq", "mp"), P(("group", "batch"), "seq", None)),
        check_vma=False,
    )
```

```python
import jax
import jax.numpy as jnp
from jax import lax
from jax.sharding import PartitionSpec as P

F = 768
HD = 96
KW = 5


step_size = 0.5
epsilon = 1e-06


def with_halo(cells, sides, width):
    for axis, dim in sides:
        count = lax.axis_size(axis)
        ends = count - 1
        head = lax.slice_in_dim(cells, 0, width, axis=dim)
        tail = lax.slice_in_dim(cells, cells.shape[dim] - width, cells.shape[dim], axis=dim)
        cells = jnp.concatenate(
            [
                lax.ppermute(tail, axis, [(i, (i + 1) % count) for i in range(ends)]),
                cells,
                lax.ppermute(head, axis, [((i + 1) % count, i) for i in range(ends)]),
            ],
            axis=dim,
        )
    return cells


def gather_blocks(cells, dim, after=(None, None)):
    spread = ("group", "batch")
    count = lax.axis_size("group") * lax.axis_size("batch")
    ring = lax.axis_size("seq")
    last = dim == cells.ndim - 1
    split = 0 if last else dim
    size = cells.shape[split] // count
    piece = lax.dynamic_slice_in_dim(cells, lax.axis_index(spread) * size, size, split)
    if after[0] is not None:
        piece = lax.optimization_barrier((piece, after[0]))[0]
    slot = cells.ndim - 1 if last else dim
    piece = jnp.expand_dims(piece, slot)
    along = jnp.zeros(piece.shape[:slot] + (ring,) + piece.shape[slot + 1 :], cells.dtype)

    def place(block, target, axis, index):
        start = [0] * target.ndim
        start[axis] = index
        return lax.dynamic_update_slice(target, block, start)

    seq_at = lax.axis_index("seq")
    along = place(piece, along, slot, seq_at)
    for shift in range(1, ring):
        arrived = lax.ppermute(piece, "seq", [(i, (i + shift) % ring) for i in range(ring)])
        along = place(arrived, along, slot, (seq_at + ring - shift) % ring)
    if after[1] is not None:
        along = lax.optimization_barrier((along, after[1]))[0]
    lane = 0 if last else dim + 1
    along = jnp.expand_dims(along, lane)
    whole = jnp.zeros(along.shape[:lane] + (count,) + along.shape[lane + 1 :], cells.dtype)
    gb_at = lax.axis_index(spread)
    whole = place(along, whole, lane, gb_at)
    for mask in range(1, count):
        arrived = lax.ppermute(along, spread, [(i, i ^ mask) for i in range(count)])
        whole = place(arrived, whole, lane, lax.bitwise_xor(gb_at, mask))
    shape = list(cells.shape)
    shape[dim] = shape[dim] * ring
    return whole.reshape(shape), (along, whole)


def gather_seq(parts, width, after=(None, None)):
    spread = ("group", "batch")
    count = lax.axis_size("group") * lax.axis_size("batch")
    ring = lax.axis_size("seq")
    flats = [cells.reshape(-1, width) for cells, _ in parts]
    flat = jnp.concatenate(flats, axis=0) if len(flats) > 1 else flats[0]
    rows = flat.shape[0]
    size = -(-rows // count)
    if size * count != rows:
        flat = jnp.pad(flat, ((0, size * count - rows), (0, 0)))
    piece = lax.dynamic_slice_in_dim(flat, lax.axis_index(spread) * size, size, 0)
    if after[0] is not None:
        piece = lax.optimization_barrier((piece, after[0]))[0]
    if ring <= 8:
        place = lax.axis_index("seq")
        along = jnp.zeros((ring,) + piece.shape, piece.dtype)
        along = lax.dynamic_update_slice_in_dim(along, piece[None], place, 0)
        for shift in range(1, ring):
            arrived = lax.ppermute(piece, "seq", [(i, (i + shift) % ring) for i in range(ring)])
            along = lax.dynamic_update_slice_in_dim(
                along, arrived[None], (place + ring - shift) % ring, 0
            )
    else:
        along = lax.all_gather(piece, "seq", axis=0, tiled=False)
    if after[1] is not None:
        along = lax.optimization_barrier((along, after[1]))[0]
    if ring <= 8 and count <= 4:
        place = lax.axis_index(spread)
        whole = jnp.zeros((count,) + along.shape, along.dtype)
        whole = lax.dynamic_update_slice_in_dim(whole, along[None], place, 0)
        for mask in range(1, count):
            arrived = lax.ppermute(along, spread, [(i, i ^ mask) for i in range(count)])
            whole = lax.dynamic_update_slice_in_dim(
                whole, arrived[None], lax.bitwise_xor(place, mask), 0
            )
    else:
        whole = lax.all_gather(along, spread, axis=0, tiled=False)
    whole = whole.transpose(1, 0, 2, 3).reshape(ring, count * size, width)
    results = []
    stages = (along, whole)
    offset = 0
    for (cells, dim), part in zip(parts, flats):
        block = whole[:, offset : offset + part.shape[0]]
        offset += part.shape[0]
        block = jnp.moveaxis(block.reshape((ring,) + cells.shape), 0, dim)
        shape = list(cells.shape)
        shape[dim] = shape[dim] * ring
        results.append(block.reshape(shape))
    return results, stages


def swap_mp(cells):
    return lax.ppermute(cells, "mp", [(0, 1), (1, 0)])


def add_halves(cells, dim):
    half = cells.shape[dim] // 2
    index = lax.axis_index("mp")
    own = lax.dynamic_slice_in_dim(cells, index * half, half, dim)
    other = lax.dynamic_slice_in_dim(cells, (1 - index) * half, half, dim)
    return (own.astype(jnp.float32) + swap_mp(other).astype(jnp.float32)).astype(
        jnp.bfloat16
    ).astype(jnp.float32)


def attend_rows(query, keys, values):
    key_total = keys.shape[0]
    block_len = min(512, key_total)
    head_size = keys.shape[1]
    score_scale = head_size ** (-0.5)
    key_blocks = keys.reshape(key_total // block_len, block_len, head_size)
    value_blocks = values.reshape(key_total // block_len, block_len, head_size)
    query_count = query.shape[0]

    def find_top(carry, key_block):
        row_top, row_mass = carry
        scores = jnp.dot(query, key_block.T, preferred_element_type=jnp.float32) * score_scale
        new_top = jnp.maximum(row_top, jnp.max(scores, axis=1))
        row_mass = row_mass * jnp.exp(row_top - new_top) + jnp.sum(
            jnp.exp(scores - new_top[:, None]), axis=1
        )
        return ((new_top, row_mass), None)

    start_top = jnp.full((query_count,), -1e30, jnp.float32)
    (row_top, row_mass), _ = lax.scan(
        find_top, (start_top, jnp.zeros((query_count,), jnp.float32)), key_blocks
    )
    log_mass = row_top + jnp.log(row_mass)

    def collect(running, blocks):
        key_block, value_block = blocks
        scores = jnp.dot(query, key_block.T, preferred_element_type=jnp.float32) * score_scale
        soft_weights = jnp.exp(scores - log_mass[:, None]).astype(jnp.bfloat16)
        return (
            running + jnp.dot(soft_weights, value_block, preferred_element_type=jnp.float32),
            None,
        )

    running, _ = lax.scan(
        collect, jnp.zeros((query_count, head_size), jnp.float32), (key_blocks, value_blocks)
    )
    return (running.astype(jnp.bfloat16), log_mass)


def attend_back(query, keys, values, attended, log_mass, out_grad):
    key_total = keys.shape[0]
    block_len = min(512, key_total)
    head_size = keys.shape[1]
    score_scale = head_size ** (-0.5)
    key_blocks = keys.reshape(key_total // block_len, block_len, head_size)
    value_blocks = values.reshape(key_total // block_len, block_len, head_size)
    row_dot = jnp.sum(out_grad.astype(jnp.float32) * attended.astype(jnp.float32), axis=1)

    def step_back(query_acc, blocks):
        key_block, value_block = blocks
        scores = jnp.dot(query, key_block.T, preferred_element_type=jnp.float32) * score_scale
        exp_weights = jnp.exp(scores - log_mass[:, None])
        value_part = jnp.einsum(
            "qk,qd->kd",
            exp_weights.astype(jnp.bfloat16),
            out_grad,
            preferred_element_type=jnp.float32,
        )
        prob_grad = jnp.dot(out_grad, value_block.T, preferred_element_type=jnp.float32)
        score_grad = (exp_weights * (prob_grad - row_dot[:, None])).astype(jnp.bfloat16)
        query_acc = (
            query_acc
            + jnp.dot(score_grad, key_block, preferred_element_type=jnp.float32) * score_scale
        )
        key_part = (
            jnp.einsum("qk,qd->kd", score_grad, query, preferred_element_type=jnp.float32)
            * score_scale
        )
        return (query_acc, jnp.concatenate([key_part, value_part], axis=1))

    query_grad, keyval_parts = lax.scan(
        step_back, jnp.zeros((query.shape[0], head_size), jnp.float32), (key_blocks, value_blocks)
    )
    return (query_grad, keyval_parts.reshape(key_total, 2 * head_size))


def forward(stack, conv_weight, conv_bias, norm_gain, qkv_weight, out_weight):
    pass_count, positions, channels = stack.shape
    reach = KW // 2
    half_width = conv_weight.shape[2]
    padded_input = with_halo(stack, (("seq", 1),), reach)
    running = jnp.zeros((pass_count, positions, half_width), jnp.float32)
    piece = conv_weight
    for offset in range(piece.shape[0]):
        running = running + jnp.einsum(
            "ptc,cf->ptf",
            padded_input[:, offset : offset + positions],
            piece[offset],
            preferred_element_type=jnp.float32,
        )
    pre_act = running + conv_bias
    paired = jax.nn.gelu(pre_act).reshape(pass_count, positions // 2, 2, half_width)
    pooled = (0.5 * (paired[:, :, 0] + paired[:, :, 1])).astype(jnp.bfloat16)
    pooled_wide = lax.optimization_barrier(pooled).astype(jnp.float32)
    whole = lax.all_gather(pooled, "mp", axis=2, tiled=True)
    whole_wide = whole.astype(jnp.float32)
    row_scale = lax.rsqrt(jnp.mean(whole_wide * whole_wide, axis=2, keepdims=True) + epsilon)
    normed = (whole_wide * row_scale * norm_gain).astype(jnp.bfloat16)
    rows = positions // 2
    proj_width = qkv_weight.shape[2]
    projected = jnp.einsum(
        "prf,jfh->jprh",
        normed,
        qkv_weight,
        preferred_element_type=jnp.float32,
    ).astype(jnp.bfloat16)
    head_size = HD
    head_count = proj_width // head_size
    devices = lax.axis_size("seq")
    query_groups = devices // head_count
    sub_rows = rows // query_groups
    query_send = (
        projected[0]
        .reshape(pass_count, query_groups, sub_rows, head_count, head_size)
        .transpose(3, 1, 0, 2, 4)
        .reshape(devices, pass_count, sub_rows * head_size)
    )
    keyval = jnp.concatenate(
        [
            projected[1].reshape(pass_count, rows, head_count, head_size),
            projected[2].reshape(pass_count, rows, head_count, head_size),
        ],
        axis=3,
    )
    keyval_flat = keyval.transpose(2, 0, 1, 3).reshape(
        head_count, 1, pass_count, rows * 2 * head_size
    )
    keyval_send = jnp.broadcast_to(
        keyval_flat, (head_count, query_groups, pass_count, rows * 2 * head_size)
    ).reshape(devices, pass_count, rows * 2 * head_size)
    query_len = query_send.shape[2]
    both_in = lax.all_to_all(
        jnp.concatenate([query_send, keyval_send], axis=2),
        "seq",
        split_axis=0,
        concat_axis=2,
        tiled=True,
    ).reshape(pass_count, devices, query_len + keyval_send.shape[2])
    query_heads = both_in[:, :, :query_len].reshape(pass_count, devices * sub_rows, head_size)
    keyval_heads = both_in[:, :, query_len:].reshape(pass_count, devices * rows, 2 * head_size)
    outputs = []
    masses = []
    for index in range(pass_count):
        out_now, mass_now = attend_rows(
            query_heads[index],
            keyval_heads[index, :, :head_size],
            keyval_heads[index, :, head_size:],
        )
        outputs.append(out_now)
        masses.append(mass_now)
    attended_heads = jnp.stack(outputs)
    log_mass = jnp.stack(masses)
    out_send = attended_heads.reshape(pass_count, devices, sub_rows * head_size).transpose(1, 0, 2)
    out_back = lax.all_to_all(out_send, "seq", split_axis=0, concat_axis=0, tiled=True)
    attended = (
        out_back.reshape(head_count, query_groups, pass_count, sub_rows, head_size)
        .transpose(2, 1, 3, 0, 4)
        .reshape(pass_count, rows, proj_width)
    )
    terms = jnp.einsum(
        "prh,hf->prf",
        attended,
        out_weight,
        preferred_element_type=jnp.float32,
    )
    mixed = (
        add_halves(terms.astype(jnp.bfloat16), 2) + pooled_wide
    )
    return (
        pre_act,
        pooled_wide,
        whole_wide,
        row_scale,
        query_heads,
        keyval_heads,
        attended_heads,
        log_mass,
        mixed,
    )


def shards(features, noise, conv_weight, conv_bias, norm_gain, qkv_weight, out_weight):
    width = conv_weight.shape[-1]
    direct = (
        lax.axis_size("seq") <= 8
        and lax.axis_size("group") * lax.axis_size("batch") <= 4
        and conv_weight.shape[1] % (4 * lax.axis_size("group") * lax.axis_size("batch")) == 0
        and qkv_weight.shape[1] % (4 * lax.axis_size("group") * lax.axis_size("batch")) == 0
        and out_weight.shape[0] % (4 * lax.axis_size("group") * lax.axis_size("batch")) == 0
    )
    if direct:
        conv_weight, _ = gather_blocks(conv_weight, 1)
        qkv_weight, _ = gather_blocks(qkv_weight, 1)
        out_weight, _ = gather_blocks(out_weight, 1)
    else:
        (conv_weight,), _ = gather_seq([(conv_weight, 1)], width)
        (qkv_weight,), _ = gather_seq([(qkv_weight, 1)], width)
        (out_weight,), _ = gather_seq([(out_weight, 1)], width)
    clean = features[0]
    moved = (clean.astype(jnp.float32) + noise[0]).astype(jnp.bfloat16)
    joint = forward(
        jnp.stack([clean, moved]), conv_weight, conv_bias, norm_gain, qkv_weight, out_weight
    )
    clean_run = [item[0:1] for item in joint]
    moved_run = [item[1:2] for item in joint]
    (
        pre_act,
        pooled_wide,
        whole_wide,
        row_scale,
        query_heads,
        keyval_heads,
        attended_heads,
        log_mass,
        mixed,
    ) = [item[0] for item in moved_run]
    clean_mixed = clean_run[8][0]
    rows, half_width = pooled_wide.shape
    positions = pre_act.shape[0]
    proj_width = qkv_weight.shape[2]
    head_size = HD
    head_count = proj_width // head_size
    devices = lax.axis_size("seq")
    query_groups = devices // head_count
    sub_rows = rows // query_groups
    difference = mixed - clean_mixed
    difference_half = difference.astype(jnp.bfloat16)
    difference_whole = lax.all_gather(difference_half, "mp", axis=1, tiled=True)
    out_grad = jnp.einsum(
        "rf,hf->rh",
        difference_whole,
        out_weight,
        preferred_element_type=jnp.float32,
    ).astype(jnp.bfloat16)
    grad_send = (
        out_grad.reshape(query_groups, sub_rows, head_count, head_size)
        .transpose(2, 0, 1, 3)
        .reshape(devices, sub_rows * head_size)
    )
    grad_in = lax.all_to_all(grad_send, "seq", split_axis=0, concat_axis=1, tiled=True)
    grad_heads = grad_in.reshape(devices * sub_rows, head_size)
    query_grad, keyval_grad = attend_back(
        query_heads,
        keyval_heads[:, :head_size],
        keyval_heads[:, head_size:],
        attended_heads,
        log_mass,
        grad_heads,
    )
    query_len = sub_rows * head_size
    both_back = lax.all_to_all(
        jnp.concatenate(
            [
                query_grad.reshape(devices, query_len).astype(jnp.bfloat16),
                keyval_grad.reshape(devices, rows * 2 * head_size).astype(jnp.bfloat16),
            ],
            axis=1,
        ),
        "seq",
        split_axis=0,
        concat_axis=0,
        tiled=True,
    ).astype(jnp.float32)
    query_back = both_back[:, :query_len]
    keyval_back = both_back[:, query_len:]
    query_rows = (
        query_back.reshape(head_count, query_groups, sub_rows, head_size)
        .transpose(1, 2, 0, 3)
        .reshape(rows, proj_width)
        .astype(jnp.bfloat16)
    )
    keyval_rows = jnp.sum(keyval_back.reshape(head_count, query_groups, rows, 2, head_size), axis=1)
    key_rows = (
        keyval_rows[:, :, 0].transpose(1, 0, 2).reshape(rows, proj_width).astype(jnp.bfloat16)
    )
    value_rows = (
        keyval_rows[:, :, 1].transpose(1, 0, 2).reshape(rows, proj_width).astype(jnp.bfloat16)
    )
    grads = jnp.stack([query_rows, key_rows, value_rows])
    normed_terms = jnp.einsum(
        "jrh,jfh->rf",
        grads,
        qkv_weight,
        preferred_element_type=jnp.float32,
    )
    offset_mp = lax.axis_index("mp") * half_width
    gain_own = lax.dynamic_slice_in_dim(norm_gain, offset_mp, half_width, 0)
    normed_grad = add_halves(normed_terms.astype(jnp.bfloat16), 1)
    weighted = lax.psum(jnp.sum(normed_grad * gain_own * pooled_wide, axis=1, keepdims=True), "mp")
    pooled_grad = (
        difference + row_scale * gain_own * normed_grad - pooled_wide * row_scale**3 * weighted / F
    )
    spread = jnp.broadcast_to((0.5 * pooled_grad)[:, None, :], (rows, 2, half_width)).reshape(
        positions, half_width
    )
    gelu_back = jax.vjp(jax.nn.gelu, pre_act)[1]
    pre_grad = gelu_back(spread)[0].astype(jnp.bfloat16)
    reach = KW // 2
    padded = with_halo(pre_grad, (("seq", 0),), reach)
    piece = conv_weight
    running = jnp.zeros((positions, piece.shape[1]), jnp.float32)
    for offset in range(piece.shape[0]):
        lower = 2 * reach - offset
        running = running + jnp.einsum(
            "tf,cf->tc",
            padded[lower : lower + positions],
            piece[offset],
            preferred_element_type=jnp.float32,
        )
    own_grad = running.astype(jnp.bfloat16)
    input_grad = (own_grad.astype(jnp.float32) + swap_mp(own_grad).astype(jnp.float32)).astype(
        jnp.bfloat16
    ).astype(jnp.float32)
    new_noise = noise[0] + step_size * input_grad * lax.rsqrt(
        jnp.mean(input_grad * input_grad, axis=1, keepdims=True) + epsilon
    )
    return (clean_mixed.astype(jnp.bfloat16)[None], new_noise[None])


def solution(mesh):
    return jax.shard_map(
        shards,
        mesh=mesh,
        in_specs=(
            P(("group", "batch"), "seq", None),
            P(("group", "batch"), "seq", None),
            P(None, "seq", "mp"),
            P("mp"),
            P(),
            P(None, "seq", "mp"),
            P("mp", "seq"),
        ),
        out_specs=(P(("group", "batch"), "seq", "mp"), P(("group", "batch"), "seq", None)),
        check_vma=False,
    )
```

```python
import jax
import jax.numpy as jnp
from jax import lax
from jax.sharding import PartitionSpec as P

F = 768
HD = 96
KW = 5


step_size = 0.5
epsilon = 1e-06


def with_halo(cells, sides, width):
    for axis, dim in sides:
        count = lax.axis_size(axis)
        ends = count - 1
        head = lax.slice_in_dim(cells, 0, width, axis=dim)
        tail = lax.slice_in_dim(cells, cells.shape[dim] - width, cells.shape[dim], axis=dim)
        cells = jnp.concatenate(
            [
                lax.ppermute(tail, axis, [(i, (i + 1) % count) for i in range(ends)]),
                cells,
                lax.ppermute(head, axis, [((i + 1) % count, i) for i in range(ends)]),
            ],
            axis=dim,
        )
    return cells


def gather_blocks(cells, dim, after=(None, None)):
    spread = ("group", "batch")
    count = lax.axis_size("group") * lax.axis_size("batch")
    ring = lax.axis_size("seq")
    last = dim == cells.ndim - 1
    split = 0 if last else dim
    size = cells.shape[split] // count
    piece = lax.dynamic_slice_in_dim(cells, lax.axis_index(spread) * size, size, split)
    if after[0] is not None:
        piece = lax.optimization_barrier((piece, after[0]))[0]
    slot = 0 if last else dim
    piece = jnp.expand_dims(piece, slot)
    along = jnp.zeros(piece.shape[:slot] + (ring,) + piece.shape[slot + 1 :], cells.dtype)

    def place(block, target, axis, index):
        start = [0] * target.ndim
        start[axis] = index
        return lax.dynamic_update_slice(target, block, start)

    seq_at = lax.axis_index("seq")
    along = place(piece, along, slot, seq_at)
    for shift in range(1, ring):
        arrived = lax.ppermute(piece, "seq", [(i, (i + shift) % ring) for i in range(ring)])
        along = place(arrived, along, slot, (seq_at + ring - shift) % ring)
    if after[1] is not None:
        along = lax.optimization_barrier((along, after[1]))[0]
    lane = 0 if last else dim + 1
    along = jnp.expand_dims(along, lane)
    whole = jnp.zeros(along.shape[:lane] + (count,) + along.shape[lane + 1 :], cells.dtype)
    gb_at = lax.axis_index(spread)
    whole = place(along, whole, lane, gb_at)
    for mask in range(1, count):
        arrived = lax.ppermute(along, spread, [(i, i ^ mask) for i in range(count)])
        whole = place(arrived, whole, lane, lax.bitwise_xor(gb_at, mask))
    if last:
        whole = jnp.moveaxis(whole, 1, -2)
    shape = list(cells.shape)
    shape[dim] = shape[dim] * ring
    return whole.reshape(shape), (along, whole)


def gather_seq(parts, width, after=(None, None)):
    spread = ("group", "batch")
    count = lax.axis_size("group") * lax.axis_size("batch")
    ring = lax.axis_size("seq")
    flats = [cells.reshape(-1, width) for cells, _ in parts]
    flat = jnp.concatenate(flats, axis=0) if len(flats) > 1 else flats[0]
    rows = flat.shape[0]
    size = -(-rows // count)
    if size * count != rows:
        flat = jnp.pad(flat, ((0, size * count - rows), (0, 0)))
    piece = lax.dynamic_slice_in_dim(flat, lax.axis_index(spread) * size, size, 0)
    if after[0] is not None:
        piece = lax.optimization_barrier((piece, after[0]))[0]
    if ring <= 8:
        place = lax.axis_index("seq")
        along = jnp.zeros((ring,) + piece.shape, piece.dtype)
        along = lax.dynamic_update_slice_in_dim(along, piece[None], place, 0)
        for shift in range(1, ring):
            arrived = lax.ppermute(piece, "seq", [(i, (i + shift) % ring) for i in range(ring)])
            along = lax.dynamic_update_slice_in_dim(
                along, arrived[None], (place + ring - shift) % ring, 0
            )
    else:
        along = lax.all_gather(piece, "seq", axis=0, tiled=False)
    if after[1] is not None:
        along = lax.optimization_barrier((along, after[1]))[0]
    if ring <= 8 and count <= 4:
        place = lax.axis_index(spread)
        whole = jnp.zeros((count,) + along.shape, along.dtype)
        whole = lax.dynamic_update_slice_in_dim(whole, along[None], place, 0)
        for mask in range(1, count):
            arrived = lax.ppermute(along, spread, [(i, i ^ mask) for i in range(count)])
            whole = lax.dynamic_update_slice_in_dim(
                whole, arrived[None], lax.bitwise_xor(place, mask), 0
            )
    else:
        whole = lax.all_gather(along, spread, axis=0, tiled=False)
    whole = whole.transpose(1, 0, 2, 3).reshape(ring, count * size, width)
    results = []
    stages = (along, whole)
    offset = 0
    for (cells, dim), part in zip(parts, flats):
        block = whole[:, offset : offset + part.shape[0]]
        offset += part.shape[0]
        block = jnp.moveaxis(block.reshape((ring,) + cells.shape), 0, dim)
        shape = list(cells.shape)
        shape[dim] = shape[dim] * ring
        results.append(block.reshape(shape))
    return results, stages


def swap_mp(cells):
    return lax.ppermute(cells, "mp", [(0, 1), (1, 0)])


def add_halves(cells, dim):
    half = cells.shape[dim] // 2
    index = lax.axis_index("mp")
    own = lax.dynamic_slice_in_dim(cells, index * half, half, dim)
    other = lax.dynamic_slice_in_dim(cells, (1 - index) * half, half, dim)
    return (own.astype(jnp.float32) + swap_mp(other).astype(jnp.float32)).astype(
        jnp.bfloat16
    ).astype(jnp.float32)


def attend_rows(query, keys, values):
    key_total = keys.shape[0]
    block_len = min(512, key_total)
    head_size = keys.shape[1]
    score_scale = head_size ** (-0.5)
    key_blocks = keys.reshape(key_total // block_len, block_len, head_size)
    value_blocks = values.reshape(key_total // block_len, block_len, head_size)
    query_count = query.shape[0]

    def find_top(carry, key_block):
        row_top, row_mass = carry
        scores = jnp.dot(query, key_block.T, preferred_element_type=jnp.float32) * score_scale
        new_top = jnp.maximum(row_top, jnp.max(scores, axis=1))
        row_mass = row_mass * jnp.exp(row_top - new_top) + jnp.sum(
            jnp.exp(scores - new_top[:, None]), axis=1
        )
        return ((new_top, row_mass), None)

    start_top = jnp.full((query_count,), -1e30, jnp.float32)
    (row_top, row_mass), _ = lax.scan(
        find_top, (start_top, jnp.zeros((query_count,), jnp.float32)), key_blocks
    )
    log_mass = row_top + jnp.log(row_mass)

    def collect(running, blocks):
        key_block, value_block = blocks
        scores = jnp.dot(query, key_block.T, preferred_element_type=jnp.float32) * score_scale
        soft_weights = jnp.exp(scores - log_mass[:, None]).astype(jnp.bfloat16)
        return (
            running + jnp.dot(soft_weights, value_block, preferred_element_type=jnp.float32),
            None,
        )

    running, _ = lax.scan(
        collect, jnp.zeros((query_count, head_size), jnp.float32), (key_blocks, value_blocks)
    )
    return (running.astype(jnp.bfloat16), log_mass)


def attend_back(query, keys, values, attended, log_mass, out_grad):
    key_total = keys.shape[0]
    block_len = min(512, key_total)
    head_size = keys.shape[1]
    score_scale = head_size ** (-0.5)
    key_blocks = keys.reshape(key_total // block_len, block_len, head_size)
    value_blocks = values.reshape(key_total // block_len, block_len, head_size)
    row_dot = jnp.sum(out_grad.astype(jnp.float32) * attended.astype(jnp.float32), axis=1)

    def step_back(query_acc, blocks):
        key_block, value_block = blocks
        scores = jnp.dot(query, key_block.T, preferred_element_type=jnp.float32) * score_scale
        exp_weights = jnp.exp(scores - log_mass[:, None])
        value_part = jnp.einsum(
            "qk,qd->kd",
            exp_weights.astype(jnp.bfloat16),
            out_grad,
            preferred_element_type=jnp.float32,
        )
        prob_grad = jnp.dot(out_grad, value_block.T, preferred_element_type=jnp.float32)
        score_grad = (exp_weights * (prob_grad - row_dot[:, None])).astype(jnp.bfloat16)
        query_acc = (
            query_acc
            + jnp.dot(score_grad, key_block, preferred_element_type=jnp.float32) * score_scale
        )
        key_part = (
            jnp.einsum("qk,qd->kd", score_grad, query, preferred_element_type=jnp.float32)
            * score_scale
        )
        return (query_acc, jnp.concatenate([key_part, value_part], axis=1))

    query_grad, keyval_parts = lax.scan(
        step_back, jnp.zeros((query.shape[0], head_size), jnp.float32), (key_blocks, value_blocks)
    )
    return (query_grad, keyval_parts.reshape(key_total, 2 * head_size))


def forward(stack, conv_weight, conv_bias, norm_gain, qkv_weight, out_weight):
    pass_count, positions, channels = stack.shape
    reach = KW // 2
    half_width = conv_weight.shape[2]
    padded_input = with_halo(stack, (("seq", 1),), reach)
    running = jnp.zeros((pass_count, positions, half_width), jnp.float32)
    piece = conv_weight
    for offset in range(piece.shape[0]):
        running = running + jnp.einsum(
            "ptc,cf->ptf",
            padded_input[:, offset : offset + positions],
            piece[offset],
            preferred_element_type=jnp.float32,
        )
    pre_act = running + conv_bias
    paired = jax.nn.gelu(pre_act).reshape(pass_count, positions // 2, 2, half_width)
    pooled = (0.5 * (paired[:, :, 0] + paired[:, :, 1])).astype(jnp.bfloat16)
    pooled_wide = lax.optimization_barrier(pooled).astype(jnp.float32)
    whole = lax.all_gather(pooled, "mp", axis=2, tiled=True)
    whole_wide = whole.astype(jnp.float32)
    row_scale = lax.rsqrt(jnp.mean(whole_wide * whole_wide, axis=2, keepdims=True) + epsilon)
    normed = (whole_wide * row_scale * norm_gain).astype(jnp.bfloat16)
    rows = positions // 2
    proj_width = qkv_weight.shape[2]
    projected = jnp.einsum(
        "prf,jfh->jprh",
        normed,
        qkv_weight,
        preferred_element_type=jnp.float32,
    ).astype(jnp.bfloat16)
    head_size = HD
    head_count = proj_width // head_size
    devices = lax.axis_size("seq")
    query_groups = devices // head_count
    sub_rows = rows // query_groups
    query_send = (
        projected[0]
        .reshape(pass_count, query_groups, sub_rows, head_count, head_size)
        .transpose(3, 1, 0, 2, 4)
        .reshape(devices, pass_count, sub_rows * head_size)
    )
    keyval = jnp.concatenate(
        [
            projected[1].reshape(pass_count, rows, head_count, head_size),
            projected[2].reshape(pass_count, rows, head_count, head_size),
        ],
        axis=3,
    )
    keyval_flat = keyval.transpose(2, 0, 1, 3).reshape(
        head_count, 1, pass_count, rows * 2 * head_size
    )
    keyval_send = jnp.broadcast_to(
        keyval_flat, (head_count, query_groups, pass_count, rows * 2 * head_size)
    ).reshape(devices, pass_count, rows * 2 * head_size)
    query_len = query_send.shape[2]
    both_in = lax.all_to_all(
        jnp.concatenate([query_send, keyval_send], axis=2),
        "seq",
        split_axis=0,
        concat_axis=2,
        tiled=True,
    ).reshape(pass_count, devices, query_len + keyval_send.shape[2])
    query_heads = both_in[:, :, :query_len].reshape(pass_count, devices * sub_rows, head_size)
    keyval_heads = both_in[:, :, query_len:].reshape(pass_count, devices * rows, 2 * head_size)
    outputs = []
    masses = []
    for index in range(pass_count):
        out_now, mass_now = attend_rows(
            query_heads[index],
            keyval_heads[index, :, :head_size],
            keyval_heads[index, :, head_size:],
        )
        outputs.append(out_now)
        masses.append(mass_now)
    attended_heads = jnp.stack(outputs)
    log_mass = jnp.stack(masses)
    out_send = attended_heads.reshape(pass_count, devices, sub_rows * head_size).transpose(1, 0, 2)
    out_back = lax.all_to_all(out_send, "seq", split_axis=0, concat_axis=0, tiled=True)
    attended = (
        out_back.reshape(head_count, query_groups, pass_count, sub_rows, head_size)
        .transpose(2, 1, 3, 0, 4)
        .reshape(pass_count, rows, proj_width)
    )
    terms = jnp.einsum(
        "prh,hf->prf",
        attended,
        out_weight,
        preferred_element_type=jnp.float32,
    )
    mixed = (
        add_halves(terms.astype(jnp.bfloat16), 2) + pooled_wide
    )
    return (
        pre_act,
        pooled_wide,
        whole_wide,
        row_scale,
        query_heads,
        keyval_heads,
        attended_heads,
        log_mass,
        mixed,
    )


def shards(features, noise, conv_weight, conv_bias, norm_gain, qkv_weight, out_weight):
    width = conv_weight.shape[-1]
    direct = (
        lax.axis_size("seq") <= 8
        and lax.axis_size("group") * lax.axis_size("batch") <= 4
        and conv_weight.shape[1] % (4 * lax.axis_size("group") * lax.axis_size("batch")) == 0
        and qkv_weight.shape[1] % (4 * lax.axis_size("group") * lax.axis_size("batch")) == 0
        and out_weight.shape[0] % (4 * lax.axis_size("group") * lax.axis_size("batch")) == 0
    )
    if direct:
        conv_weight, _ = gather_blocks(conv_weight, 1)
        qkv_weight, _ = gather_blocks(qkv_weight, 1)
        out_weight, _ = gather_blocks(out_weight, 1)
        qkv_weight, out_weight = lax.optimization_barrier((qkv_weight, out_weight))
    else:
        (conv_weight,), _ = gather_seq([(conv_weight, 1)], width)
        (qkv_weight,), _ = gather_seq([(qkv_weight, 1)], width)
        (out_weight,), _ = gather_seq([(out_weight, 1)], width)
    clean = features[0]
    moved = (clean.astype(jnp.float32) + noise[0]).astype(jnp.bfloat16)
    joint = forward(
        jnp.stack([clean, moved]), conv_weight, conv_bias, norm_gain, qkv_weight, out_weight
    )
    clean_run = [item[0:1] for item in joint]
    moved_run = [item[1:2] for item in joint]
    (
        pre_act,
        pooled_wide,
        whole_wide,
        row_scale,
        query_heads,
        keyval_heads,
        attended_heads,
        log_mass,
        mixed,
    ) = [item[0] for item in moved_run]
    clean_mixed = clean_run[8][0]
    rows, half_width = pooled_wide.shape
    positions = pre_act.shape[0]
    proj_width = qkv_weight.shape[2]
    head_size = HD
    head_count = proj_width // head_size
    devices = lax.axis_size("seq")
    query_groups = devices // head_count
    sub_rows = rows // query_groups
    difference = mixed - clean_mixed
    difference_half = difference.astype(jnp.bfloat16)
    difference_whole = lax.all_gather(difference_half, "mp", axis=1, tiled=True)
    out_grad = jnp.einsum(
        "rf,hf->rh",
        difference_whole,
        out_weight,
        preferred_element_type=jnp.float32,
    ).astype(jnp.bfloat16)
    grad_send = (
        out_grad.reshape(query_groups, sub_rows, head_count, head_size)
        .transpose(2, 0, 1, 3)
        .reshape(devices, sub_rows * head_size)
    )
    grad_in = lax.all_to_all(grad_send, "seq", split_axis=0, concat_axis=1, tiled=True)
    grad_heads = grad_in.reshape(devices * sub_rows, head_size)
    query_grad, keyval_grad = attend_back(
        query_heads,
        keyval_heads[:, :head_size],
        keyval_heads[:, head_size:],
        attended_heads,
        log_mass,
        grad_heads,
    )
    query_len = sub_rows * head_size
    both_back = lax.all_to_all(
        jnp.concatenate(
            [
                query_grad.reshape(devices, query_len).astype(jnp.bfloat16),
                keyval_grad.reshape(devices, rows * 2 * head_size).astype(jnp.bfloat16),
            ],
            axis=1,
        ),
        "seq",
        split_axis=0,
        concat_axis=0,
        tiled=True,
    ).astype(jnp.float32)
    query_back = both_back[:, :query_len]
    keyval_back = both_back[:, query_len:]
    query_rows = (
        query_back.reshape(head_count, query_groups, sub_rows, head_size)
        .transpose(1, 2, 0, 3)
        .reshape(rows, proj_width)
        .astype(jnp.bfloat16)
    )
    keyval_rows = jnp.sum(keyval_back.reshape(head_count, query_groups, rows, 2, head_size), axis=1)
    key_rows = (
        keyval_rows[:, :, 0].transpose(1, 0, 2).reshape(rows, proj_width).astype(jnp.bfloat16)
    )
    value_rows = (
        keyval_rows[:, :, 1].transpose(1, 0, 2).reshape(rows, proj_width).astype(jnp.bfloat16)
    )
    grads = jnp.stack([query_rows, key_rows, value_rows])
    normed_terms = jnp.einsum(
        "jrh,jfh->rf",
        grads,
        qkv_weight,
        preferred_element_type=jnp.float32,
    )
    offset_mp = lax.axis_index("mp") * half_width
    gain_own = lax.dynamic_slice_in_dim(norm_gain, offset_mp, half_width, 0)
    normed_grad = add_halves(normed_terms.astype(jnp.bfloat16), 1)
    weighted = lax.psum(jnp.sum(normed_grad * gain_own * pooled_wide, axis=1, keepdims=True), "mp")
    pooled_grad = (
        difference + row_scale * gain_own * normed_grad - pooled_wide * row_scale**3 * weighted / F
    )
    spread = jnp.broadcast_to((0.5 * pooled_grad)[:, None, :], (rows, 2, half_width)).reshape(
        positions, half_width
    )
    gelu_back = jax.vjp(jax.nn.gelu, pre_act)[1]
    pre_grad = gelu_back(spread)[0].astype(jnp.bfloat16)
    reach = KW // 2
    padded = with_halo(pre_grad, (("seq", 0),), reach)
    piece = conv_weight
    running = jnp.zeros((positions, piece.shape[1]), jnp.float32)
    for offset in range(piece.shape[0]):
        lower = 2 * reach - offset
        running = running + jnp.einsum(
            "tf,cf->tc",
            padded[lower : lower + positions],
            piece[offset],
            preferred_element_type=jnp.float32,
        )
    own_grad = running.astype(jnp.bfloat16)
    input_grad = (own_grad.astype(jnp.float32) + swap_mp(own_grad).astype(jnp.float32)).astype(
        jnp.bfloat16
    ).astype(jnp.float32)
    new_noise = noise[0] + step_size * input_grad * lax.rsqrt(
        jnp.mean(input_grad * input_grad, axis=1, keepdims=True) + epsilon
    )
    return (clean_mixed.astype(jnp.bfloat16)[None], new_noise[None])


def solution(mesh):
    return jax.shard_map(
        shards,
        mesh=mesh,
        in_specs=(
            P(("group", "batch"), "seq", None),
            P(("group", "batch"), "seq", None),
            P(None, "seq", "mp"),
            P("mp"),
            P(),
            P(None, "seq", "mp"),
            P("mp", "seq"),
        ),
        out_specs=(P(("group", "batch"), "seq", "mp"), P(("group", "batch"), "seq", None)),
        check_vma=False,
    )
```

```python
import jax
import jax.numpy as jnp
from jax import lax
from jax.sharding import PartitionSpec as P

F = 768
HD = 96
KW = 5


step_size = 0.5
epsilon = 1e-06


def with_halo(cells, sides, width):
    for axis, dim in sides:
        count = lax.axis_size(axis)
        ends = count - 1
        head = lax.slice_in_dim(cells, 0, width, axis=dim)
        tail = lax.slice_in_dim(cells, cells.shape[dim] - width, cells.shape[dim], axis=dim)
        cells = jnp.concatenate(
            [
                lax.ppermute(tail, axis, [(i, (i + 1) % count) for i in range(ends)]),
                cells,
                lax.ppermute(head, axis, [((i + 1) % count, i) for i in range(ends)]),
            ],
            axis=dim,
        )
    return cells


def gather_seq(parts, width):
    spread = ("group", "batch")
    count = lax.axis_size("group") * lax.axis_size("batch")
    ring = lax.axis_size("seq")
    flats = [cells.reshape(-1, width) for cells, _ in parts]
    flat = jnp.concatenate(flats, axis=0) if len(flats) > 1 else flats[0]
    rows = flat.shape[0]
    size = -(-rows // count)
    if size * count != rows:
        flat = jnp.pad(flat, ((0, size * count - rows), (0, 0)))
    piece = lax.dynamic_slice_in_dim(flat, lax.axis_index(spread) * size, size, 0)
    if ring <= 8:
        place = lax.axis_index("seq")
        along = jnp.zeros((ring,) + piece.shape, piece.dtype)
        along = lax.dynamic_update_slice_in_dim(along, piece[None], place, 0)
        for shift in range(1, ring):
            arrived = lax.ppermute(piece, "seq", [(i, (i + shift) % ring) for i in range(ring)])
            along = lax.dynamic_update_slice_in_dim(
                along, arrived[None], (place + ring - shift) % ring, 0
            )
    else:
        along = lax.all_gather(piece, "seq", axis=0, tiled=False)
    if ring <= 8 and count <= 4:
        place = lax.axis_index(spread)
        whole = jnp.zeros((count,) + along.shape, along.dtype)
        whole = lax.dynamic_update_slice_in_dim(whole, along[None], place, 0)
        for mask in range(1, count):
            arrived = lax.ppermute(along, spread, [(i, i ^ mask) for i in range(count)])
            whole = lax.dynamic_update_slice_in_dim(
                whole, arrived[None], lax.bitwise_xor(place, mask), 0
            )
    else:
        whole = lax.all_gather(along, spread, axis=0, tiled=False)
    whole = whole.transpose(1, 0, 2, 3).reshape(ring, count * size, width)
    results = []
    offset = 0
    for (cells, dim), part in zip(parts, flats):
        block = whole[:, offset : offset + part.shape[0]]
        offset += part.shape[0]
        block = jnp.moveaxis(block.reshape((ring,) + cells.shape), 0, dim)
        shape = list(cells.shape)
        shape[dim] = shape[dim] * ring
        results.append(block.reshape(shape))
    return results


def swap_mp(cells):
    return lax.ppermute(cells, "mp", [(0, 1), (1, 0)])


def join_mp(cells, dim):
    other = swap_mp(cells)
    first = lax.axis_index("mp") == 0
    return jnp.where(
        first, jnp.concatenate([cells, other], axis=dim), jnp.concatenate([other, cells], axis=dim)
    )


def add_halves(cells, dim):
    half = cells.shape[dim] // 2
    index = lax.axis_index("mp")
    own = lax.dynamic_slice_in_dim(cells, index * half, half, dim)
    other = lax.dynamic_slice_in_dim(cells, (1 - index) * half, half, dim)
    return (own.astype(jnp.float32) + swap_mp(other).astype(jnp.float32)).astype(
        jnp.bfloat16
    ).astype(jnp.float32)


def attend_rows(query, keys, values):
    key_total = keys.shape[0]
    block_len = min(512, key_total)
    head_size = keys.shape[1]
    score_scale = head_size ** (-0.5)
    key_blocks = keys.reshape(key_total // block_len, block_len, head_size)
    value_blocks = values.reshape(key_total // block_len, block_len, head_size)
    query_count = query.shape[0]

    def find_top(carry, key_block):
        row_top, row_mass = carry
        scores = jnp.dot(query, key_block.T, preferred_element_type=jnp.float32) * score_scale
        new_top = jnp.maximum(row_top, jnp.max(scores, axis=1))
        row_mass = row_mass * jnp.exp(row_top - new_top) + jnp.sum(
            jnp.exp(scores - new_top[:, None]), axis=1
        )
        return ((new_top, row_mass), None)

    start_top = jnp.full((query_count,), -1e30, jnp.float32)
    (row_top, row_mass), _ = lax.scan(
        find_top, (start_top, jnp.zeros((query_count,), jnp.float32)), key_blocks
    )
    log_mass = row_top + jnp.log(row_mass)

    def collect(running, blocks):
        key_block, value_block = blocks
        scores = jnp.dot(query, key_block.T, preferred_element_type=jnp.float32) * score_scale
        soft_weights = jnp.exp(scores - log_mass[:, None]).astype(jnp.bfloat16)
        return (
            running + jnp.dot(soft_weights, value_block, preferred_element_type=jnp.float32),
            None,
        )

    running, _ = lax.scan(
        collect, jnp.zeros((query_count, head_size), jnp.float32), (key_blocks, value_blocks)
    )
    return (running.astype(jnp.bfloat16), log_mass)


def attend_back(query, keys, values, attended, log_mass, out_grad):
    key_total = keys.shape[0]
    block_len = min(512, key_total)
    head_size = keys.shape[1]
    score_scale = head_size ** (-0.5)
    key_blocks = keys.reshape(key_total // block_len, block_len, head_size)
    value_blocks = values.reshape(key_total // block_len, block_len, head_size)
    row_dot = jnp.sum(out_grad.astype(jnp.float32) * attended.astype(jnp.float32), axis=1)

    def step_back(query_acc, blocks):
        key_block, value_block = blocks
        scores = jnp.dot(query, key_block.T, preferred_element_type=jnp.float32) * score_scale
        exp_weights = jnp.exp(scores - log_mass[:, None])
        value_part = jnp.einsum(
            "qk,qd->kd",
            exp_weights.astype(jnp.bfloat16),
            out_grad,
            preferred_element_type=jnp.float32,
        )
        prob_grad = jnp.dot(out_grad, value_block.T, preferred_element_type=jnp.float32)
        score_grad = (exp_weights * (prob_grad - row_dot[:, None])).astype(jnp.bfloat16)
        query_acc = (
            query_acc
            + jnp.dot(score_grad, key_block, preferred_element_type=jnp.float32) * score_scale
        )
        key_part = (
            jnp.einsum("qk,qd->kd", score_grad, query, preferred_element_type=jnp.float32)
            * score_scale
        )
        return (query_acc, jnp.concatenate([key_part, value_part], axis=1))

    query_grad, keyval_parts = lax.scan(
        step_back, jnp.zeros((query.shape[0], head_size), jnp.float32), (key_blocks, value_blocks)
    )
    return (query_grad, keyval_parts.reshape(key_total, 2 * head_size))


def forward(stack, conv_weight, conv_bias, norm_gain, qkv_weight, out_weight):
    pass_count, positions, channels = stack.shape
    reach = KW // 2
    half_width = conv_weight.shape[2]
    padded_input = with_halo(stack, (("seq", 1),), reach)
    running = jnp.zeros((pass_count, positions, half_width), jnp.float32)
    piece = conv_weight
    for offset in range(piece.shape[0]):
        running = running + jnp.einsum(
            "ptc,cf->ptf",
            padded_input[:, offset : offset + positions],
            piece[offset],
            preferred_element_type=jnp.float32,
        )
    pre_act = running + conv_bias
    paired = jax.nn.gelu(pre_act).reshape(pass_count, positions // 2, 2, half_width)
    pooled = (0.5 * (paired[:, :, 0] + paired[:, :, 1])).astype(jnp.bfloat16)
    pooled_wide = lax.optimization_barrier(pooled).astype(jnp.float32)
    whole = join_mp(pooled, 2)
    whole_wide = whole.astype(jnp.float32)
    row_scale = lax.rsqrt(jnp.mean(whole_wide * whole_wide, axis=2, keepdims=True) + epsilon)
    normed = (whole_wide * row_scale * norm_gain).astype(jnp.bfloat16)
    rows = positions // 2
    proj_width = qkv_weight.shape[2]
    projected = jnp.einsum(
        "prf,jfh->jprh",
        normed,
        qkv_weight,
        preferred_element_type=jnp.float32,
    ).astype(jnp.bfloat16)
    head_size = HD
    head_count = proj_width // head_size
    devices = lax.axis_size("seq")
    query_groups = devices // head_count
    sub_rows = rows // query_groups
    query_send = (
        projected[0]
        .reshape(pass_count, query_groups, sub_rows, head_count, head_size)
        .transpose(3, 1, 0, 2, 4)
        .reshape(devices, pass_count, sub_rows * head_size)
    )
    keyval = jnp.concatenate(
        [
            projected[1].reshape(pass_count, rows, head_count, head_size),
            projected[2].reshape(pass_count, rows, head_count, head_size),
        ],
        axis=3,
    )
    keyval_flat = keyval.transpose(2, 0, 1, 3).reshape(
        head_count, 1, pass_count, rows * 2 * head_size
    )
    keyval_send = jnp.broadcast_to(
        keyval_flat, (head_count, query_groups, pass_count, rows * 2 * head_size)
    ).reshape(devices, pass_count, rows * 2 * head_size)
    query_len = query_send.shape[2]
    both_in = lax.all_to_all(
        jnp.concatenate([query_send, keyval_send], axis=2),
        "seq",
        split_axis=0,
        concat_axis=2,
        tiled=True,
    ).reshape(pass_count, devices, query_len + keyval_send.shape[2])
    query_heads = both_in[:, :, :query_len].reshape(pass_count, devices * sub_rows, head_size)
    keyval_heads = both_in[:, :, query_len:].reshape(pass_count, devices * rows, 2 * head_size)
    outputs = []
    masses = []
    for index in range(pass_count):
        out_now, mass_now = attend_rows(
            query_heads[index],
            keyval_heads[index, :, :head_size],
            keyval_heads[index, :, head_size:],
        )
        outputs.append(out_now)
        masses.append(mass_now)
    attended_heads = jnp.stack(outputs)
    log_mass = jnp.stack(masses)
    out_send = attended_heads.reshape(pass_count, devices, sub_rows * head_size).transpose(1, 0, 2)
    out_back = lax.all_to_all(out_send, "seq", split_axis=0, concat_axis=0, tiled=True)
    attended = (
        out_back.reshape(head_count, query_groups, pass_count, sub_rows, head_size)
        .transpose(2, 1, 3, 0, 4)
        .reshape(pass_count, rows, proj_width)
    )
    terms = jnp.einsum(
        "prh,hf->prf",
        attended,
        out_weight,
        preferred_element_type=jnp.float32,
    )
    mixed = (
        add_halves(terms.astype(jnp.bfloat16), 2) + pooled_wide
    )
    return (
        pre_act,
        pooled_wide,
        whole_wide,
        row_scale,
        query_heads,
        keyval_heads,
        attended_heads,
        log_mass,
        mixed,
    )


def shards(features, noise, conv_weight, conv_bias, norm_gain, qkv_weight, out_weight):
    width = conv_weight.shape[-1]
    (conv_weight,) = gather_seq([(conv_weight, 1)], width)
    (qkv_weight,) = gather_seq([(qkv_weight, 1)], width)
    (out_weight,) = gather_seq([(out_weight, 1)], width)
    clean = features[0]
    moved = (clean.astype(jnp.float32) + noise[0]).astype(jnp.bfloat16)
    joint = forward(
        jnp.stack([clean, moved]), conv_weight, conv_bias, norm_gain, qkv_weight, out_weight
    )
    clean_run = [item[0:1] for item in joint]
    moved_run = [item[1:2] for item in joint]
    (
        pre_act,
        pooled_wide,
        whole_wide,
        row_scale,
        query_heads,
        keyval_heads,
        attended_heads,
        log_mass,
        mixed,
    ) = [item[0] for item in moved_run]
    clean_mixed = clean_run[8][0]
    rows, half_width = pooled_wide.shape
    positions = pre_act.shape[0]
    proj_width = qkv_weight.shape[2]
    head_size = HD
    head_count = proj_width // head_size
    devices = lax.axis_size("seq")
    query_groups = devices // head_count
    sub_rows = rows // query_groups
    difference = mixed - clean_mixed
    difference_half = difference.astype(jnp.bfloat16)
    difference_whole = join_mp(difference_half, 1)
    out_grad = jnp.einsum(
        "rf,hf->rh",
        difference_whole,
        out_weight,
        preferred_element_type=jnp.float32,
    ).astype(jnp.bfloat16)
    grad_send = (
        out_grad.reshape(query_groups, sub_rows, head_count, head_size)
        .transpose(2, 0, 1, 3)
        .reshape(devices, sub_rows * head_size)
    )
    grad_in = lax.all_to_all(grad_send, "seq", split_axis=0, concat_axis=1, tiled=True)
    grad_heads = grad_in.reshape(devices * sub_rows, head_size)
    query_grad, keyval_grad = attend_back(
        query_heads,
        keyval_heads[:, :head_size],
        keyval_heads[:, head_size:],
        attended_heads,
        log_mass,
        grad_heads,
    )
    query_len = sub_rows * head_size
    both_back = lax.all_to_all(
        jnp.concatenate(
            [
                query_grad.reshape(devices, query_len).astype(jnp.bfloat16),
                keyval_grad.reshape(devices, rows * 2 * head_size).astype(jnp.bfloat16),
            ],
            axis=1,
        ),
        "seq",
        split_axis=0,
        concat_axis=0,
        tiled=True,
    ).astype(jnp.float32)
    query_back = both_back[:, :query_len]
    keyval_back = both_back[:, query_len:]
    query_rows = (
        query_back.reshape(head_count, query_groups, sub_rows, head_size)
        .transpose(1, 2, 0, 3)
        .reshape(rows, proj_width)
        .astype(jnp.bfloat16)
    )
    keyval_rows = jnp.sum(keyval_back.reshape(head_count, query_groups, rows, 2, head_size), axis=1)
    key_rows = (
        keyval_rows[:, :, 0].transpose(1, 0, 2).reshape(rows, proj_width).astype(jnp.bfloat16)
    )
    value_rows = (
        keyval_rows[:, :, 1].transpose(1, 0, 2).reshape(rows, proj_width).astype(jnp.bfloat16)
    )
    grads = jnp.stack([query_rows, key_rows, value_rows])
    normed_terms = jnp.einsum(
        "jrh,jfh->rf",
        grads,
        qkv_weight,
        preferred_element_type=jnp.float32,
    )
    offset_mp = lax.axis_index("mp") * half_width
    gain_own = lax.dynamic_slice_in_dim(norm_gain, offset_mp, half_width, 0)
    normed_grad = add_halves(normed_terms.astype(jnp.bfloat16), 1)
    weighted_own = jnp.sum(normed_grad * gain_own * pooled_wide, axis=1, keepdims=True)
    weighted = weighted_own + swap_mp(weighted_own)
    pooled_grad = (
        difference + row_scale * gain_own * normed_grad - pooled_wide * row_scale**3 * weighted / F
    )
    spread = jnp.broadcast_to((0.5 * pooled_grad)[:, None, :], (rows, 2, half_width)).reshape(
        positions, half_width
    )
    gelu_back = jax.vjp(jax.nn.gelu, pre_act)[1]
    pre_grad = gelu_back(spread)[0].astype(jnp.bfloat16)
    reach = KW // 2
    padded = with_halo(pre_grad, (("seq", 0),), reach)
    piece = conv_weight
    running = jnp.zeros((positions, piece.shape[1]), jnp.float32)
    for offset in range(piece.shape[0]):
        lower = 2 * reach - offset
        running = running + jnp.einsum(
            "tf,cf->tc",
            padded[lower : lower + positions],
            piece[offset],
            preferred_element_type=jnp.float32,
        )
    own_grad = running.astype(jnp.bfloat16)
    input_grad = (own_grad.astype(jnp.float32) + swap_mp(own_grad).astype(jnp.float32)).astype(
        jnp.bfloat16
    ).astype(jnp.float32)
    new_noise = noise[0] + step_size * input_grad * lax.rsqrt(
        jnp.mean(input_grad * input_grad, axis=1, keepdims=True) + epsilon
    )
    return (clean_mixed.astype(jnp.bfloat16)[None], new_noise[None])


def solution(mesh):
    return jax.shard_map(
        shards,
        mesh=mesh,
        in_specs=(
            P(("group", "batch"), "seq", None),
            P(("group", "batch"), "seq", None),
            P(None, "seq", "mp"),
            P("mp"),
            P(),
            P(None, "seq", "mp"),
            P("mp", "seq"),
        ),
        out_specs=(P(("group", "batch"), "seq", "mp"), P(("group", "batch"), "seq", None)),
        check_vma=False,
    )
```

```python
import jax
import jax.numpy as jnp
from jax import lax
from jax.sharding import PartitionSpec as P

F = 768
HD = 96
KW = 5


step_size = 0.5
epsilon = 1e-06


def with_halo(cells, sides, width):
    for axis, dim in sides:
        count = lax.axis_size(axis)
        ends = count - 1
        head = lax.slice_in_dim(cells, 0, width, axis=dim)
        tail = lax.slice_in_dim(cells, cells.shape[dim] - width, cells.shape[dim], axis=dim)
        cells = jnp.concatenate(
            [
                lax.ppermute(tail, axis, [(i, (i + 1) % count) for i in range(ends)]),
                cells,
                lax.ppermute(head, axis, [((i + 1) % count, i) for i in range(ends)]),
            ],
            axis=dim,
        )
    return cells


def gather_seq(parts, width):
    spread = ("group", "batch")
    count = lax.axis_size("group") * lax.axis_size("batch")
    ring = lax.axis_size("seq")
    flats = [cells.reshape(-1, width) for cells, _ in parts]
    flat = jnp.concatenate(flats, axis=0) if len(flats) > 1 else flats[0]
    rows = flat.shape[0]
    size = -(-rows // count)
    if size * count != rows:
        flat = jnp.pad(flat, ((0, size * count - rows), (0, 0)))
    piece = lax.dynamic_slice_in_dim(flat, lax.axis_index(spread) * size, size, 0)
    if ring <= 8:
        place = lax.axis_index("seq")
        along = jnp.zeros((ring,) + piece.shape, piece.dtype)
        along = lax.dynamic_update_slice_in_dim(along, piece[None], place, 0)
        for shift in range(1, ring):
            arrived = lax.ppermute(piece, "seq", [(i, (i + shift) % ring) for i in range(ring)])
            along = lax.dynamic_update_slice_in_dim(
                along, arrived[None], (place + ring - shift) % ring, 0
            )
    else:
        along = lax.all_gather(piece, "seq", axis=0, tiled=False)
    if ring <= 8 and count <= 4:
        place = lax.axis_index(spread)
        whole = jnp.zeros((count,) + along.shape, along.dtype)
        whole = lax.dynamic_update_slice_in_dim(whole, along[None], place, 0)
        for mask in range(1, count):
            arrived = lax.ppermute(along, spread, [(i, i ^ mask) for i in range(count)])
            whole = lax.dynamic_update_slice_in_dim(
                whole, arrived[None], lax.bitwise_xor(place, mask), 0
            )
    else:
        whole = lax.all_gather(along, spread, axis=0, tiled=False)
    whole = whole.transpose(1, 0, 2, 3).reshape(ring, count * size, width)
    results = []
    offset = 0
    for (cells, dim), part in zip(parts, flats):
        block = whole[:, offset : offset + part.shape[0]]
        offset += part.shape[0]
        block = jnp.moveaxis(block.reshape((ring,) + cells.shape), 0, dim)
        shape = list(cells.shape)
        shape[dim] = shape[dim] * ring
        results.append(block.reshape(shape))
    return results


def swap_mp(cells):
    return lax.ppermute(cells, "mp", [(0, 1), (1, 0)])


def add_halves(cells, dim):
    half = cells.shape[dim] // 2
    index = lax.axis_index("mp")
    own = lax.dynamic_slice_in_dim(cells, index * half, half, dim)
    other = lax.dynamic_slice_in_dim(cells, (1 - index) * half, half, dim)
    return (own.astype(jnp.float32) + swap_mp(other).astype(jnp.float32)).astype(
        jnp.bfloat16
    ).astype(jnp.float32)


def attend_rows(query, keys, values):
    key_total = keys.shape[0]
    block_len = min(512, key_total)
    head_size = keys.shape[1]
    score_scale = head_size ** (-0.5)
    key_blocks = keys.reshape(key_total // block_len, block_len, head_size)
    value_blocks = values.reshape(key_total // block_len, block_len, head_size)
    query_count = query.shape[0]

    def find_top(carry, key_block):
        row_top, row_mass = carry
        scores = jnp.dot(query, key_block.T, preferred_element_type=jnp.float32) * score_scale
        new_top = jnp.maximum(row_top, jnp.max(scores, axis=1))
        row_mass = row_mass * jnp.exp(row_top - new_top) + jnp.sum(
            jnp.exp(scores - new_top[:, None]), axis=1
        )
        return ((new_top, row_mass), None)

    start_top = jnp.full((query_count,), -1e30, jnp.float32)
    (row_top, row_mass), _ = lax.scan(
        find_top, (start_top, jnp.zeros((query_count,), jnp.float32)), key_blocks
    )
    log_mass = row_top + jnp.log(row_mass)

    def collect(running, blocks):
        key_block, value_block = blocks
        scores = jnp.dot(query, key_block.T, preferred_element_type=jnp.float32) * score_scale
        soft_weights = jnp.exp(scores - log_mass[:, None]).astype(jnp.bfloat16)
        return (
            running + jnp.dot(soft_weights, value_block, preferred_element_type=jnp.float32),
            None,
        )

    running, _ = lax.scan(
        collect, jnp.zeros((query_count, head_size), jnp.float32), (key_blocks, value_blocks)
    )
    return (running.astype(jnp.bfloat16), log_mass)


def attend_back(query, keys, values, attended, log_mass, out_grad):
    key_total = keys.shape[0]
    block_len = min(512, key_total)
    head_size = keys.shape[1]
    score_scale = head_size ** (-0.5)
    key_blocks = keys.reshape(key_total // block_len, block_len, head_size)
    value_blocks = values.reshape(key_total // block_len, block_len, head_size)
    row_dot = jnp.sum(out_grad.astype(jnp.float32) * attended.astype(jnp.float32), axis=1)

    def step_back(query_acc, blocks):
        key_block, value_block = blocks
        scores = jnp.dot(query, key_block.T, preferred_element_type=jnp.float32) * score_scale
        exp_weights = jnp.exp(scores - log_mass[:, None])
        value_part = jnp.einsum(
            "qk,qd->kd",
            exp_weights.astype(jnp.bfloat16),
            out_grad,
            preferred_element_type=jnp.float32,
        )
        prob_grad = jnp.dot(out_grad, value_block.T, preferred_element_type=jnp.float32)
        score_grad = (exp_weights * (prob_grad - row_dot[:, None])).astype(jnp.bfloat16)
        query_acc = (
            query_acc
            + jnp.dot(score_grad, key_block, preferred_element_type=jnp.float32) * score_scale
        )
        key_part = (
            jnp.einsum("qk,qd->kd", score_grad, query, preferred_element_type=jnp.float32)
            * score_scale
        )
        return (query_acc, jnp.concatenate([key_part, value_part], axis=1))

    query_grad, keyval_parts = lax.scan(
        step_back, jnp.zeros((query.shape[0], head_size), jnp.float32), (key_blocks, value_blocks)
    )
    return (query_grad, keyval_parts.reshape(key_total, 2 * head_size))


def forward(stack, conv_weight, conv_bias, norm_gain, qkv_weight, out_weight):
    pass_count, positions, _ = stack.shape
    reach = KW // 2
    half_width = conv_weight.shape[2]
    padded_input = with_halo(stack, (("seq", 1),), reach)
    running = jnp.zeros((pass_count, positions, half_width), jnp.float32)
    piece = conv_weight
    for offset in range(piece.shape[0]):
        running = running + jnp.einsum(
            "ptc,cf->ptf",
            padded_input[:, offset : offset + positions],
            piece[offset],
            preferred_element_type=jnp.float32,
        )
    pre_act = running + conv_bias
    paired = jax.nn.gelu(pre_act).reshape(pass_count, positions // 2, 2, half_width)
    pooled = (0.5 * (paired[:, :, 0] + paired[:, :, 1])).astype(jnp.bfloat16)
    pooled_wide = lax.optimization_barrier(pooled).astype(jnp.float32)
    whole = lax.all_gather(pooled, "mp", axis=2, tiled=True)
    whole_wide = whole.astype(jnp.float32)
    row_scale = lax.rsqrt(jnp.mean(whole_wide * whole_wide, axis=2, keepdims=True) + epsilon)
    normed = (whole_wide * row_scale * norm_gain).astype(jnp.bfloat16)
    rows = positions // 2
    proj_width = qkv_weight.shape[2]
    projected = jnp.einsum(
        "prf,jfh->jprh",
        normed,
        qkv_weight,
        preferred_element_type=jnp.float32,
    ).astype(jnp.bfloat16)
    head_size = HD
    head_count = proj_width // head_size
    devices = lax.axis_size("seq")
    query_groups = devices // head_count
    sub_rows = rows // query_groups
    query_send = (
        projected[0]
        .reshape(pass_count, query_groups, sub_rows, head_count, head_size)
        .transpose(3, 1, 0, 2, 4)
        .reshape(devices, pass_count, sub_rows * head_size)
    )
    keyval = jnp.concatenate(
        [
            projected[1].reshape(pass_count, rows, head_count, head_size),
            projected[2].reshape(pass_count, rows, head_count, head_size),
        ],
        axis=3,
    )
    keyval_flat = keyval.transpose(2, 0, 1, 3).reshape(
        head_count, 1, pass_count, rows * 2 * head_size
    )
    keyval_send = jnp.broadcast_to(
        keyval_flat, (head_count, query_groups, pass_count, rows * 2 * head_size)
    ).reshape(devices, pass_count, rows * 2 * head_size)
    query_len = query_send.shape[2]
    both_in = lax.all_to_all(
        jnp.concatenate([query_send, keyval_send], axis=2),
        "seq",
        split_axis=0,
        concat_axis=2,
        tiled=True,
    ).reshape(pass_count, devices, query_len + keyval_send.shape[2])
    query_heads = both_in[:, :, :query_len].reshape(pass_count, devices * sub_rows, head_size)
    keyval_heads = both_in[:, :, query_len:].reshape(pass_count, devices * rows, 2 * head_size)
    outputs = []
    masses = []
    for index in range(pass_count):
        out_now, mass_now = attend_rows(
            query_heads[index],
            keyval_heads[index, :, :head_size],
            keyval_heads[index, :, head_size:],
        )
        outputs.append(out_now)
        masses.append(mass_now)
    attended_heads = jnp.stack(outputs)
    log_mass = jnp.stack(masses)
    out_send = attended_heads.reshape(pass_count, devices, sub_rows * head_size).transpose(1, 0, 2)
    out_back = lax.all_to_all(out_send, "seq", split_axis=0, concat_axis=0, tiled=True)
    attended = (
        out_back.reshape(head_count, query_groups, pass_count, sub_rows, head_size)
        .transpose(2, 1, 3, 0, 4)
        .reshape(pass_count, rows, proj_width)
    )
    terms = jnp.einsum(
        "prh,hf->prf",
        attended,
        out_weight,
        preferred_element_type=jnp.float32,
    )
    mixed = (
        add_halves(terms.astype(jnp.bfloat16), 2) + pooled_wide
    )
    return (
        pre_act,
        pooled_wide,
        whole_wide,
        row_scale,
        query_heads,
        keyval_heads,
        attended_heads,
        log_mass,
        mixed,
    )


def shards(features, noise, conv_weight, conv_bias, norm_gain, qkv_weight, out_weight):
    width = conv_weight.shape[-1]
    (conv_weight,) = gather_seq([(conv_weight, 1)], width)
    (qkv_weight,) = gather_seq([(qkv_weight, 1)], width)
    (out_weight,) = gather_seq([(out_weight, 1)], width)
    clean = features[0]
    moved = (clean.astype(jnp.float32) + noise[0]).astype(jnp.bfloat16)
    joint = forward(
        jnp.stack([clean, moved]), conv_weight, conv_bias, norm_gain, qkv_weight, out_weight
    )
    clean_run = [item[0:1] for item in joint]
    moved_run = [item[1:2] for item in joint]
    (
        pre_act,
        pooled_wide,
        _,
        row_scale,
        query_heads,
        keyval_heads,
        attended_heads,
        log_mass,
        mixed,
    ) = [item[0] for item in moved_run]
    clean_mixed = clean_run[8][0]
    rows, half_width = pooled_wide.shape
    positions = pre_act.shape[0]
    proj_width = qkv_weight.shape[2]
    head_size = HD
    head_count = proj_width // head_size
    devices = lax.axis_size("seq")
    query_groups = devices // head_count
    sub_rows = rows // query_groups
    difference = mixed - clean_mixed
    difference_half = difference.astype(jnp.bfloat16)
    difference_whole = lax.all_gather(difference_half, "mp", axis=1, tiled=True)
    out_grad = jnp.einsum(
        "rf,hf->rh",
        difference_whole,
        out_weight,
        preferred_element_type=jnp.float32,
    ).astype(jnp.bfloat16)
    grad_send = (
        out_grad.reshape(query_groups, sub_rows, head_count, head_size)
        .transpose(2, 0, 1, 3)
        .reshape(devices, sub_rows * head_size)
    )
    grad_in = lax.all_to_all(grad_send, "seq", split_axis=0, concat_axis=1, tiled=True)
    grad_heads = grad_in.reshape(devices * sub_rows, head_size)
    query_grad, keyval_grad = attend_back(
        query_heads,
        keyval_heads[:, :head_size],
        keyval_heads[:, head_size:],
        attended_heads,
        log_mass,
        grad_heads,
    )
    query_len = sub_rows * head_size
    both_back = lax.all_to_all(
        jnp.concatenate(
            [
                query_grad.reshape(devices, query_len).astype(jnp.bfloat16),
                keyval_grad.reshape(devices, rows * 2 * head_size).astype(jnp.bfloat16),
            ],
            axis=1,
        ),
        "seq",
        split_axis=0,
        concat_axis=0,
        tiled=True,
    ).astype(jnp.float32)
    query_back = both_back[:, :query_len]
    keyval_back = both_back[:, query_len:]
    query_rows = (
        query_back.reshape(head_count, query_groups, sub_rows, head_size)
        .transpose(1, 2, 0, 3)
        .reshape(rows, proj_width)
        .astype(jnp.bfloat16)
    )
    keyval_rows = jnp.sum(keyval_back.reshape(head_count, query_groups, rows, 2, head_size), axis=1)
    key_rows = (
        keyval_rows[:, :, 0].transpose(1, 0, 2).reshape(rows, proj_width).astype(jnp.bfloat16)
    )
    value_rows = (
        keyval_rows[:, :, 1].transpose(1, 0, 2).reshape(rows, proj_width).astype(jnp.bfloat16)
    )
    grads = jnp.stack([query_rows, key_rows, value_rows])
    normed_terms = jnp.einsum(
        "jrh,jfh->rf",
        grads,
        qkv_weight,
        preferred_element_type=jnp.float32,
    )
    offset_mp = lax.axis_index("mp") * half_width
    gain_own = lax.dynamic_slice_in_dim(norm_gain, offset_mp, half_width, 0)
    normed_grad = add_halves(normed_terms.astype(jnp.bfloat16), 1)
    weighted_own = jnp.sum(normed_grad * gain_own * pooled_wide, axis=1, keepdims=True)
    weighted = weighted_own + swap_mp(weighted_own)
    pooled_grad = (
        difference + row_scale * gain_own * normed_grad - pooled_wide * row_scale**3 * weighted / F
    )
    spread = jnp.broadcast_to((0.5 * pooled_grad)[:, None, :], (rows, 2, half_width)).reshape(
        positions, half_width
    )
    gelu_back = jax.vjp(jax.nn.gelu, pre_act)[1]
    pre_grad = gelu_back(spread)[0].astype(jnp.bfloat16)
    reach = KW // 2
    padded = with_halo(pre_grad, (("seq", 0),), reach)
    piece = conv_weight
    running = jnp.zeros((positions, piece.shape[1]), jnp.float32)
    for offset in range(piece.shape[0]):
        lower = 2 * reach - offset
        running = running + jnp.einsum(
            "tf,cf->tc",
            padded[lower : lower + positions],
            piece[offset],
            preferred_element_type=jnp.float32,
        )
    own_grad = running.astype(jnp.bfloat16)
    input_grad = (own_grad.astype(jnp.float32) + swap_mp(own_grad).astype(jnp.float32)).astype(
        jnp.bfloat16
    ).astype(jnp.float32)
    new_noise = noise[0] + step_size * input_grad * lax.rsqrt(
        jnp.mean(input_grad * input_grad, axis=1, keepdims=True) + epsilon
    )
    return (clean_mixed.astype(jnp.bfloat16)[None], new_noise[None])


def solution(mesh):
    return jax.shard_map(
        shards,
        mesh=mesh,
        in_specs=(
            P(("group", "batch"), "seq", None),
            P(("group", "batch"), "seq", None),
            P(None, "seq", "mp"),
            P("mp"),
            P(),
            P(None, "seq", "mp"),
            P("mp", "seq"),
        ),
        out_specs=(P(("group", "batch"), "seq", "mp"), P(("group", "batch"), "seq", None)),
        check_vma=False,
    )
```

```python
import jax
import jax.numpy as jnp
from jax import lax
from jax.sharding import PartitionSpec as P

F = 768
HD = 96
KW = 5


step_size = 0.5
epsilon = 1e-06


def with_halo(cells, sides, width):
    for axis, dim in sides:
        count = lax.axis_size(axis)
        ends = count - 1
        head = lax.slice_in_dim(cells, 0, width, axis=dim)
        tail = lax.slice_in_dim(cells, cells.shape[dim] - width, cells.shape[dim], axis=dim)
        cells = jnp.concatenate(
            [
                lax.ppermute(tail, axis, [(i, (i + 1) % count) for i in range(ends)]),
                cells,
                lax.ppermute(head, axis, [((i + 1) % count, i) for i in range(ends)]),
            ],
            axis=dim,
        )
    return cells


def gather_seq(parts, width):
    spread = ("group", "batch")
    count = lax.axis_size("group") * lax.axis_size("batch")
    ring = lax.axis_size("seq")
    flats = [cells.reshape(-1, width) for cells, _ in parts]
    flat = jnp.concatenate(flats, axis=0) if len(flats) > 1 else flats[0]
    rows = flat.shape[0]
    size = -(-rows // count)
    if size * count != rows:
        flat = jnp.pad(flat, ((0, size * count - rows), (0, 0)))
    piece = lax.dynamic_slice_in_dim(flat, lax.axis_index(spread) * size, size, 0)
    if ring <= 8:
        place = lax.axis_index("seq")
        along = jnp.zeros((ring,) + piece.shape, piece.dtype)
        along = lax.dynamic_update_slice_in_dim(along, piece[None], place, 0)
        for shift in range(1, ring):
            arrived = lax.ppermute(piece, "seq", [(i, (i + shift) % ring) for i in range(ring)])
            along = lax.dynamic_update_slice_in_dim(
                along, arrived[None], (place + ring - shift) % ring, 0
            )
    else:
        along = lax.all_gather(piece, "seq", axis=0, tiled=False)
    if ring <= 8 and count <= 4:
        place = lax.axis_index(spread)
        whole = jnp.zeros((count,) + along.shape, along.dtype)
        whole = lax.dynamic_update_slice_in_dim(whole, along[None], place, 0)
        for mask in range(1, count):
            arrived = lax.ppermute(along, spread, [(i, i ^ mask) for i in range(count)])
            whole = lax.dynamic_update_slice_in_dim(
                whole, arrived[None], lax.bitwise_xor(place, mask), 0
            )
    else:
        whole = lax.all_gather(along, spread, axis=0, tiled=False)
    whole = whole.transpose(1, 0, 2, 3).reshape(ring, count * size, width)
    results = []
    offset = 0
    for (cells, dim), part in zip(parts, flats):
        block = whole[:, offset : offset + part.shape[0]]
        offset += part.shape[0]
        block = jnp.moveaxis(block.reshape((ring,) + cells.shape), 0, dim)
        shape = list(cells.shape)
        shape[dim] = shape[dim] * ring
        results.append(block.reshape(shape))
    return results


def swap_mp(cells):
    return lax.ppermute(cells, "mp", [(0, 1), (1, 0)])


def join_mp(cells, dim):
    other = swap_mp(cells)
    first = lax.axis_index("mp") == 0
    return jnp.where(
        first, jnp.concatenate([cells, other], axis=dim), jnp.concatenate([other, cells], axis=dim)
    )


def add_halves(cells, dim):
    half = cells.shape[dim] // 2
    index = lax.axis_index("mp")
    own = lax.dynamic_slice_in_dim(cells, index * half, half, dim)
    other = lax.dynamic_slice_in_dim(cells, (1 - index) * half, half, dim)
    return (own.astype(jnp.float32) + swap_mp(other).astype(jnp.float32)).astype(
        jnp.bfloat16
    ).astype(jnp.float32)


def attend_rows(query, keys, values):
    key_total = keys.shape[0]
    block_len = min(512, key_total)
    head_size = keys.shape[1]
    score_scale = head_size ** (-0.5)
    key_blocks = keys.reshape(key_total // block_len, block_len, head_size)
    value_blocks = values.reshape(key_total // block_len, block_len, head_size)
    query_count = query.shape[0]

    def find_top(carry, key_block):
        row_top, row_mass = carry
        scores = jnp.dot(query, key_block.T, preferred_element_type=jnp.float32) * score_scale
        new_top = jnp.maximum(row_top, jnp.max(scores, axis=1))
        row_mass = row_mass * jnp.exp(row_top - new_top) + jnp.sum(
            jnp.exp(scores - new_top[:, None]), axis=1
        )
        return ((new_top, row_mass), None)

    start_top = jnp.full((query_count,), -1e30, jnp.float32)
    (row_top, row_mass), _ = lax.scan(
        find_top, (start_top, jnp.zeros((query_count,), jnp.float32)), key_blocks
    )
    log_mass = row_top + jnp.log(row_mass)

    def collect(running, blocks):
        key_block, value_block = blocks
        scores = jnp.dot(query, key_block.T, preferred_element_type=jnp.float32) * score_scale
        soft_weights = jnp.exp(scores - log_mass[:, None]).astype(jnp.bfloat16)
        return (
            running + jnp.dot(soft_weights, value_block, preferred_element_type=jnp.float32),
            None,
        )

    running, _ = lax.scan(
        collect, jnp.zeros((query_count, head_size), jnp.float32), (key_blocks, value_blocks)
    )
    return (running.astype(jnp.bfloat16), log_mass)


def attend_back(query, keys, values, attended, log_mass, out_grad):
    key_total = keys.shape[0]
    block_len = min(512, key_total)
    head_size = keys.shape[1]
    score_scale = head_size ** (-0.5)
    key_blocks = keys.reshape(key_total // block_len, block_len, head_size)
    value_blocks = values.reshape(key_total // block_len, block_len, head_size)
    row_dot = jnp.sum(out_grad.astype(jnp.float32) * attended.astype(jnp.float32), axis=1)

    def step_back(query_acc, blocks):
        key_block, value_block = blocks
        scores = jnp.dot(query, key_block.T, preferred_element_type=jnp.float32) * score_scale
        exp_weights = jnp.exp(scores - log_mass[:, None])
        value_part = jnp.einsum(
            "qk,qd->kd",
            exp_weights.astype(jnp.bfloat16),
            out_grad,
            preferred_element_type=jnp.float32,
        )
        prob_grad = jnp.dot(out_grad, value_block.T, preferred_element_type=jnp.float32)
        score_grad = (exp_weights * (prob_grad - row_dot[:, None])).astype(jnp.bfloat16)
        query_acc = (
            query_acc
            + jnp.dot(score_grad, key_block, preferred_element_type=jnp.float32) * score_scale
        )
        key_part = (
            jnp.einsum("qk,qd->kd", score_grad, query, preferred_element_type=jnp.float32)
            * score_scale
        )
        return (query_acc, jnp.concatenate([key_part, value_part], axis=1))

    query_grad, keyval_parts = lax.scan(
        step_back, jnp.zeros((query.shape[0], head_size), jnp.float32), (key_blocks, value_blocks)
    )
    return (query_grad, keyval_parts.reshape(key_total, 2 * head_size))


def forward(stack, conv_weight, conv_bias, norm_gain, qkv_weight, out_weight):
    pass_count, positions, _ = stack.shape
    reach = KW // 2
    half_width = conv_weight.shape[2]
    padded_input = with_halo(stack, (("seq", 1),), reach)
    running = jnp.zeros((pass_count, positions, half_width), jnp.float32)
    piece = conv_weight
    for offset in range(piece.shape[0]):
        running = running + jnp.einsum(
            "ptc,cf->ptf",
            padded_input[:, offset : offset + positions],
            piece[offset],
            preferred_element_type=jnp.float32,
        )
    pre_act = running + conv_bias
    paired = jax.nn.gelu(pre_act).reshape(pass_count, positions // 2, 2, half_width)
    pooled = (0.5 * (paired[:, :, 0] + paired[:, :, 1])).astype(jnp.bfloat16)
    pooled_wide = lax.optimization_barrier(pooled).astype(jnp.float32)
    whole = lax.all_gather(pooled, "mp", axis=2, tiled=True)
    whole_wide = whole.astype(jnp.float32)
    row_scale = lax.rsqrt(jnp.mean(whole_wide * whole_wide, axis=2, keepdims=True) + epsilon)
    normed = (whole_wide * row_scale * norm_gain).astype(jnp.bfloat16)
    rows = positions // 2
    proj_width = qkv_weight.shape[2]
    projected = jnp.einsum(
        "prf,jfh->jprh",
        normed,
        qkv_weight,
        preferred_element_type=jnp.float32,
    ).astype(jnp.bfloat16)
    head_size = HD
    head_count = proj_width // head_size
    devices = lax.axis_size("seq")
    query_groups = devices // head_count
    sub_rows = rows // query_groups
    query_send = (
        projected[0]
        .reshape(pass_count, query_groups, sub_rows, head_count, head_size)
        .transpose(3, 1, 0, 2, 4)
        .reshape(devices, pass_count, sub_rows * head_size)
    )
    keyval = jnp.concatenate(
        [
            projected[1].reshape(pass_count, rows, head_count, head_size),
            projected[2].reshape(pass_count, rows, head_count, head_size),
        ],
        axis=3,
    )
    keyval_flat = keyval.transpose(2, 0, 1, 3).reshape(
        head_count, 1, pass_count, rows * 2 * head_size
    )
    keyval_send = jnp.broadcast_to(
        keyval_flat, (head_count, query_groups, pass_count, rows * 2 * head_size)
    ).reshape(devices, pass_count, rows * 2 * head_size)
    query_len = query_send.shape[2]
    both_in = lax.all_to_all(
        jnp.concatenate([query_send, keyval_send], axis=2),
        "seq",
        split_axis=0,
        concat_axis=2,
        tiled=True,
    ).reshape(pass_count, devices, query_len + keyval_send.shape[2])
    query_heads = both_in[:, :, :query_len].reshape(pass_count, devices * sub_rows, head_size)
    keyval_heads = both_in[:, :, query_len:].reshape(pass_count, devices * rows, 2 * head_size)
    outputs = []
    masses = []
    for index in range(pass_count):
        out_now, mass_now = attend_rows(
            query_heads[index],
            keyval_heads[index, :, :head_size],
            keyval_heads[index, :, head_size:],
        )
        outputs.append(out_now)
        masses.append(mass_now)
    attended_heads = jnp.stack(outputs)
    log_mass = jnp.stack(masses)
    out_send = attended_heads.reshape(pass_count, devices, sub_rows * head_size).transpose(1, 0, 2)
    out_back = lax.all_to_all(out_send, "seq", split_axis=0, concat_axis=0, tiled=True)
    attended = (
        out_back.reshape(head_count, query_groups, pass_count, sub_rows, head_size)
        .transpose(2, 1, 3, 0, 4)
        .reshape(pass_count, rows, proj_width)
    )
    terms = jnp.einsum(
        "prh,hf->prf",
        attended,
        out_weight,
        preferred_element_type=jnp.float32,
    )
    mixed = (
        add_halves(terms.astype(jnp.bfloat16), 2) + pooled_wide
    )
    return (
        pre_act,
        pooled_wide,
        whole_wide,
        row_scale,
        query_heads,
        keyval_heads,
        attended_heads,
        log_mass,
        mixed,
    )


def shards(features, noise, conv_weight, conv_bias, norm_gain, qkv_weight, out_weight):
    width = conv_weight.shape[-1]
    (conv_weight,) = gather_seq([(conv_weight, 1)], width)
    (qkv_weight,) = gather_seq([(qkv_weight, 1)], width)
    (out_weight,) = gather_seq([(out_weight, 1)], width)
    clean = features[0]
    moved = (clean.astype(jnp.float32) + noise[0]).astype(jnp.bfloat16)
    joint = forward(
        jnp.stack([clean, moved]), conv_weight, conv_bias, norm_gain, qkv_weight, out_weight
    )
    clean_run = [item[0:1] for item in joint]
    moved_run = [item[1:2] for item in joint]
    (
        pre_act,
        pooled_wide,
        _,
        row_scale,
        query_heads,
        keyval_heads,
        attended_heads,
        log_mass,
        mixed,
    ) = [item[0] for item in moved_run]
    clean_mixed = clean_run[8][0]
    rows, half_width = pooled_wide.shape
    positions = pre_act.shape[0]
    proj_width = qkv_weight.shape[2]
    head_size = HD
    head_count = proj_width // head_size
    devices = lax.axis_size("seq")
    query_groups = devices // head_count
    sub_rows = rows // query_groups
    difference = mixed - clean_mixed
    difference_half = difference.astype(jnp.bfloat16)
    difference_whole = join_mp(difference_half, 1)
    out_grad = jnp.einsum(
        "rf,hf->rh",
        difference_whole,
        out_weight,
        preferred_element_type=jnp.float32,
    ).astype(jnp.bfloat16)
    grad_send = (
        out_grad.reshape(query_groups, sub_rows, head_count, head_size)
        .transpose(2, 0, 1, 3)
        .reshape(devices, sub_rows * head_size)
    )
    grad_in = lax.all_to_all(grad_send, "seq", split_axis=0, concat_axis=1, tiled=True)
    grad_heads = grad_in.reshape(devices * sub_rows, head_size)
    query_grad, keyval_grad = attend_back(
        query_heads,
        keyval_heads[:, :head_size],
        keyval_heads[:, head_size:],
        attended_heads,
        log_mass,
        grad_heads,
    )
    query_len = sub_rows * head_size
    both_back = lax.all_to_all(
        jnp.concatenate(
            [
                query_grad.reshape(devices, query_len).astype(jnp.bfloat16),
                keyval_grad.reshape(devices, rows * 2 * head_size).astype(jnp.bfloat16),
            ],
            axis=1,
        ),
        "seq",
        split_axis=0,
        concat_axis=0,
        tiled=True,
    ).astype(jnp.float32)
    query_back = both_back[:, :query_len]
    keyval_back = both_back[:, query_len:]
    query_rows = (
        query_back.reshape(head_count, query_groups, sub_rows, head_size)
        .transpose(1, 2, 0, 3)
        .reshape(rows, proj_width)
        .astype(jnp.bfloat16)
    )
    keyval_rows = jnp.sum(keyval_back.reshape(head_count, query_groups, rows, 2, head_size), axis=1)
    key_rows = (
        keyval_rows[:, :, 0].transpose(1, 0, 2).reshape(rows, proj_width).astype(jnp.bfloat16)
    )
    value_rows = (
        keyval_rows[:, :, 1].transpose(1, 0, 2).reshape(rows, proj_width).astype(jnp.bfloat16)
    )
    grads = jnp.stack([query_rows, key_rows, value_rows])
    normed_terms = jnp.einsum(
        "jrh,jfh->rf",
        grads,
        qkv_weight,
        preferred_element_type=jnp.float32,
    )
    offset_mp = lax.axis_index("mp") * half_width
    gain_own = lax.dynamic_slice_in_dim(norm_gain, offset_mp, half_width, 0)
    normed_grad = add_halves(normed_terms.astype(jnp.bfloat16), 1)
    weighted_own = jnp.sum(normed_grad * gain_own * pooled_wide, axis=1, keepdims=True)
    weighted = weighted_own + swap_mp(weighted_own)
    pooled_grad = (
        difference + row_scale * gain_own * normed_grad - pooled_wide * row_scale**3 * weighted / F
    )
    spread = jnp.broadcast_to((0.5 * pooled_grad)[:, None, :], (rows, 2, half_width)).reshape(
        positions, half_width
    )
    gelu_back = jax.vjp(jax.nn.gelu, pre_act)[1]
    pre_grad = gelu_back(spread)[0].astype(jnp.bfloat16)
    reach = KW // 2
    padded = with_halo(pre_grad, (("seq", 0),), reach)
    piece = conv_weight
    running = jnp.zeros((positions, piece.shape[1]), jnp.float32)
    for offset in range(piece.shape[0]):
        lower = 2 * reach - offset
        running = running + jnp.einsum(
            "tf,cf->tc",
            padded[lower : lower + positions],
            piece[offset],
            preferred_element_type=jnp.float32,
        )
    own_grad = running.astype(jnp.bfloat16)
    input_grad = (own_grad.astype(jnp.float32) + swap_mp(own_grad).astype(jnp.float32)).astype(
        jnp.bfloat16
    ).astype(jnp.float32)
    new_noise = noise[0] + step_size * input_grad * lax.rsqrt(
        jnp.mean(input_grad * input_grad, axis=1, keepdims=True) + epsilon
    )
    return (clean_mixed.astype(jnp.bfloat16)[None], new_noise[None])


def solution(mesh):
    return jax.shard_map(
        shards,
        mesh=mesh,
        in_specs=(
            P(("group", "batch"), "seq", None),
            P(("group", "batch"), "seq", None),
            P(None, "seq", "mp"),
            P("mp"),
            P(),
            P(None, "seq", "mp"),
            P("mp", "seq"),
        ),
        out_specs=(P(("group", "batch"), "seq", "mp"), P(("group", "batch"), "seq", None)),
        check_vma=False,
    )
```
